32 devices in a mesh: gx: 8 (over z, y), gy: 4 (over x, core).
Axes of the slice: x: 2, y: 2, z: 4, core: 2. Of those that a mesh axis runs over, the one named last changes fastest.
Arguments:
- conc_prev: float32 [128, 64, 128], P('gx', 'gy'), may hold values from 0.5 to 2
- right_side: float32 [128, 64, 128], P('gx', 'gy'), may hold values from -5 to 7
- soil_id: int32 [128, 64, 128], P('gx', 'gy'), may hold values from 0 to 7
- soil_table: float32 [5, 8], replicated, may hold values from 0.3 to 3
Outputs:
- correction: float32 [128, 64, 128], P('gx', 'gy')
The draws below stay inside these ranges and needn't reach their ends.
All inputs are finite; a program needn't handle non-finite values.
Results may differ from the reference program's by a relative error of at most 0.00002.
Values sent between devices are 32-bit elements; how exact they have to be, the bound alone decides.
No kernel may reach another device: no remote copies, remote signals or barrier semaphores. Data moves between devices by JAX's collectives and lax.ppermute only.
A program may use at most 128 MiB of HBM per device.

```python
import math
import jax
import jax.numpy as jnp

NZ = 128
MAT = 8
CHEB = 3
COARSE_SWEEPS = 8
NX = 128
NY = 64


def draw_right_side(key, part):
    first, second, third = jax.random.split(jax.random.fold_in(key, 11), 3)
    rough_part = jnp.clip(jax.random.normal(first, (NX, NY, NZ), jnp.float32), -5.0, 5.0)
    amplitude = jax.random.uniform(third, (), jnp.float32, 0.6, 1.0)
    phases = jax.random.uniform(second, (2,), jnp.float32, 0.0, 6.2831853)
    across = jnp.arange(NX, dtype=jnp.float32) / NX
    along = jnp.arange(NY, dtype=jnp.float32) / NY
    wave_x = jnp.sin(6.2831853 * 3.0 * across + phases[0])
    wave_y = jnp.sin(6.2831853 * along + phases[1])
    smooth_part = 1.0 + 0.5 * wave_x[:, None, None] * wave_y[None, :, None]
    return rough_part + amplitude * smooth_part


def draw_soil_id(key, part):
    blocks = jax.random.randint(jax.random.fold_in(key, 23), (NX // 4, NY // 4, NZ // 4), 0, MAT)
    blocks = blocks.at[0, 0, 0].set(MAT - 1).at[0, 0, 1].set(0)
    blocks = jnp.repeat(jnp.repeat(jnp.repeat(blocks, 4, axis=0), 4, axis=1), 4, axis=2)
    return blocks.astype(jnp.int32)


def levels(rng, extent, cuts, least, largest):
    gain, own = 1.0, jax.random.fold_in(rng, 6)
    for axis_at, blocks in cuts:
        draws = jnp.exp(jax.random.uniform(jax.random.fold_in(own, axis_at), (blocks,), jnp.float32, least / len(cuts), largest / len(cuts)))
        gain = gain * jnp.repeat(draws, extent[axis_at] // blocks).reshape([-1 if axis == axis_at else 1 for axis in range(len(extent))])
    return gain


def setup_inputs(seed: int = 0) -> dict:
    seeds = jax.random.split(jax.random.key(seed), 5)
    conc_prev = jnp.clip(jnp.exp(math.log(2.0) - 1.3862944 * jax.random.uniform(seeds[0], (NX, NY, NZ), jnp.float32) ** levels(seeds[0], (NX, NY, NZ), ((0, 8), (1, 4)), -0.2, 0.2)), 0.5, 2.0)
    right_side = draw_right_side(jax.random.fold_in(seeds[4], 71), 0)
    soil_id = draw_soil_id(jax.random.fold_in(seeds[4], 71), 0)
    soil_table = jnp.clip(jnp.exp(jax.random.uniform(seeds[3], (5, MAT), jnp.float32, math.log(0.3), math.log(3.0))), 0.3, 3.0)
    return {"conc_prev": conc_prev, "right_side": right_side, "soil_id": soil_id, "soil_table": soil_table}


storage_scale = 0.05
cheb_centre = 1.1
cheb_half = 0.9
cheb_ratio = cheb_centre / cheb_half
jacobi_weight = 0.8


def harmonic(first, second):
    return first * second / jnp.maximum(0.5 * (first + second), 0.1)


def face_terms(coeffs, spacing):
    eastward = coeffs[0]
    northward = coeffs[1]
    upward = coeffs[2]
    centre_x = eastward[1:-1, 1:-1]
    centre_y = northward[1:-1, 1:-1]
    centre_z = upward[1:-1, 1:-1]
    east_face = harmonic(eastward[2:, 1:-1], centre_x) * spacing
    west_face = harmonic(eastward[:-2, 1:-1], centre_x) * spacing
    north_face = harmonic(northward[1:-1, 2:], centre_y) * spacing
    south_face = harmonic(northward[1:-1, :-2], centre_y) * spacing
    vertical = harmonic(centre_z[:, :, 1:], centre_z[:, :, :-1]) * spacing
    closed = jnp.zeros_like(centre_z[:, :, :1])
    above_face = jnp.concatenate([vertical, closed], axis=2)
    below_face = jnp.concatenate([closed, vertical], axis=2)
    storage = coeffs[3, 1:-1, 1:-1]
    return east_face, west_face, north_face, south_face, above_face, below_face, storage


def main_diagonal(coeffs, spacing):
    east_face, west_face, north_face, south_face, above_face, below_face, storage = face_terms(coeffs, spacing)
    return jnp.maximum(storage + east_face + west_face + north_face + south_face + above_face + below_face, 0.01)


def operate(values, coeffs, spacing):
    east_face, west_face, north_face, south_face, above_face, below_face, storage = face_terms(coeffs, spacing)
    centre = values[1:-1, 1:-1]
    upper_cell = jnp.concatenate([centre[:, :, 1:], centre[:, :, :1]], axis=2)
    lower_cell = jnp.concatenate([centre[:, :, -1:], centre[:, :, :-1]], axis=2)
    fluxes = east_face * (centre - values[2:, 1:-1]) + west_face * (centre - values[:-2, 1:-1])
    fluxes = fluxes + north_face * (centre - values[1:-1, 2:]) + south_face * (centre - values[1:-1, :-2])
    fluxes = fluxes + above_face * (centre - upper_cell) + below_face * (centre - lower_cell)
    return storage * centre + fluxes


def coarsen(values):
    lead = values.shape[:-3]
    size_x, size_y, size_z = values.shape[-3:]
    split = values.reshape(lead + (size_x // 2, 2, size_y // 2, 2, size_z // 2, 2))
    return jnp.mean(split, axis=(-5, -3, -1))


def prolong(values):
    return jnp.repeat(jnp.repeat(jnp.repeat(values, 2, axis=0), 2, axis=1), 2, axis=2)


def pad_field(values):
    return jnp.pad(values, ((1, 1), (1, 1), (0, 0)))


def pad_coeffs(coeffs):
    return jnp.pad(coeffs, ((0, 0), (1, 1), (1, 1), (0, 0)))


def soil_fields(conc_prev, soil_id, soil_table):
    looked = soil_table[:, soil_id]
    storage = storage_scale * (1.0 + looked[3] * jnp.exp((looked[4] - 1.0) * jnp.log(conc_prev)))
    return jnp.stack([looked[0], looked[1], looked[2], storage])


def chebyshev(target, initial, coeffs, spacing):
    padded = pad_coeffs(coeffs)
    diagonal = main_diagonal(padded, spacing)
    if initial is None:
        misfit = target
    else:
        misfit = target - operate(pad_field(initial), padded, spacing)
    update = misfit / diagonal * (1.0 / cheb_centre)
    iterate = update if initial is None else initial + update
    factor = 1.0 / cheb_ratio
    for repeat in range(CHEB - 1):
        misfit = target - operate(pad_field(iterate), padded, spacing)
        factor_new = 1.0 / (2.0 * cheb_ratio - factor)
        update = (factor_new * factor) * update + (2.0 * factor_new / cheb_half) * (misfit / diagonal)
        iterate = iterate + update
        factor = factor_new
    return iterate


def reference(conc_prev, right_side, soil_id, soil_table):
    fine_coeffs = soil_fields(conc_prev, soil_id, soil_table)
    mid_coeffs = coarsen(fine_coeffs)
    coarse_coeffs = coarsen(mid_coeffs)
    fine_iterate = chebyshev(right_side, None, fine_coeffs, 1.0)
    fine_misfit = right_side - operate(pad_field(fine_iterate), pad_coeffs(fine_coeffs), 1.0)
    mid_source = coarsen(fine_misfit)
    mid_iterate = chebyshev(mid_source, None, mid_coeffs, 0.25)
    mid_misfit = mid_source - operate(pad_field(mid_iterate), pad_coeffs(mid_coeffs), 0.25)
    coarse_source = coarsen(mid_misfit)
    padded = pad_coeffs(coarse_coeffs)
    diagonal = main_diagonal(padded, 0.0625)
    line_total = jnp.sum(coarse_source, axis=1)
    line_store = jnp.sum(coarse_coeffs[3], axis=1)
    line_mean = line_total / line_store
    coarse_value = jnp.broadcast_to(line_mean[:, None, :], coarse_source.shape)
    for sweeps in range(COARSE_SWEEPS):
        applied = operate(pad_field(coarse_value), padded, 0.0625)
        coarse_value = coarse_value + jacobi_weight * ((coarse_source - applied) / diagonal)
    mid_result = chebyshev(mid_source, mid_iterate + prolong(coarse_value), mid_coeffs, 0.25)
    return chebyshev(right_side, fine_iterate + prolong(mid_result), fine_coeffs, 1.0)
```

```python
import jax
import jax.numpy as jnp
from jax import lax
from jax.sharding import PartitionSpec as P

CHEB = 3
COARSE_SWEEPS = 8

storage_scale = 0.05
cheb_centre = 1.1
cheb_half = 0.9
cheb_ratio = cheb_centre / cheb_half
jacobi_weight = 0.8

FINE_HALO = 10
MID_HALO = 5
HIGH = lax.Precision.HIGHEST


def shift_from(cells, axis, offset):
    count = lax.axis_size(axis)
    if offset > 0:
        pairs = [(i + offset, i) for i in range(count - offset)]
    else:
        pairs = [(i, i - offset) for i in range(count + offset)]
    if not pairs:
        return jnp.zeros_like(cells)
    return lax.ppermute(cells, axis, pairs)


def halo(cells, sides, width):
    for axis, dim in sides:
        size = cells.shape[dim]
        head = lax.slice_in_dim(cells, 0, width, axis=dim)
        tail = lax.slice_in_dim(cells, size - width, size, axis=dim)
        cells = jnp.concatenate(
            [shift_from(tail, axis, -1), cells, shift_from(head, axis, 1)], axis=dim
        )
    return cells


def harmonic(first, second):
    return first * second / jnp.maximum(0.5 * (first + second), 0.1)


def win(a, n, margin, r, dx=0, dy=0):
    lo = margin - r
    hi = margin + n + r
    return a[..., lo + dx : hi + dx, lo + dy : hi + dy, :]


def pair_matrix(size, dtype=jnp.float32):
    rows = jnp.arange(size)[:, None] // 2
    cols = jnp.arange(size // 2)[None, :]
    return (rows == cols).astype(dtype)


def coarsen(values):
    lead = values.shape[:-3]
    sx, sy, sz = values.shape[-3:]
    v = values.reshape(lead + (sx // 2, 2, sy, sz))
    v = v[..., 0, :, :] + v[..., 1, :, :]
    v = jnp.einsum("...yz,zw->...yw", v, pair_matrix(sz), precision=HIGH)
    v = jnp.einsum("...yw,yv->...vw", v, pair_matrix(sy), precision=HIGH)
    return v * 0.125


def prolong(values):
    sx, sy, sz = values.shape
    v = jnp.einsum("xyz,wz->xyw", values, pair_matrix(2 * sz), precision=HIGH)
    v = jnp.einsum("xyw,vy->xvw", v, pair_matrix(2 * sy), precision=HIGH)
    v = jnp.broadcast_to(v[:, None], (sx, 2) + v.shape[1:]).reshape((2 * sx,) + v.shape[1:])
    return v


def build_level(coeffs, n, margin, spacing):
    kx, ky, kz, store = coeffs[0], coeffs[1], coeffs[2], coeffs[3]
    fx = harmonic(kx[1:], kx[:-1]) * spacing
    fy = harmonic(ky[:, 1:], ky[:, :-1]) * spacing
    vertical = harmonic(kz[:, :, 1:], kz[:, :, :-1]) * spacing
    closed = jnp.zeros_like(kz[:, :, :1])
    above = jnp.concatenate([vertical, closed], axis=2)
    below = jnp.concatenate([closed, vertical], axis=2)
    level = dict(n=n, m=margin, fx=fx, fy=fy, above=above, below=below, store=store)
    r = margin - 1
    level["diag"] = jnp.maximum(faces_sum(level, r) + win(store, n, margin, r), 0.01)
    level["dm"] = r
    return level


def faces_sum(level, r):
    n, m = level["n"], level["m"]
    east = win(level["fx"], n, m, r)
    west = win(level["fx"], n, m, r, dx=-1)
    north = win(level["fy"], n, m, r)
    south = win(level["fy"], n, m, r, dy=-1)
    above = win(level["above"], n, m, r)
    below = win(level["below"], n, m, r)
    return east + west + north + south + above + below


def operate(values, vm, level):
    n, m = level["n"], level["m"]
    r = vm - 1
    centre = win(values, n, vm, r)
    upper = jnp.concatenate([centre[:, :, 1:], centre[:, :, :1]], axis=2)
    lower = jnp.concatenate([centre[:, :, -1:], centre[:, :, :-1]], axis=2)
    fx, fy = level["fx"], level["fy"]
    fluxes = win(fx, n, m, r) * (centre - win(values, n, vm, r, dx=1))
    fluxes = fluxes + win(fx, n, m, r, dx=-1) * (centre - win(values, n, vm, r, dx=-1))
    fluxes = fluxes + win(fy, n, m, r) * (centre - win(values, n, vm, r, dy=1))
    fluxes = fluxes + win(fy, n, m, r, dy=-1) * (centre - win(values, n, vm, r, dy=-1))
    fluxes = fluxes + win(level["above"], n, m, r) * (centre - upper)
    fluxes = fluxes + win(level["below"], n, m, r) * (centre - lower)
    return win(level["store"], n, m, r) * centre + fluxes


def chebyshev(target, tm, initial, im, level):
    n = level["n"]
    diag, dm = level["diag"], level["dm"]
    if initial is None:
        cur = min(tm, dm)
        misfit = win(target, n, tm, cur)
        update = misfit / win(diag, n, dm, cur) * (1.0 / cheb_centre)
        iterate = update
    else:
        applied = operate(initial, im, level)
        cur = im - 1
        misfit = win(target, n, tm, cur) - applied
        update = misfit / win(diag, n, dm, cur) * (1.0 / cheb_centre)
        iterate = win(initial, n, im, cur) + update
    factor = 1.0 / cheb_ratio
    for repeat in range(CHEB - 1):
        applied = operate(iterate, cur, level)
        nxt = cur - 1
        misfit = win(target, n, tm, nxt) - applied
        factor_new = 1.0 / (2.0 * cheb_ratio - factor)
        update = factor_new * factor * win(update, n, cur, nxt) + 2.0 * factor_new / cheb_half * (
            misfit / win(diag, n, dm, nxt)
        )
        iterate = win(iterate, n, cur, nxt) + update
        cur = nxt
        factor = factor_new
    return iterate, cur


def lookup(soil_id, soil_table, record):
    looked = jnp.full(soil_id.shape, soil_table[record, soil_table.shape[1] - 1])
    for material in range(soil_table.shape[1] - 2, -1, -1):
        looked = jnp.where(soil_id == material, soil_table[record, material], looked)
    return looked


def local(conc_prev, right_side, soil_id, soil_table):
    n = conc_prev.shape[0]
    ny = conc_prev.shape[1]
    hf = FINE_HALO
    gx_count = lax.axis_size("gx")
    gy_count = lax.axis_size("gy")
    ix = lax.axis_index("gx")
    iy = lax.axis_index("gy")

    stacked = jnp.stack([conc_prev, right_side, soil_id.astype(jnp.float32)])
    ext = halo(stacked, (("gx", 1), ("gy", 2)), hf)
    conc, rhs, idf = ext[0], ext[1], ext[2]
    ids = idf.astype(jnp.int32)
    gxi = ix * n - hf + jnp.arange(n + 2 * hf)
    gyi = iy * ny - hf + jnp.arange(ny + 2 * hf)
    inside = ((gxi >= 0) & (gxi < gx_count * n))[:, None, None] & (
        (gyi >= 0) & (gyi < gy_count * ny)
    )[None, :, None]
    kx = jnp.where(inside, lookup(ids, soil_table, 0), 0.0)
    ky = jnp.where(inside, lookup(ids, soil_table, 1), 0.0)
    kz = jnp.where(inside, lookup(ids, soil_table, 2), 0.0)
    s3 = lookup(ids, soil_table, 3)
    s4 = lookup(ids, soil_table, 4)
    store = storage_scale * (1.0 + s3 * jnp.exp((s4 - 1.0) * jnp.log(conc)))
    store = jnp.where(inside, store, 0.0)
    fine_c = jnp.stack([kx, ky, kz, store])
    fine = build_level(fine_c, n, hf, 1.0)

    x0, x0m = chebyshev(rhs, hf, None, 0, fine)
    r0 = win(rhs, n, hf, x0m - 1) - operate(x0, x0m, fine)
    r0m = x0m - 1
    nm = n // 2
    mm = hf // 2
    mid_c = coarsen(fine_c)
    mid = build_level(mid_c, nm, mm, 0.25)
    b1 = coarsen(win(r0, n, r0m, 2 * (r0m // 2)))
    b1m = r0m // 2
    x1, x1m = chebyshev(b1, b1m, None, 0, mid)
    r1 = win(b1, nm, b1m, x1m - 1) - operate(x1, x1m, mid)
    r1m = x1m - 1
    b2 = coarsen(win(r1, nm, r1m, 0))
    coarse_own = coarsen(win(mid_c, nm, mm, 0))

    nc = b2.shape[0]
    reach = 2
    cpack = jnp.concatenate([b2[None], coarse_own], axis=0)
    cpack = lax.all_gather(cpack, "gy", axis=2, tiled=True)
    parts = [shift_from(cpack, "gx", -d) for d in range(reach, 0, -1)]
    parts += [cpack]
    parts += [shift_from(cpack, "gx", d) for d in range(1, reach + 1)]
    cpack = jnp.concatenate(parts, axis=1)
    cm = reach * nc
    source = cpack[0]
    cc = cpack[1:]
    line_total = jnp.sum(source, axis=1)
    line_store = jnp.sum(cc[3], axis=1)
    line_mean = jnp.where(line_store > 0, line_total / jnp.where(line_store > 0, line_store, 1.0), 0.0)
    width = source.shape[0]
    ccp = jnp.pad(cc, ((0, 0), (0, 0), (1, 1), (0, 0)))
    kx_, ky_, kz_, st_ = ccp[0], ccp[1], ccp[2], ccp[3]
    q = 0.0625
    cx = kx_[1:-1, 1:-1]
    cy = ky_[1:-1, 1:-1]
    cz = kz_[1:-1, 1:-1]
    east = harmonic(kx_[2:, 1:-1], cx) * q
    west = harmonic(kx_[:-2, 1:-1], cx) * q
    north = harmonic(ky_[1:-1, 2:], cy) * q
    south = harmonic(ky_[1:-1, :-2], cy) * q
    vert = harmonic(cz[:, :, 1:], cz[:, :, :-1]) * q
    closed = jnp.zeros_like(cz[:, :, :1])
    above = jnp.concatenate([vert, closed], axis=2)
    below = jnp.concatenate([closed, vert], axis=2)
    cst = st_[1:-1, 1:-1]
    cdiag = jnp.maximum(cst + east + west + north + south + above + below, 0.01)
    csrc = source[1:-1]
    u = jnp.broadcast_to(line_mean[:, None, :], source.shape)
    for sweep in range(COARSE_SWEEPS):
        lo = sweep
        cur = u
        up = jnp.pad(cur, ((0, 0), (1, 1), (0, 0)))
        centre = up[1:-1, 1:-1]
        sl = slice(lo, width - 2 - lo)
        upper = jnp.concatenate([centre[:, :, 1:], centre[:, :, :1]], axis=2)
        lower = jnp.concatenate([centre[:, :, -1:], centre[:, :, :-1]], axis=2)
        fl = east[sl] * (centre - up[2:, 1:-1]) + west[sl] * (centre - up[:-2, 1:-1])
        fl = fl + north[sl] * (centre - up[1:-1, 2:]) + south[sl] * (centre - up[1:-1, :-2])
        fl = fl + above[sl] * (centre - upper) + below[sl] * (centre - lower)
        applied = cst[sl] * centre + fl
        u = centre + jacobi_weight * ((csrc[sl] - applied) / cdiag[sl])
    ncy = nc
    u = lax.dynamic_slice_in_dim(u, iy * ncy, ncy, 1)

    s1 = win(x1, nm, x1m, 0) + prolong(u)
    mpack = jnp.stack([s1, win(b1, nm, b1m, 0)])
    mpack = halo(mpack, (("gx", 1), ("gy", 2)), MID_HALO)
    s1e, b1e = mpack[0], mpack[1]
    y1, y1m = chebyshev(b1e, MID_HALO, s1e, MID_HALO, mid)
    fm = 2 * y1m
    s0 = win(x0, n, x0m, fm) + prolong(y1)
    fs = min(fm, CHEB)
    s0 = win(s0, n, fm, fs)
    out, om = chebyshev(rhs, hf, s0, fs, fine)
    return out


def solution(mesh):
    placed = (P("gx", "gy", None), P("gx", "gy", None), P("gx", "gy", None), P())
    return jax.shard_map(
        local, mesh=mesh, in_specs=placed, out_specs=P("gx", "gy", None), check_vma=False
    )
```

```python
import jax
import jax.numpy as jnp
from jax import lax
from jax.sharding import PartitionSpec as P
from jax.experimental import pallas as pl
from jax.experimental.pallas import tpu as pltpu

CHEB = 3
COARSE_SWEEPS = 8

storage_scale = 0.05
cheb_centre = 1.1
cheb_half = 0.9
cheb_ratio = cheb_centre / cheb_half
jacobi_weight = 0.8

FINE_HALO = 10
MID_HALO = 5
HIGH = lax.Precision.HIGHEST


def shift_from(cells, axis, offset):
    count = lax.axis_size(axis)
    if offset > 0:
        pairs = [(i + offset, i) for i in range(count - offset)]
    else:
        pairs = [(i, i - offset) for i in range(count + offset)]
    if not pairs:
        return jnp.zeros_like(cells)
    return lax.ppermute(cells, axis, pairs)


def halo(cells, sides, width):
    for axis, dim in sides:
        size = cells.shape[dim]
        head = lax.slice_in_dim(cells, 0, width, axis=dim)
        tail = lax.slice_in_dim(cells, size - width, size, axis=dim)
        cells = jnp.concatenate(
            [shift_from(tail, axis, -1), cells, shift_from(head, axis, 1)], axis=dim
        )
    return cells


def harmonic(first, second):
    return first * second / jnp.maximum(0.5 * (first + second), 0.1)


def win(a, n, margin, r, dx=0, dy=0):
    lo = margin - r
    hi = margin + n + r
    return a[..., lo + dx : hi + dx, lo + dy : hi + dy, :]


def pair_matrix(size, dtype=jnp.float32):
    rows = jnp.arange(size)[:, None] // 2
    cols = jnp.arange(size // 2)[None, :]
    return (rows == cols).astype(dtype)


def coarsen(values):
    lead = values.shape[:-3]
    sx, sy, sz = values.shape[-3:]
    v = values.reshape(lead + (sx // 2, 2, sy, sz))
    v = v[..., 0, :, :] + v[..., 1, :, :]
    v = v[..., 0::2, :] + v[..., 1::2, :]
    v = jnp.einsum("...yz,zw->...yw", v, pair_matrix(sz), precision=HIGH)
    return v * 0.125


def prolong(values):
    sx, sy, sz = values.shape
    v = jnp.einsum("xyz,wz->xyw", values, pair_matrix(2 * sz), precision=HIGH)
    v = jnp.repeat(v, 2, axis=1)
    v = jnp.broadcast_to(v[:, None], (sx, 2) + v.shape[1:]).reshape((2 * sx,) + v.shape[1:])
    return v


def build_level(coeffs, n, margin, spacing):
    kx, ky, kz, store = coeffs[0], coeffs[1], coeffs[2], coeffs[3]
    fx = harmonic(kx[1:], kx[:-1]) * spacing
    fy = harmonic(ky[:, 1:], ky[:, :-1]) * spacing
    vertical = harmonic(kz[:, :, 1:], kz[:, :, :-1]) * spacing
    closed = jnp.zeros_like(kz[:, :, :1])
    above = jnp.concatenate([vertical, closed], axis=2)
    below = jnp.concatenate([closed, vertical], axis=2)
    level = dict(n=n, m=margin, fx=fx, fy=fy, above=above, below=below, store=store)
    r = margin - 1
    level["diag"] = jnp.maximum(faces_sum(level, r) + win(store, n, margin, r), 0.01)
    level["dm"] = r
    return level


def faces_sum(level, r):
    n, m = level["n"], level["m"]
    east = win(level["fx"], n, m, r)
    west = win(level["fx"], n, m, r, dx=-1)
    north = win(level["fy"], n, m, r)
    south = win(level["fy"], n, m, r, dy=-1)
    above = win(level["above"], n, m, r)
    below = win(level["below"], n, m, r)
    return east + west + north + south + above + below


def operate(values, vm, level):
    n, m = level["n"], level["m"]
    r = vm - 1
    centre = win(values, n, vm, r)
    upper = jnp.concatenate([centre[:, :, 1:], centre[:, :, :1]], axis=2)
    lower = jnp.concatenate([centre[:, :, -1:], centre[:, :, :-1]], axis=2)
    fx, fy = level["fx"], level["fy"]
    fluxes = win(fx, n, m, r) * (centre - win(values, n, vm, r, dx=1))
    fluxes = fluxes + win(fx, n, m, r, dx=-1) * (centre - win(values, n, vm, r, dx=-1))
    fluxes = fluxes + win(fy, n, m, r) * (centre - win(values, n, vm, r, dy=1))
    fluxes = fluxes + win(fy, n, m, r, dy=-1) * (centre - win(values, n, vm, r, dy=-1))
    fluxes = fluxes + win(level["above"], n, m, r) * (centre - upper)
    fluxes = fluxes + win(level["below"], n, m, r) * (centre - lower)
    return win(level["store"], n, m, r) * centre + fluxes


def chebyshev(target, tm, initial, im, level):
    n = level["n"]
    diag, dm = level["diag"], level["dm"]
    if initial is None:
        cur = min(tm, dm)
        misfit = win(target, n, tm, cur)
        update = misfit / win(diag, n, dm, cur) * (1.0 / cheb_centre)
        iterate = update
    else:
        applied = operate(initial, im, level)
        cur = im - 1
        misfit = win(target, n, tm, cur) - applied
        update = misfit / win(diag, n, dm, cur) * (1.0 / cheb_centre)
        iterate = win(initial, n, im, cur) + update
    factor = 1.0 / cheb_ratio
    for repeat in range(CHEB - 1):
        applied = operate(iterate, cur, level)
        nxt = cur - 1
        misfit = win(target, n, tm, nxt) - applied
        factor_new = 1.0 / (2.0 * cheb_ratio - factor)
        update = factor_new * factor * win(update, n, cur, nxt) + 2.0 * factor_new / cheb_half * (
            misfit / win(diag, n, dm, nxt)
        )
        iterate = win(iterate, n, cur, nxt) + update
        cur = nxt
        factor = factor_new
    return iterate, cur


def fields_kernel(bounds_ref, table_ref, conc_ref, idf_ref, out_ref):
    rows = conc_ref.shape[0]
    shape = conc_ref.shape[1:]
    mats = table_ref.shape[1]
    col = lax.broadcasted_iota(jnp.int32, shape, 0)
    col_ok = (col >= bounds_ref[2]) & (col < bounds_ref[3])

    def body(i, carry):
        ids = idf_ref[i]
        conc = conc_ref[i]
        row = jnp.zeros(shape, jnp.int32) + i
        ok = col_ok & (row >= bounds_ref[0]) & (row < bounds_ref[1])
        vals = []
        for record in range(5):
            acc = jnp.zeros(shape, jnp.float32) + table_ref[record, mats - 1]
            for material in range(mats - 2, -1, -1):
                acc = jnp.where(ids == float(material), table_ref[record, material], acc)
            vals.append(acc)
        store = storage_scale * (1.0 + vals[3] * jnp.exp((vals[4] - 1.0) * jnp.log(conc)))
        out_ref[0, i] = jnp.where(ok, vals[0], 0.0)
        out_ref[1, i] = jnp.where(ok, vals[1], 0.0)
        out_ref[2, i] = jnp.where(ok, vals[2], 0.0)
        out_ref[3, i] = jnp.where(ok, store, 0.0)
        return carry

    lax.fori_loop(0, rows, body, 0)


def soil_fields(bounds, soil_table, conc, idf):
    cells = conc.size
    return pl.pallas_call(
        fields_kernel,
        out_shape=jax.ShapeDtypeStruct((4,) + conc.shape, jnp.float32),
        in_specs=[
            pl.BlockSpec(memory_space=pltpu.SMEM),
            pl.BlockSpec(memory_space=pltpu.SMEM),
            pl.BlockSpec(memory_space=pltpu.VMEM),
            pl.BlockSpec(memory_space=pltpu.VMEM),
        ],
        out_specs=pl.BlockSpec(memory_space=pltpu.VMEM),
        cost_estimate=pl.CostEstimate(
            flops=100 * cells, transcendentals=2 * cells, bytes_accessed=24 * cells
        ),
    )(bounds, soil_table, conc, idf)


def local(conc_prev, right_side, soil_id, soil_table):
    n = conc_prev.shape[0]
    ny = conc_prev.shape[1]
    hf = FINE_HALO
    gx_count = lax.axis_size("gx")
    gy_count = lax.axis_size("gy")
    ix = lax.axis_index("gx")
    iy = lax.axis_index("gy")

    stacked = jnp.stack([conc_prev, right_side, soil_id.astype(jnp.float32)])
    ext = halo(stacked, (("gx", 1), ("gy", 2)), hf)
    conc, rhs, idf = ext[0], ext[1], ext[2]
    x_lo = hf - ix * n
    y_lo = hf - iy * ny
    bounds = jnp.stack([x_lo, x_lo + gx_count * n, y_lo, y_lo + gy_count * ny]).astype(jnp.int32)
    fine_c = soil_fields(bounds, soil_table, conc, idf)
    fine = build_level(fine_c, n, hf, 1.0)

    x0, x0m = chebyshev(rhs, hf, None, 0, fine)
    r0 = win(rhs, n, hf, x0m - 1) - operate(x0, x0m, fine)
    r0m = x0m - 1
    nm = n // 2
    mm = hf // 2
    mid_c = coarsen(fine_c)
    mid = build_level(mid_c, nm, mm, 0.25)
    b1 = coarsen(win(r0, n, r0m, 2 * (r0m // 2)))
    b1m = r0m // 2
    x1, x1m = chebyshev(b1, b1m, None, 0, mid)
    r1 = win(b1, nm, b1m, x1m - 1) - operate(x1, x1m, mid)
    r1m = x1m - 1
    b2 = coarsen(win(r1, nm, r1m, 0))
    coarse_own = coarsen(win(mid_c, nm, mm, 0))

    nc = b2.shape[0]
    reach = 2
    cpack = jnp.concatenate([b2[None], coarse_own], axis=0)
    cpack = lax.all_gather(cpack, "gy", axis=2, tiled=True)
    parts = [shift_from(cpack, "gx", -d) for d in range(reach, 0, -1)]
    parts += [cpack]
    parts += [shift_from(cpack, "gx", d) for d in range(1, reach + 1)]
    cpack = jnp.concatenate(parts, axis=1)
    cm = reach * nc
    source = cpack[0]
    cc = cpack[1:]
    line_total = jnp.sum(source, axis=1)
    line_store = jnp.sum(cc[3], axis=1)
    line_mean = jnp.where(line_store > 0, line_total / jnp.where(line_store > 0, line_store, 1.0), 0.0)
    width = source.shape[0]
    ccp = jnp.pad(cc, ((0, 0), (0, 0), (1, 1), (0, 0)))
    kx_, ky_, kz_, st_ = ccp[0], ccp[1], ccp[2], ccp[3]
    q = 0.0625
    cx = kx_[1:-1, 1:-1]
    cy = ky_[1:-1, 1:-1]
    cz = kz_[1:-1, 1:-1]
    east = harmonic(kx_[2:, 1:-1], cx) * q
    west = harmonic(kx_[:-2, 1:-1], cx) * q
    north = harmonic(ky_[1:-1, 2:], cy) * q
    south = harmonic(ky_[1:-1, :-2], cy) * q
    vert = harmonic(cz[:, :, 1:], cz[:, :, :-1]) * q
    closed = jnp.zeros_like(cz[:, :, :1])
    above = jnp.concatenate([vert, closed], axis=2)
    below = jnp.concatenate([closed, vert], axis=2)
    cst = st_[1:-1, 1:-1]
    cdiag = jnp.maximum(cst + east + west + north + south + above + below, 0.01)
    csrc = source[1:-1]
    u = jnp.broadcast_to(line_mean[:, None, :], source.shape)
    for sweep in range(COARSE_SWEEPS):
        lo = sweep
        cur = u
        up = jnp.pad(cur, ((0, 0), (1, 1), (0, 0)))
        centre = up[1:-1, 1:-1]
        sl = slice(lo, width - 2 - lo)
        upper = jnp.concatenate([centre[:, :, 1:], centre[:, :, :1]], axis=2)
        lower = jnp.concatenate([centre[:, :, -1:], centre[:, :, :-1]], axis=2)
        fl = east[sl] * (centre - up[2:, 1:-1]) + west[sl] * (centre - up[:-2, 1:-1])
        fl = fl + north[sl] * (centre - up[1:-1, 2:]) + south[sl] * (centre - up[1:-1, :-2])
        fl = fl + above[sl] * (centre - upper) + below[sl] * (centre - lower)
        applied = cst[sl] * centre + fl
        u = centre + jacobi_weight * ((csrc[sl] - applied) / cdiag[sl])
    ncy = nc
    u = lax.dynamic_slice_in_dim(u, iy * ncy, ncy, 1)

    s1 = win(x1, nm, x1m, 0) + prolong(u)
    mpack = jnp.stack([s1, win(b1, nm, b1m, 0)])
    mpack = halo(mpack, (("gx", 1), ("gy", 2)), MID_HALO)
    s1e, b1e = mpack[0], mpack[1]
    y1, y1m = chebyshev(b1e, MID_HALO, s1e, MID_HALO, mid)
    fm = 2 * y1m
    s0 = win(x0, n, x0m, fm) + prolong(y1)
    fs = min(fm, CHEB)
    s0 = win(s0, n, fm, fs)
    out, om = chebyshev(rhs, hf, s0, fs, fine)
    return out


def solution(mesh):
    placed = (P("gx", "gy", None), P("gx", "gy", None), P("gx", "gy", None), P())
    return jax.shard_map(
        local, mesh=mesh, in_specs=placed, out_specs=P("gx", "gy", None), check_vma=False
    )
```

```python
import jax
import jax.numpy as jnp
from jax import lax
from jax.sharding import PartitionSpec as P
from jax.experimental import pallas as pl
from jax.experimental.pallas import tpu as pltpu

CHEB = 3
COARSE_SWEEPS = 8

storage_scale = 0.05
cheb_centre = 1.1
cheb_half = 0.9
cheb_ratio = cheb_centre / cheb_half
jacobi_weight = 0.8

FINE_HALO = 10
MID_HALO = 5
HIGH = lax.Precision.HIGHEST


def shift_from(cells, axis, offset):
    count = lax.axis_size(axis)
    if offset > 0:
        pairs = [(i + offset, i) for i in range(count - offset)]
    else:
        pairs = [(i, i - offset) for i in range(count + offset)]
    if not pairs:
        return jnp.zeros_like(cells)
    return lax.ppermute(cells, axis, pairs)


def halo(cells, sides, width):
    for axis, dim in sides:
        size = cells.shape[dim]
        head = lax.slice_in_dim(cells, 0, width, axis=dim)
        tail = lax.slice_in_dim(cells, size - width, size, axis=dim)
        cells = jnp.concatenate(
            [shift_from(tail, axis, -1), cells, shift_from(head, axis, 1)], axis=dim
        )
    return cells


def harmonic(first, second):
    return first * second / jnp.maximum(0.5 * (first + second), 0.1)


def win(a, n, margin, r, dx=0, dy=0):
    lo = margin - r
    hi = margin + n + r
    return a[..., lo + dx : hi + dx, lo + dy : hi + dy, :]


def pair_matrix(size, dtype=jnp.float32):
    rows = jnp.arange(size)[:, None] // 2
    cols = jnp.arange(size // 2)[None, :]
    return (rows == cols).astype(dtype)


def coarsen(values):
    lead = values.shape[:-3]
    sx, sy, sz = values.shape[-3:]
    v = values.reshape(lead + (sx // 2, 2, sy, sz))
    v = v[..., 0, :, :] + v[..., 1, :, :]
    v = jnp.einsum("...yz,zw->...yw", v, pair_matrix(sz), precision=HIGH)
    rows = v.reshape((-1, sy, sz // 2))
    pick = jnp.broadcast_to(pair_matrix(sy).T, (rows.shape[0], sy // 2, sy))
    rows = lax.dot_general(pick, rows, (((2,), (1,)), ((0,), (0,))), precision=HIGH)
    v = rows.reshape(lead + (sx // 2, sy // 2, sz // 2))
    return v * 0.125


def prolong(values):
    sx, sy, sz = values.shape
    v = jnp.einsum("xyz,wz->xyw", values, pair_matrix(2 * sz), precision=HIGH)
    v = jnp.repeat(v, 2, axis=1)
    v = jnp.broadcast_to(v[:, None], (sx, 2) + v.shape[1:]).reshape((2 * sx,) + v.shape[1:])
    return v


def build_level(coeffs, n, margin, spacing):
    kx, ky, kz, store = coeffs[0], coeffs[1], coeffs[2], coeffs[3]
    fx = harmonic(kx[1:], kx[:-1]) * spacing
    fy = harmonic(ky[:, 1:], ky[:, :-1]) * spacing
    vertical = harmonic(kz[:, :, 1:], kz[:, :, :-1]) * spacing
    closed = jnp.zeros_like(kz[:, :, :1])
    above = jnp.concatenate([vertical, closed], axis=2)
    below = jnp.concatenate([closed, vertical], axis=2)
    level = dict(n=n, m=margin, fx=fx, fy=fy, above=above, below=below, store=store)
    r = margin - 1
    level["diag"] = jnp.maximum(faces_sum(level, r) + win(store, n, margin, r), 0.01)
    level["dm"] = r
    return level


def faces_sum(level, r):
    n, m = level["n"], level["m"]
    east = win(level["fx"], n, m, r)
    west = win(level["fx"], n, m, r, dx=-1)
    north = win(level["fy"], n, m, r)
    south = win(level["fy"], n, m, r, dy=-1)
    above = win(level["above"], n, m, r)
    below = win(level["below"], n, m, r)
    return east + west + north + south + above + below


def operate(values, vm, level):
    n, m = level["n"], level["m"]
    r = vm - 1
    centre = win(values, n, vm, r)
    upper = jnp.concatenate([centre[:, :, 1:], centre[:, :, :1]], axis=2)
    lower = jnp.concatenate([centre[:, :, -1:], centre[:, :, :-1]], axis=2)
    fx, fy = level["fx"], level["fy"]
    fluxes = win(fx, n, m, r) * (centre - win(values, n, vm, r, dx=1))
    fluxes = fluxes + win(fx, n, m, r, dx=-1) * (centre - win(values, n, vm, r, dx=-1))
    fluxes = fluxes + win(fy, n, m, r) * (centre - win(values, n, vm, r, dy=1))
    fluxes = fluxes + win(fy, n, m, r, dy=-1) * (centre - win(values, n, vm, r, dy=-1))
    fluxes = fluxes + win(level["above"], n, m, r) * (centre - upper)
    fluxes = fluxes + win(level["below"], n, m, r) * (centre - lower)
    return win(level["store"], n, m, r) * centre + fluxes


def chebyshev(target, tm, initial, im, level):
    n = level["n"]
    diag, dm = level["diag"], level["dm"]
    if initial is None:
        cur = min(tm, dm)
        misfit = win(target, n, tm, cur)
        update = misfit / win(diag, n, dm, cur) * (1.0 / cheb_centre)
        iterate = update
    else:
        applied = operate(initial, im, level)
        cur = im - 1
        misfit = win(target, n, tm, cur) - applied
        update = misfit / win(diag, n, dm, cur) * (1.0 / cheb_centre)
        iterate = win(initial, n, im, cur) + update
    factor = 1.0 / cheb_ratio
    for repeat in range(CHEB - 1):
        applied = operate(iterate, cur, level)
        nxt = cur - 1
        misfit = win(target, n, tm, nxt) - applied
        factor_new = 1.0 / (2.0 * cheb_ratio - factor)
        update = factor_new * factor * win(update, n, cur, nxt) + 2.0 * factor_new / cheb_half * (
            misfit / win(diag, n, dm, nxt)
        )
        iterate = win(iterate, n, cur, nxt) + update
        cur = nxt
        factor = factor_new
    return iterate, cur


def fields_kernel(bounds_ref, table_ref, conc_ref, idf_ref, out_ref):
    rows = conc_ref.shape[0]
    shape = conc_ref.shape[1:]
    mats = table_ref.shape[1]
    col = lax.broadcasted_iota(jnp.int32, shape, 0)
    col_ok = (col >= bounds_ref[2]) & (col < bounds_ref[3])

    def body(i, carry):
        ids = idf_ref[i]
        conc = conc_ref[i]
        row = jnp.zeros(shape, jnp.int32) + i
        ok = col_ok & (row >= bounds_ref[0]) & (row < bounds_ref[1])
        vals = []
        for record in range(5):
            acc = jnp.zeros(shape, jnp.float32) + table_ref[record, mats - 1]
            for material in range(mats - 2, -1, -1):
                acc = jnp.where(ids == float(material), table_ref[record, material], acc)
            vals.append(acc)
        store = storage_scale * (1.0 + vals[3] * jnp.exp((vals[4] - 1.0) * jnp.log(conc)))
        out_ref[0, i] = jnp.where(ok, vals[0], 0.0)
        out_ref[1, i] = jnp.where(ok, vals[1], 0.0)
        out_ref[2, i] = jnp.where(ok, vals[2], 0.0)
        out_ref[3, i] = jnp.where(ok, store, 0.0)
        return carry

    lax.fori_loop(0, rows, body, 0)


def soil_fields(bounds, soil_table, conc, idf):
    cells = conc.size
    return pl.pallas_call(
        fields_kernel,
        out_shape=jax.ShapeDtypeStruct((4,) + conc.shape, jnp.float32),
        in_specs=[
            pl.BlockSpec(memory_space=pltpu.SMEM),
            pl.BlockSpec(memory_space=pltpu.SMEM),
            pl.BlockSpec(memory_space=pltpu.VMEM),
            pl.BlockSpec(memory_space=pltpu.VMEM),
        ],
        out_specs=pl.BlockSpec(memory_space=pltpu.VMEM),
        cost_estimate=pl.CostEstimate(
            flops=100 * cells, transcendentals=2 * cells, bytes_accessed=24 * cells
        ),
    )(bounds, soil_table, conc, idf)


def local(conc_prev, right_side, soil_id, soil_table):
    n = conc_prev.shape[0]
    ny = conc_prev.shape[1]
    hf = FINE_HALO
    gx_count = lax.axis_size("gx")
    gy_count = lax.axis_size("gy")
    ix = lax.axis_index("gx")
    iy = lax.axis_index("gy")

    stacked = jnp.stack([conc_prev, right_side, soil_id.astype(jnp.float32)])
    ext = halo(stacked, (("gx", 1), ("gy", 2)), hf)
    conc, rhs, idf = ext[0], ext[1], ext[2]
    x_lo = hf - ix * n
    y_lo = hf - iy * ny
    bounds = jnp.stack([x_lo, x_lo + gx_count * n, y_lo, y_lo + gy_count * ny]).astype(jnp.int32)
    fine_c = soil_fields(bounds, soil_table, conc, idf)
    fine = build_level(fine_c, n, hf, 1.0)

    x0, x0m = chebyshev(rhs, hf, None, 0, fine)
    r0 = win(rhs, n, hf, x0m - 1) - operate(x0, x0m, fine)
    r0m = x0m - 1
    nm = n // 2
    mm = hf // 2
    mid_c = coarsen(fine_c)
    mid = build_level(mid_c, nm, mm, 0.25)
    b1 = coarsen(win(r0, n, r0m, 2 * (r0m // 2)))
    b1m = r0m // 2
    x1, x1m = chebyshev(b1, b1m, None, 0, mid)
    r1 = win(b1, nm, b1m, x1m - 1) - operate(x1, x1m, mid)
    r1m = x1m - 1
    b2 = coarsen(win(r1, nm, r1m, 0))
    coarse_own = coarsen(win(mid_c, nm, mm, 0))

    nc = b2.shape[0]
    cpack = jnp.concatenate([b2[None], coarse_own], axis=0)
    mpack = jnp.stack([win(x1, nm, x1m, 0), win(b1, nm, b1m, 0)])
    hm = MID_HALO
    blocks = [cpack]
    for step in range(1, gy_count):
        pairs = [(j, (j - step) % gy_count) for j in range(gy_count)]
        blocks.append(lax.ppermute(cpack, "gy", pairs))
    north = shift_from(mpack[:, :, :hm], "gy", 1)
    south = shift_from(mpack[:, :, nm - hm :], "gy", -1)
    mext = jnp.concatenate([south, mpack, north], axis=2)
    full = jnp.concatenate(blocks, axis=2)
    full = jnp.roll(full, iy * nc, axis=2)
    reach = 3
    parts = [shift_from(full, "gx", -d) for d in range(reach, 0, -1)]
    parts += [full]
    parts += [shift_from(full, "gx", d) for d in range(1, reach + 1)]
    cpack = jnp.concatenate(parts, axis=1)
    west_m = shift_from(mext[:, nm - hm :], "gx", -1)
    east_m = shift_from(mext[:, :hm], "gx", 1)
    mext = jnp.concatenate([west_m, mext, east_m], axis=1)
    source = cpack[0]
    cc = cpack[1:]
    line_total = jnp.sum(source, axis=1)
    line_store = jnp.sum(cc[3], axis=1)
    line_mean = jnp.where(line_store > 0, line_total / jnp.where(line_store > 0, line_store, 1.0), 0.0)
    width = source.shape[0]
    ccp = jnp.pad(cc, ((0, 0), (0, 0), (1, 1), (0, 0)))
    kx_, ky_, kz_, st_ = ccp[0], ccp[1], ccp[2], ccp[3]
    q = 0.0625
    cx = kx_[1:-1, 1:-1]
    cy = ky_[1:-1, 1:-1]
    cz = kz_[1:-1, 1:-1]
    east = harmonic(kx_[2:, 1:-1], cx) * q
    west = harmonic(kx_[:-2, 1:-1], cx) * q
    north = harmonic(ky_[1:-1, 2:], cy) * q
    south = harmonic(ky_[1:-1, :-2], cy) * q
    vert = harmonic(cz[:, :, 1:], cz[:, :, :-1]) * q
    closed = jnp.zeros_like(cz[:, :, :1])
    above = jnp.concatenate([vert, closed], axis=2)
    below = jnp.concatenate([closed, vert], axis=2)
    cst = st_[1:-1, 1:-1]
    cdiag = jnp.maximum(cst + east + west + north + south + above + below, 0.01)
    csrc = source[1:-1]
    u = jnp.broadcast_to(line_mean[:, None, :], source.shape)
    for sweep in range(COARSE_SWEEPS):
        lo = sweep
        up = jnp.pad(u, ((0, 0), (1, 1), (0, 0)))
        centre = up[1:-1, 1:-1]
        sl = slice(lo, width - 2 - lo)
        upper = jnp.concatenate([centre[:, :, 1:], centre[:, :, :1]], axis=2)
        lower = jnp.concatenate([centre[:, :, -1:], centre[:, :, :-1]], axis=2)
        fl = east[sl] * (centre - up[2:, 1:-1]) + west[sl] * (centre - up[:-2, 1:-1])
        fl = fl + north[sl] * (centre - up[1:-1, 2:]) + south[sl] * (centre - up[1:-1, :-2])
        fl = fl + above[sl] * (centre - upper) + below[sl] * (centre - lower)
        applied = cst[sl] * centre + fl
        u = centre + jacobi_weight * ((csrc[sl] - applied) / cdiag[sl])
    um = (hm + 1) // 2
    have = reach * nc - COARSE_SWEEPS
    u = u[have - um : u.shape[0] - (have - um)]
    u = jnp.pad(u, ((0, 0), (um, um), (0, 0)))
    u = lax.dynamic_slice_in_dim(u, iy * nc, nc + 2 * um, 1)
    s1e = win(mext[0], nm, hm, hm) + win(prolong(u), nm, 2 * um, hm)
    b1e = mext[1]
    y1, y1m = chebyshev(b1e, hm, s1e, hm, mid)
    fm = 2 * y1m
    s0 = win(x0, n, x0m, fm) + prolong(y1)
    fs = min(fm, CHEB)
    s0 = win(s0, n, fm, fs)
    out, om = chebyshev(rhs, hf, s0, fs, fine)
    return out


def solution(mesh):
    placed = (P("gx", "gy", None), P("gx", "gy", None), P("gx", "gy", None), P())
    return jax.shard_map(
        local, mesh=mesh, in_specs=placed, out_specs=P("gx", "gy", None), check_vma=False
    )
```

```python
import jax
import jax.numpy as jnp
from jax import lax
from jax.sharding import PartitionSpec as P
from jax.experimental import pallas as pl
from jax.experimental.pallas import tpu as pltpu

CHEB = 3
COARSE_SWEEPS = 8

storage_scale = 0.05
cheb_centre = 1.1
cheb_half = 0.9
cheb_ratio = cheb_centre / cheb_half
jacobi_weight = 0.8

FINE_HALO = 10
MID_HALO = 5
HIGH = lax.Precision.HIGHEST


def shift_from(cells, axis, offset):
    count = lax.axis_size(axis)
    if offset > 0:
        pairs = [(i + offset, i) for i in range(count - offset)]
    else:
        pairs = [(i, i - offset) for i in range(count + offset)]
    if not pairs:
        return jnp.zeros_like(cells)
    return lax.ppermute(cells, axis, pairs)


def halo(cells, sides, width):
    for axis, dim in sides:
        size = cells.shape[dim]
        head = lax.slice_in_dim(cells, 0, width, axis=dim)
        tail = lax.slice_in_dim(cells, size - width, size, axis=dim)
        cells = jnp.concatenate(
            [shift_from(tail, axis, -1), cells, shift_from(head, axis, 1)], axis=dim
        )
    return cells


def pack(pieces):
    return jnp.concatenate([p.reshape(-1) for p in pieces])


def unpack(flat, pieces):
    out, at = [], 0
    for p in pieces:
        out.append(flat[at : at + p.size].reshape(p.shape))
        at += p.size
    return out


def harmonic(first, second):
    return first * second / jnp.maximum(0.5 * (first + second), 0.1)


def win(a, n, margin, r, dx=0, dy=0):
    lo = margin - r
    hi = margin + n + r
    return a[..., lo + dx : hi + dx, lo + dy : hi + dy, :]


def pair_matrix(size, dtype=jnp.float32):
    rows = jnp.arange(size)[:, None] // 2
    cols = jnp.arange(size // 2)[None, :]
    return (rows == cols).astype(dtype)


def coarsen(values):
    lead = values.shape[:-3]
    sx, sy, sz = values.shape[-3:]
    v = values.reshape(lead + (sx // 2, 2, sy, sz))
    v = v[..., 0, :, :] + v[..., 1, :, :]
    v = jnp.einsum("...yz,zw->...yw", v, pair_matrix(sz), precision=HIGH)
    rows = v.reshape((-1, sy, sz // 2))
    pick = jnp.broadcast_to(pair_matrix(sy).T, (rows.shape[0], sy // 2, sy))
    rows = lax.dot_general(pick, rows, (((2,), (1,)), ((0,), (0,))), precision=HIGH)
    v = rows.reshape(lead + (sx // 2, sy // 2, sz // 2))
    return v * 0.125


def prolong(values):
    sx, sy, sz = values.shape
    v = jnp.einsum("xyz,wz->xyw", values, pair_matrix(2 * sz), precision=HIGH)
    v = jnp.repeat(v, 2, axis=1)
    v = jnp.broadcast_to(v[:, None], (sx, 2) + v.shape[1:]).reshape((2 * sx,) + v.shape[1:])
    return v


def build_level(coeffs, n, margin, spacing):
    kx, ky, kz, store = coeffs[0], coeffs[1], coeffs[2], coeffs[3]
    fx = harmonic(kx[1:], kx[:-1]) * spacing
    fy = harmonic(ky[:, 1:], ky[:, :-1]) * spacing
    vertical = harmonic(kz[:, :, 1:], kz[:, :, :-1]) * spacing
    closed = jnp.zeros_like(kz[:, :, :1])
    above = jnp.concatenate([vertical, closed], axis=2)
    below = jnp.concatenate([closed, vertical], axis=2)
    level = dict(n=n, m=margin, fx=fx, fy=fy, above=above, below=below, store=store)
    r = margin - 1
    level["diag"] = jnp.maximum(faces_sum(level, r) + win(store, n, margin, r), 0.01)
    level["dm"] = r
    return level


def faces_sum(level, r):
    n, m = level["n"], level["m"]
    east = win(level["fx"], n, m, r)
    west = win(level["fx"], n, m, r, dx=-1)
    north = win(level["fy"], n, m, r)
    south = win(level["fy"], n, m, r, dy=-1)
    above = win(level["above"], n, m, r)
    below = win(level["below"], n, m, r)
    return east + west + north + south + above + below


def operate(values, vm, level):
    n, m = level["n"], level["m"]
    r = vm - 1
    centre = win(values, n, vm, r)
    upper = jnp.concatenate([centre[:, :, 1:], centre[:, :, :1]], axis=2)
    lower = jnp.concatenate([centre[:, :, -1:], centre[:, :, :-1]], axis=2)
    fx, fy = level["fx"], level["fy"]
    fluxes = win(fx, n, m, r) * (centre - win(values, n, vm, r, dx=1))
    fluxes = fluxes + win(fx, n, m, r, dx=-1) * (centre - win(values, n, vm, r, dx=-1))
    fluxes = fluxes + win(fy, n, m, r) * (centre - win(values, n, vm, r, dy=1))
    fluxes = fluxes + win(fy, n, m, r, dy=-1) * (centre - win(values, n, vm, r, dy=-1))
    fluxes = fluxes + win(level["above"], n, m, r) * (centre - upper)
    fluxes = fluxes + win(level["below"], n, m, r) * (centre - lower)
    return win(level["store"], n, m, r) * centre + fluxes


def chebyshev(target, tm, initial, im, level):
    n = level["n"]
    diag, dm = level["diag"], level["dm"]
    if initial is None:
        cur = min(tm, dm)
        misfit = win(target, n, tm, cur)
        update = misfit / win(diag, n, dm, cur) * (1.0 / cheb_centre)
        iterate = update
    else:
        applied = operate(initial, im, level)
        cur = im - 1
        misfit = win(target, n, tm, cur) - applied
        update = misfit / win(diag, n, dm, cur) * (1.0 / cheb_centre)
        iterate = win(initial, n, im, cur) + update
    factor = 1.0 / cheb_ratio
    for repeat in range(CHEB - 1):
        applied = operate(iterate, cur, level)
        nxt = cur - 1
        misfit = win(target, n, tm, nxt) - applied
        factor_new = 1.0 / (2.0 * cheb_ratio - factor)
        update = factor_new * factor * win(update, n, cur, nxt) + 2.0 * factor_new / cheb_half * (
            misfit / win(diag, n, dm, nxt)
        )
        iterate = win(iterate, n, cur, nxt) + update
        cur = nxt
        factor = factor_new
    return iterate, cur


def fields_kernel(bounds_ref, table_ref, conc_ref, idf_ref, out_ref):
    rows = conc_ref.shape[0]
    shape = conc_ref.shape[1:]
    mats = table_ref.shape[1]
    col = lax.broadcasted_iota(jnp.int32, shape, 0)
    col_ok = (col >= bounds_ref[2]) & (col < bounds_ref[3])

    def body(i, carry):
        ids = idf_ref[i]
        conc = conc_ref[i]
        row = jnp.zeros(shape, jnp.int32) + i
        ok = col_ok & (row >= bounds_ref[0]) & (row < bounds_ref[1])
        vals = []
        for record in range(5):
            acc = jnp.zeros(shape, jnp.float32) + table_ref[record, mats - 1]
            for material in range(mats - 2, -1, -1):
                acc = jnp.where(ids == float(material), table_ref[record, material], acc)
            vals.append(acc)
        store = storage_scale * (1.0 + vals[3] * jnp.exp((vals[4] - 1.0) * jnp.log(conc)))
        out_ref[0, i] = jnp.where(ok, vals[0], 0.0)
        out_ref[1, i] = jnp.where(ok, vals[1], 0.0)
        out_ref[2, i] = jnp.where(ok, vals[2], 0.0)
        out_ref[3, i] = jnp.where(ok, store, 0.0)
        return carry

    lax.fori_loop(0, rows, body, 0)


def soil_fields(bounds, soil_table, conc, idf):
    cells = conc.size
    return pl.pallas_call(
        fields_kernel,
        out_shape=jax.ShapeDtypeStruct((4,) + conc.shape, jnp.float32),
        in_specs=[
            pl.BlockSpec(memory_space=pltpu.SMEM),
            pl.BlockSpec(memory_space=pltpu.SMEM),
            pl.BlockSpec(memory_space=pltpu.VMEM),
            pl.BlockSpec(memory_space=pltpu.VMEM),
        ],
        out_specs=pl.BlockSpec(memory_space=pltpu.VMEM),
        cost_estimate=pl.CostEstimate(
            flops=100 * cells, transcendentals=2 * cells, bytes_accessed=24 * cells
        ),
    )(bounds, soil_table, conc, idf)


def local(conc_prev, right_side, soil_id, soil_table):
    n = conc_prev.shape[0]
    ny = conc_prev.shape[1]
    hf = FINE_HALO
    gx_count = lax.axis_size("gx")
    gy_count = lax.axis_size("gy")
    ix = lax.axis_index("gx")
    iy = lax.axis_index("gy")

    stacked = jnp.stack([conc_prev, right_side, soil_id.astype(jnp.float32)])
    ext = halo(stacked, (("gx", 1), ("gy", 2)), hf)
    conc, rhs, idf = ext[0], ext[1], ext[2]
    x_lo = hf - ix * n
    y_lo = hf - iy * ny
    bounds = jnp.stack([x_lo, x_lo + gx_count * n, y_lo, y_lo + gy_count * ny]).astype(jnp.int32)
    fine_c = soil_fields(bounds, soil_table, conc, idf)
    fine = build_level(fine_c, n, hf, 1.0)

    x0, x0m = chebyshev(rhs, hf, None, 0, fine)
    r0 = win(rhs, n, hf, x0m - 1) - operate(x0, x0m, fine)
    r0m = x0m - 1
    nm = n // 2
    mm = hf // 2
    mid_c = coarsen(fine_c)
    mid = build_level(mid_c, nm, mm, 0.25)
    b1 = coarsen(win(r0, n, r0m, 2 * (r0m // 2)))
    b1m = r0m // 2
    x1, x1m = chebyshev(b1, b1m, None, 0, mid)
    r1 = win(b1, nm, b1m, x1m - 1) - operate(x1, x1m, mid)
    r1m = x1m - 1
    b2 = coarsen(win(r1, nm, r1m, 0))
    coarse_own = coarsen(win(mid_c, nm, mm, 0))

    nc = b2.shape[0]
    cpack = jnp.concatenate([b2[None], coarse_own], axis=0)
    mpack = jnp.stack([win(x1, nm, x1m, 0), win(b1, nm, b1m, 0)])
    hm = MID_HALO
    north_slab = mpack[:, :, :hm]
    south_slab = mpack[:, :, nm - hm :]
    blocks = [cpack]
    north = south = None
    for step in range(1, gy_count):
        pairs = [(j, (j - step) % gy_count) for j in range(gy_count)]
        pieces = [cpack]
        if step == 1:
            pieces.append(north_slab)
        if step == gy_count - 1:
            pieces.append(south_slab)
        got = unpack(lax.ppermute(pack(pieces), "gy", pairs), pieces)
        blocks.append(got[0])
        if step == 1:
            north = got[1]
        if step == gy_count - 1:
            south = got[-1]
    if gy_count == 1:
        north = jnp.zeros_like(north_slab)
        south = jnp.zeros_like(south_slab)
    north = jnp.where(iy < gy_count - 1, north, 0.0)
    south = jnp.where(iy > 0, south, 0.0)
    mext = jnp.concatenate([south, mpack, north], axis=2)
    full = jnp.zeros(cpack.shape[:2] + (nc * gy_count,) + cpack.shape[3:], cpack.dtype)
    for step, block in enumerate(blocks):
        at = ((iy + step) % gy_count) * nc
        full = lax.dynamic_update_slice_in_dim(full, block, at, axis=2)
    reach = 3
    west_slab = mext[:, nm - hm :]
    east_slab = mext[:, :hm]
    before, after = [], []
    west_m = east_m = None
    for d in range(1, reach + 1):
        if d == 1:
            got = unpack(shift_from(pack([full, west_slab]), "gx", -1), [full, west_slab])
            before.append(got[0])
            west_m = got[1]
            got = unpack(shift_from(pack([full, east_slab]), "gx", 1), [full, east_slab])
            after.append(got[0])
            east_m = got[1]
        else:
            before.append(shift_from(full, "gx", -d))
            after.append(shift_from(full, "gx", d))
    cpack = jnp.concatenate(before[::-1] + [full] + after, axis=1)
    mext = jnp.concatenate([west_m, mext, east_m], axis=1)
    source = cpack[0]
    cc = cpack[1:]
    line_total = jnp.sum(source, axis=1)
    line_store = jnp.sum(cc[3], axis=1)
    line_mean = jnp.where(line_store > 0, line_total / jnp.where(line_store > 0, line_store, 1.0), 0.0)
    width = source.shape[0]
    ccp = jnp.pad(cc, ((0, 0), (0, 0), (1, 1), (0, 0)))
    kx_, ky_, kz_, st_ = ccp[0], ccp[1], ccp[2], ccp[3]
    q = 0.0625
    cx = kx_[1:-1, 1:-1]
    cy = ky_[1:-1, 1:-1]
    cz = kz_[1:-1, 1:-1]
    east = harmonic(kx_[2:, 1:-1], cx) * q
    west = harmonic(kx_[:-2, 1:-1], cx) * q
    north = harmonic(ky_[1:-1, 2:], cy) * q
    south = harmonic(ky_[1:-1, :-2], cy) * q
    vert = harmonic(cz[:, :, 1:], cz[:, :, :-1]) * q
    closed = jnp.zeros_like(cz[:, :, :1])
    above = jnp.concatenate([vert, closed], axis=2)
    below = jnp.concatenate([closed, vert], axis=2)
    cst = st_[1:-1, 1:-1]
    cdiag = jnp.maximum(cst + east + west + north + south + above + below, 0.01)
    csrc = source[1:-1]
    u = jnp.broadcast_to(line_mean[:, None, :], source.shape)
    for sweep in range(COARSE_SWEEPS):
        lo = sweep
        up = jnp.pad(u, ((0, 0), (1, 1), (0, 0)))
        centre = up[1:-1, 1:-1]
        sl = slice(lo, width - 2 - lo)
        upper = jnp.concatenate([centre[:, :, 1:], centre[:, :, :1]], axis=2)
        lower = jnp.concatenate([centre[:, :, -1:], centre[:, :, :-1]], axis=2)
        fl = east[sl] * (centre - up[2:, 1:-1]) + west[sl] * (centre - up[:-2, 1:-1])
        fl = fl + north[sl] * (centre - up[1:-1, 2:]) + south[sl] * (centre - up[1:-1, :-2])
        fl = fl + above[sl] * (centre - upper) + below[sl] * (centre - lower)
        applied = cst[sl] * centre + fl
        u = centre + jacobi_weight * ((csrc[sl] - applied) / cdiag[sl])
    um = (hm + 1) // 2
    have = reach * nc - COARSE_SWEEPS
    u = u[have - um : u.shape[0] - (have - um)]
    u = jnp.pad(u, ((0, 0), (um, um), (0, 0)))
    u = lax.dynamic_slice_in_dim(u, iy * nc, nc + 2 * um, 1)
    s1e = win(mext[0], nm, hm, hm) + win(prolong(u), nm, 2 * um, hm)
    b1e = mext[1]
    y1, y1m = chebyshev(b1e, hm, s1e, hm, mid)
    fm = 2 * y1m
    s0 = win(x0, n, x0m, fm) + prolong(y1)
    fs = min(fm, CHEB)
    s0 = win(s0, n, fm, fs)
    out, om = chebyshev(rhs, hf, s0, fs, fine)
    return out


def solution(mesh):
    placed = (P("gx", "gy", None), P("gx", "gy", None), P("gx", "gy", None), P())
    return jax.shard_map(
        local, mesh=mesh, in_specs=placed, out_specs=P("gx", "gy", None), check_vma=False
    )
```

```python
import jax
import jax.numpy as jnp
from jax import lax
from jax.sharding import PartitionSpec as P
from jax.experimental import pallas as pl
from jax.experimental.pallas import tpu as pltpu

CHEB = 3
COARSE_SWEEPS = 8

storage_scale = 0.05
cheb_centre = 1.1
cheb_half = 0.9
cheb_ratio = cheb_centre / cheb_half
jacobi_weight = 0.8

FINE_HALO = 10
MID_HALO = 5
HIGH = lax.Precision.HIGHEST


def shift_from(cells, axis, offset):
    count = lax.axis_size(axis)
    if offset > 0:
        pairs = [(i + offset, i) for i in range(count - offset)]
    else:
        pairs = [(i, i - offset) for i in range(count + offset)]
    if not pairs:
        return jnp.zeros_like(cells)
    return lax.ppermute(cells, axis, pairs)


def halo(cells, sides, width):
    for axis, dim in sides:
        size = cells.shape[dim]
        head = lax.slice_in_dim(cells, 0, width, axis=dim)
        tail = lax.slice_in_dim(cells, size - width, size, axis=dim)
        cells = jnp.concatenate(
            [shift_from(tail, axis, -1), cells, shift_from(head, axis, 1)], axis=dim
        )
    return cells


def harmonic(first, second):
    return first * second / jnp.maximum(0.5 * (first + second), 0.1)


def win(a, n, margin, r, dx=0, dy=0):
    lo = margin - r
    hi = margin + n + r
    return a[..., lo + dx : hi + dx, lo + dy : hi + dy, :]


def pair_matrix(size, dtype=jnp.float32):
    rows = jnp.arange(size)[:, None] // 2
    cols = jnp.arange(size // 2)[None, :]
    return (rows == cols).astype(dtype)


def coarsen(values):
    lead = values.shape[:-3]
    sx, sy, sz = values.shape[-3:]
    v = values.reshape(lead + (sx // 2, 2, sy, sz))
    v = v[..., 0, :, :] + v[..., 1, :, :]
    v = jnp.einsum("...yz,zw->...yw", v, pair_matrix(sz), precision=HIGH)
    rows = v.reshape((-1, sy, sz // 2))
    pick = jnp.broadcast_to(pair_matrix(sy).T, (rows.shape[0], sy // 2, sy))
    rows = lax.dot_general(pick, rows, (((2,), (1,)), ((0,), (0,))), precision=HIGH)
    v = rows.reshape(lead + (sx // 2, sy // 2, sz // 2))
    return v * 0.125


def prolong(values):
    sx, sy, sz = values.shape
    v = jnp.einsum("xyz,wz->xyw", values, pair_matrix(2 * sz), precision=HIGH)
    pick = jnp.broadcast_to(pair_matrix(2 * sy), (sx, 2 * sy, sy))
    v = lax.dot_general(pick, v, (((2,), (1,)), ((0,), (0,))), precision=HIGH)
    v = jnp.broadcast_to(v[:, None], (sx, 2) + v.shape[1:]).reshape((2 * sx,) + v.shape[1:])
    return v


def build_level(coeffs, n, margin, spacing):
    kx, ky, kz, store = coeffs[0], coeffs[1], coeffs[2], coeffs[3]
    fx = harmonic(kx[1:], kx[:-1]) * spacing
    fy = harmonic(ky[:, 1:], ky[:, :-1]) * spacing
    vertical = harmonic(kz[:, :, 1:], kz[:, :, :-1]) * spacing
    closed = jnp.zeros_like(kz[:, :, :1])
    above = jnp.concatenate([vertical, closed], axis=2)
    below = jnp.concatenate([closed, vertical], axis=2)
    level = dict(n=n, m=margin, fx=fx, fy=fy, above=above, below=below, store=store)
    r = margin - 1
    level["diag"] = jnp.maximum(faces_sum(level, r) + win(store, n, margin, r), 0.01)
    level["dm"] = r
    return level


def faces_sum(level, r):
    n, m = level["n"], level["m"]
    east = win(level["fx"], n, m, r)
    west = win(level["fx"], n, m, r, dx=-1)
    north = win(level["fy"], n, m, r)
    south = win(level["fy"], n, m, r, dy=-1)
    above = win(level["above"], n, m, r)
    below = win(level["below"], n, m, r)
    return east + west + north + south + above + below


def operate(values, vm, level):
    n, m = level["n"], level["m"]
    r = vm - 1
    centre = win(values, n, vm, r)
    upper = jnp.concatenate([centre[:, :, 1:], centre[:, :, :1]], axis=2)
    lower = jnp.concatenate([centre[:, :, -1:], centre[:, :, :-1]], axis=2)
    fx, fy = level["fx"], level["fy"]
    fluxes = win(fx, n, m, r) * (centre - win(values, n, vm, r, dx=1))
    fluxes = fluxes + win(fx, n, m, r, dx=-1) * (centre - win(values, n, vm, r, dx=-1))
    fluxes = fluxes + win(fy, n, m, r) * (centre - win(values, n, vm, r, dy=1))
    fluxes = fluxes + win(fy, n, m, r, dy=-1) * (centre - win(values, n, vm, r, dy=-1))
    fluxes = fluxes + win(level["above"], n, m, r) * (centre - upper)
    fluxes = fluxes + win(level["below"], n, m, r) * (centre - lower)
    return win(level["store"], n, m, r) * centre + fluxes


def chebyshev(target, tm, initial, im, level):
    n = level["n"]
    diag, dm = level["diag"], level["dm"]
    if initial is None:
        cur = min(tm, dm)
        misfit = win(target, n, tm, cur)
        update = misfit / win(diag, n, dm, cur) * (1.0 / cheb_centre)
        iterate = update
    else:
        applied = operate(initial, im, level)
        cur = im - 1
        misfit = win(target, n, tm, cur) - applied
        update = misfit / win(diag, n, dm, cur) * (1.0 / cheb_centre)
        iterate = win(initial, n, im, cur) + update
    factor = 1.0 / cheb_ratio
    for repeat in range(CHEB - 1):
        applied = operate(iterate, cur, level)
        nxt = cur - 1
        misfit = win(target, n, tm, nxt) - applied
        factor_new = 1.0 / (2.0 * cheb_ratio - factor)
        update = factor_new * factor * win(update, n, cur, nxt) + 2.0 * factor_new / cheb_half * (
            misfit / win(diag, n, dm, nxt)
        )
        iterate = win(iterate, n, cur, nxt) + update
        cur = nxt
        factor = factor_new
    return iterate, cur


def fields_kernel(bounds_ref, table_ref, conc_ref, idf_ref, out_ref):
    rows = conc_ref.shape[0]
    shape = conc_ref.shape[1:]
    mats = table_ref.shape[1]
    col = lax.broadcasted_iota(jnp.int32, shape, 0)
    col_ok = (col >= bounds_ref[2]) & (col < bounds_ref[3])

    def body(i, carry):
        ids = idf_ref[i]
        conc = conc_ref[i]
        row = jnp.zeros(shape, jnp.int32) + i
        ok = col_ok & (row >= bounds_ref[0]) & (row < bounds_ref[1])
        vals = []
        for record in range(5):
            acc = jnp.zeros(shape, jnp.float32) + table_ref[record, mats - 1]
            for material in range(mats - 2, -1, -1):
                acc = jnp.where(ids == float(material), table_ref[record, material], acc)
            vals.append(acc)
        store = storage_scale * (1.0 + vals[3] * jnp.exp((vals[4] - 1.0) * jnp.log(conc)))
        out_ref[0, i] = jnp.where(ok, vals[0], 0.0)
        out_ref[1, i] = jnp.where(ok, vals[1], 0.0)
        out_ref[2, i] = jnp.where(ok, vals[2], 0.0)
        out_ref[3, i] = jnp.where(ok, store, 0.0)
        return carry

    lax.fori_loop(0, rows, body, 0)


def soil_fields(bounds, soil_table, conc, idf):
    cells = conc.size
    return pl.pallas_call(
        fields_kernel,
        out_shape=jax.ShapeDtypeStruct((4,) + conc.shape, jnp.float32),
        in_specs=[
            pl.BlockSpec(memory_space=pltpu.SMEM),
            pl.BlockSpec(memory_space=pltpu.SMEM),
            pl.BlockSpec(memory_space=pltpu.VMEM),
            pl.BlockSpec(memory_space=pltpu.VMEM),
        ],
        out_specs=pl.BlockSpec(memory_space=pltpu.VMEM),
        cost_estimate=pl.CostEstimate(
            flops=100 * cells, transcendentals=2 * cells, bytes_accessed=24 * cells
        ),
    )(bounds, soil_table, conc, idf)


def local(conc_prev, right_side, soil_id, soil_table):
    n = conc_prev.shape[0]
    ny = conc_prev.shape[1]
    hf = FINE_HALO
    gx_count = lax.axis_size("gx")
    gy_count = lax.axis_size("gy")
    ix = lax.axis_index("gx")
    iy = lax.axis_index("gy")

    stacked = jnp.stack([conc_prev, right_side, soil_id.astype(jnp.float32)])
    ext = halo(stacked, (("gx", 1), ("gy", 2)), hf)
    conc, rhs, idf = ext[0], ext[1], ext[2]
    x_lo = hf - ix * n
    y_lo = hf - iy * ny
    bounds = jnp.stack([x_lo, x_lo + gx_count * n, y_lo, y_lo + gy_count * ny]).astype(jnp.int32)
    fine_c = soil_fields(bounds, soil_table, conc, idf)
    fine = build_level(fine_c, n, hf, 1.0)

    x0, x0m = chebyshev(rhs, hf, None, 0, fine)
    r0 = win(rhs, n, hf, x0m - 1) - operate(x0, x0m, fine)
    r0m = x0m - 1
    nm = n // 2
    mm = hf // 2
    mid_c = coarsen(fine_c)
    mid = build_level(mid_c, nm, mm, 0.25)
    b1 = coarsen(win(r0, n, r0m, 2 * (r0m // 2)))
    b1m = r0m // 2
    x1, x1m = chebyshev(b1, b1m, None, 0, mid)
    r1 = win(b1, nm, b1m, x1m - 1) - operate(x1, x1m, mid)
    r1m = x1m - 1
    b2 = coarsen(win(r1, nm, r1m, 0))
    coarse_own = coarsen(win(mid_c, nm, mm, 0))

    nc = b2.shape[0]
    cpack = jnp.concatenate([b2[None], coarse_own], axis=0)
    mpack = jnp.stack([win(x1, nm, x1m, 0), win(b1, nm, b1m, 0)])
    hm = MID_HALO
    blocks = [cpack]
    for step in range(1, gy_count):
        pairs = [(j, (j - step) % gy_count) for j in range(gy_count)]
        blocks.append(lax.ppermute(cpack, "gy", pairs))
    north = shift_from(mpack[:, :, :hm], "gy", 1)
    south = shift_from(mpack[:, :, nm - hm :], "gy", -1)
    mext = jnp.concatenate([south, mpack, north], axis=2)
    full = jnp.concatenate(blocks, axis=2)
    reach = 3
    parts = [shift_from(full, "gx", -d) for d in range(reach, 0, -1)]
    parts += [full]
    parts += [shift_from(full, "gx", d) for d in range(1, reach + 1)]
    cpack = jnp.concatenate(parts, axis=1)
    west_m = shift_from(mext[:, nm - hm :], "gx", -1)
    east_m = shift_from(mext[:, :hm], "gx", 1)
    mext = jnp.concatenate([west_m, mext, east_m], axis=1)
    source = cpack[0]
    cc = cpack[1:]
    line_total = jnp.sum(source, axis=1)
    line_store = jnp.sum(cc[3], axis=1)
    line_mean = jnp.where(line_store > 0, line_total / jnp.where(line_store > 0, line_store, 1.0), 0.0)
    width = source.shape[0]
    lines = source.shape[1]
    gline = (iy * nc + jnp.arange(lines)) % lines
    kx_, ky_, kz_, st_ = cc[0], cc[1], cc[2], cc[3]
    q = 0.0625
    cx = kx_[1:-1]
    cy = ky_[1:-1]
    cz = kz_[1:-1]
    east = harmonic(kx_[2:], cx) * q
    west = harmonic(kx_[:-2], cx) * q
    north = harmonic(jnp.roll(cy, -1, axis=1), cy) * q
    north = jnp.where((gline != lines - 1)[None, :, None], north, 0.0)
    south = jnp.roll(north, 1, axis=1)
    vert = harmonic(cz[:, :, 1:], cz[:, :, :-1]) * q
    closed = jnp.zeros_like(cz[:, :, :1])
    above = jnp.concatenate([vert, closed], axis=2)
    below = jnp.concatenate([closed, vert], axis=2)
    cst = st_[1:-1]
    cdiag = jnp.maximum(cst + east + west + north + south + above + below, 0.01)
    csrc = source[1:-1]
    u = jnp.broadcast_to(line_mean[:, None, :], source.shape)
    for sweep in range(COARSE_SWEEPS):
        lo = sweep
        centre = u[1:-1]
        sl = slice(lo, width - 2 - lo)
        upper = jnp.concatenate([centre[:, :, 1:], centre[:, :, :1]], axis=2)
        lower = jnp.concatenate([centre[:, :, -1:], centre[:, :, :-1]], axis=2)
        fl = east[sl] * (centre - u[2:]) + west[sl] * (centre - u[:-2])
        fl = fl + north[sl] * (centre - jnp.roll(centre, -1, axis=1))
        fl = fl + south[sl] * (centre - jnp.roll(centre, 1, axis=1))
        fl = fl + above[sl] * (centre - upper) + below[sl] * (centre - lower)
        applied = cst[sl] * centre + fl
        u = centre + jacobi_weight * ((csrc[sl] - applied) / cdiag[sl])
    um = (hm + 1) // 2
    have = reach * nc - COARSE_SWEEPS
    u = u[have - um : u.shape[0] - (have - um)]
    rows = [(k % lines) for k in range(-um, nc + um)]
    runs = []
    for r in rows:
        if runs and runs[-1][1] == r:
            runs[-1][1] = r + 1
        else:
            runs.append([r, r + 1])
    u = jnp.concatenate([u[:, a:b] for a, b in runs], axis=1)
    kept = iy * nc + jnp.arange(-um, nc + um)
    u = jnp.where(((kept >= 0) & (kept < lines))[None, :, None], u, 0.0)
    s1e = win(mext[0], nm, hm, hm) + win(prolong(u), nm, 2 * um, hm)
    b1e = mext[1]
    y1, y1m = chebyshev(b1e, hm, s1e, hm, mid)
    fm = 2 * y1m
    s0 = win(x0, n, x0m, fm) + prolong(y1)
    fs = min(fm, CHEB)
    s0 = win(s0, n, fm, fs)
    out, om = chebyshev(rhs, hf, s0, fs, fine)
    return out


def solution(mesh):
    placed = (P("gx", "gy", None), P("gx", "gy", None), P("gx", "gy", None), P())
    return jax.shard_map(
        local, mesh=mesh, in_specs=placed, out_specs=P("gx", "gy", None), check_vma=False
    )
```

```python
import jax
import jax.numpy as jnp
from jax import lax
from jax.sharding import PartitionSpec as P
from jax.experimental import pallas as pl
from jax.experimental.pallas import tpu as pltpu

CHEB = 3
COARSE_SWEEPS = 8

storage_scale = 0.05
cheb_centre = 1.1
cheb_half = 0.9
cheb_ratio = cheb_centre / cheb_half
jacobi_weight = 0.8

FINE_HALO = 10
MID_HALO = 5
HIGH = lax.Precision.HIGHEST


def shift_from(cells, axis, offset):
    count = lax.axis_size(axis)
    if offset > 0:
        pairs = [(i + offset, i) for i in range(count - offset)]
    else:
        pairs = [(i, i - offset) for i in range(count + offset)]
    if not pairs:
        return jnp.zeros_like(cells)
    return lax.ppermute(cells, axis, pairs)


def halo(cells, sides, width):
    for axis, dim in sides:
        size = cells.shape[dim]
        head = lax.slice_in_dim(cells, 0, width, axis=dim)
        tail = lax.slice_in_dim(cells, size - width, size, axis=dim)
        cells = jnp.concatenate(
            [shift_from(tail, axis, -1), cells, shift_from(head, axis, 1)], axis=dim
        )
    return cells


def harmonic(first, second):
    return first * second / jnp.maximum(0.5 * (first + second), 0.1)


def win(a, n, margin, r, dx=0, dy=0):
    lo = margin - r
    hi = margin + n + r
    return a[..., lo + dx : hi + dx, lo + dy : hi + dy, :]


def pair_matrix(size, dtype=jnp.float32):
    rows = jnp.arange(size)[:, None] // 2
    cols = jnp.arange(size // 2)[None, :]
    return (rows == cols).astype(dtype)


def coarsen(values):
    lead = values.shape[:-3]
    sx, sy, sz = values.shape[-3:]
    v = values.reshape(lead + (sx // 2, 2, sy, sz))
    v = v[..., 0, :, :] + v[..., 1, :, :]
    v = jnp.einsum("...yz,zw->...yw", v, pair_matrix(sz), precision=HIGH)
    rows = v.reshape((-1, sy, sz // 2))
    pick = jnp.broadcast_to(pair_matrix(sy).T, (rows.shape[0], sy // 2, sy))
    rows = lax.dot_general(pick, rows, (((2,), (1,)), ((0,), (0,))), precision=HIGH)
    v = rows.reshape(lead + (sx // 2, sy // 2, sz // 2))
    return v * 0.125


def prolong(values):
    sx, sy, sz = values.shape
    v = jnp.einsum("xyz,wz->xyw", values, pair_matrix(2 * sz), precision=HIGH)
    pick = jnp.broadcast_to(pair_matrix(2 * sy), (sx, 2 * sy, sy))
    v = lax.dot_general(pick, v, (((2,), (1,)), ((0,), (0,))), precision=HIGH)
    v = jnp.broadcast_to(v[:, None], (sx, 2) + v.shape[1:]).reshape((2 * sx,) + v.shape[1:])
    return v


def build_level(coeffs, n, margin, spacing):
    kx, ky, kz, store = coeffs[0], coeffs[1], coeffs[2], coeffs[3]
    fx = harmonic(kx[1:], kx[:-1]) * spacing
    fy = harmonic(ky[:, 1:], ky[:, :-1]) * spacing
    vertical = harmonic(kz[:, :, 1:], kz[:, :, :-1]) * spacing
    closed = jnp.zeros_like(kz[:, :, :1])
    above = jnp.concatenate([vertical, closed], axis=2)
    below = jnp.concatenate([closed, vertical], axis=2)
    level = dict(n=n, m=margin, fx=fx, fy=fy, above=above, below=below, store=store)
    r = margin - 1
    level["diag"] = jnp.maximum(faces_sum(level, r) + win(store, n, margin, r), 0.01)
    level["dm"] = r
    return level


def faces_sum(level, r):
    n, m = level["n"], level["m"]
    east = win(level["fx"], n, m, r)
    west = win(level["fx"], n, m, r, dx=-1)
    north = win(level["fy"], n, m, r)
    south = win(level["fy"], n, m, r, dy=-1)
    above = win(level["above"], n, m, r)
    below = win(level["below"], n, m, r)
    return east + west + north + south + above + below


def operate(values, vm, level):
    n, m = level["n"], level["m"]
    r = vm - 1
    centre = win(values, n, vm, r)
    upper = jnp.concatenate([centre[:, :, 1:], centre[:, :, :1]], axis=2)
    lower = jnp.concatenate([centre[:, :, -1:], centre[:, :, :-1]], axis=2)
    fx, fy = level["fx"], level["fy"]
    fluxes = win(fx, n, m, r) * (centre - win(values, n, vm, r, dx=1))
    fluxes = fluxes + win(fx, n, m, r, dx=-1) * (centre - win(values, n, vm, r, dx=-1))
    fluxes = fluxes + win(fy, n, m, r) * (centre - win(values, n, vm, r, dy=1))
    fluxes = fluxes + win(fy, n, m, r, dy=-1) * (centre - win(values, n, vm, r, dy=-1))
    fluxes = fluxes + win(level["above"], n, m, r) * (centre - upper)
    fluxes = fluxes + win(level["below"], n, m, r) * (centre - lower)
    return win(level["store"], n, m, r) * centre + fluxes


def chebyshev(target, tm, initial, im, level):
    n = level["n"]
    diag, dm = level["diag"], level["dm"]
    if initial is None:
        cur = min(tm, dm)
        misfit = win(target, n, tm, cur)
        update = misfit / win(diag, n, dm, cur) * (1.0 / cheb_centre)
        iterate = update
    else:
        applied = operate(initial, im, level)
        cur = im - 1
        misfit = win(target, n, tm, cur) - applied
        update = misfit / win(diag, n, dm, cur) * (1.0 / cheb_centre)
        iterate = win(initial, n, im, cur) + update
    factor = 1.0 / cheb_ratio
    for repeat in range(CHEB - 1):
        applied = operate(iterate, cur, level)
        nxt = cur - 1
        misfit = win(target, n, tm, nxt) - applied
        factor_new = 1.0 / (2.0 * cheb_ratio - factor)
        update = factor_new * factor * win(update, n, cur, nxt) + 2.0 * factor_new / cheb_half * (
            misfit / win(diag, n, dm, nxt)
        )
        iterate = win(iterate, n, cur, nxt) + update
        cur = nxt
        factor = factor_new
    return iterate, cur


def fields_kernel(bounds_ref, table_ref, ext_ref, kx_ref, ky_ref, kz_ref, st_ref):
    rows = ext_ref.shape[1]
    shape = ext_ref.shape[2:]
    mats = table_ref.shape[1]
    col = lax.broadcasted_iota(jnp.int32, shape, 0)
    col_ok = (col >= bounds_ref[2]) & (col < bounds_ref[3])
    table = [[table_ref[record, material] for material in range(mats)] for record in range(5)]
    outs = (kx_ref, ky_ref, kz_ref)

    def body(i, carry):
        conc = ext_ref[0, i]
        ids = ext_ref[2, i]
        row = jnp.zeros(shape, jnp.int32) + i
        ok = col_ok & (row >= bounds_ref[0]) & (row < bounds_ref[1])
        masks = [ids == float(material) for material in range(mats - 1)]
        vals = []
        for record in range(5):
            acc = jnp.zeros(shape, jnp.float32) + table[record][mats - 1]
            for material in range(mats - 2, -1, -1):
                acc = jnp.where(masks[material], table[record][material], acc)
            vals.append(acc)
        store = storage_scale * (1.0 + vals[3] * jnp.exp((vals[4] - 1.0) * jnp.log(conc)))
        for record in range(3):
            outs[record][i] = jnp.where(ok, vals[record], 0.0)
        st_ref[i] = jnp.where(ok, store, 0.0)
        return carry

    lax.fori_loop(0, rows, body, 0)


def soil_fields(bounds, soil_table, ext):
    frame = ext.shape[1:]
    cells = ext[0].size
    field = jax.ShapeDtypeStruct(frame, jnp.float32)
    return pl.pallas_call(
        fields_kernel,
        out_shape=(field, field, field, field),
        in_specs=[
            pl.BlockSpec(memory_space=pltpu.SMEM),
            pl.BlockSpec(memory_space=pltpu.SMEM),
            pl.BlockSpec(memory_space=pltpu.VMEM),
        ],
        out_specs=tuple(pl.BlockSpec(memory_space=pltpu.VMEM) for _ in range(4)),
        cost_estimate=pl.CostEstimate(
            flops=100 * cells, transcendentals=2 * cells, bytes_accessed=28 * cells
        ),
    )(bounds, soil_table, ext)


def local(conc_prev, right_side, soil_id, soil_table):
    n = conc_prev.shape[0]
    ny = conc_prev.shape[1]
    hf = FINE_HALO
    gx_count = lax.axis_size("gx")
    gy_count = lax.axis_size("gy")
    ix = lax.axis_index("gx")
    iy = lax.axis_index("gy")

    stacked = jnp.stack([conc_prev, right_side, soil_id.astype(jnp.float32)])
    ext = halo(stacked, (("gx", 1), ("gy", 2)), hf)
    rhs = ext[1]
    x_lo = hf - ix * n
    y_lo = hf - iy * ny
    bounds = jnp.stack([x_lo, x_lo + gx_count * n, y_lo, y_lo + gy_count * ny]).astype(jnp.int32)
    fine_c = jnp.stack(soil_fields(bounds, soil_table, ext))
    fine = build_level(fine_c, n, hf, 1.0)

    x0, x0m = chebyshev(rhs, hf, None, 0, fine)
    r0 = win(rhs, n, hf, x0m - 1) - operate(x0, x0m, fine)
    r0m = x0m - 1
    nm = n // 2
    mm = hf // 2
    mid_c = coarsen(fine_c)
    mid = build_level(mid_c, nm, mm, 0.25)
    b1 = coarsen(win(r0, n, r0m, 2 * (r0m // 2)))
    b1m = r0m // 2
    x1, x1m = chebyshev(b1, b1m, None, 0, mid)
    r1 = win(b1, nm, b1m, x1m - 1) - operate(x1, x1m, mid)
    r1m = x1m - 1
    b2 = coarsen(win(r1, nm, r1m, 0))
    coarse_own = coarsen(win(mid_c, nm, mm, 0))

    nc = b2.shape[0]
    cpack = jnp.concatenate([b2[None], coarse_own], axis=0)
    mpack = jnp.stack([win(x1, nm, x1m, 0), win(b1, nm, b1m, 0)])
    hm = MID_HALO
    blocks = [cpack]
    for step in range(1, gy_count):
        pairs = [(j, (j - step) % gy_count) for j in range(gy_count)]
        blocks.append(lax.ppermute(cpack, "gy", pairs))
    north = shift_from(mpack[:, :, :hm], "gy", 1)
    south = shift_from(mpack[:, :, nm - hm :], "gy", -1)
    mext = jnp.concatenate([south, mpack, north], axis=2)
    full = jnp.concatenate(blocks, axis=2)
    reach = 3
    parts = [shift_from(full, "gx", -d) for d in range(reach, 0, -1)]
    parts += [full]
    parts += [shift_from(full, "gx", d) for d in range(1, reach + 1)]
    cpack = jnp.concatenate(parts, axis=1)
    west_m = shift_from(mext[:, nm - hm :], "gx", -1)
    east_m = shift_from(mext[:, :hm], "gx", 1)
    mext = jnp.concatenate([west_m, mext, east_m], axis=1)
    source = cpack[0]
    cc = cpack[1:]
    line_total = jnp.sum(source, axis=1)
    line_store = jnp.sum(cc[3], axis=1)
    line_mean = jnp.where(line_store > 0, line_total / jnp.where(line_store > 0, line_store, 1.0), 0.0)
    width = source.shape[0]
    lines = source.shape[1]
    gline = (iy * nc + jnp.arange(lines)) % lines
    kx_, ky_, kz_, st_ = cc[0], cc[1], cc[2], cc[3]
    q = 0.0625
    cx = kx_[1:-1]
    cy = ky_[1:-1]
    cz = kz_[1:-1]
    east = harmonic(kx_[2:], cx) * q
    west = harmonic(kx_[:-2], cx) * q
    north = harmonic(jnp.roll(cy, -1, axis=1), cy) * q
    north = jnp.where((gline != lines - 1)[None, :, None], north, 0.0)
    south = jnp.roll(north, 1, axis=1)
    vert = harmonic(cz[:, :, 1:], cz[:, :, :-1]) * q
    closed = jnp.zeros_like(cz[:, :, :1])
    above = jnp.concatenate([vert, closed], axis=2)
    below = jnp.concatenate([closed, vert], axis=2)
    cst = st_[1:-1]
    cdiag = jnp.maximum(cst + east + west + north + south + above + below, 0.01)
    csrc = source[1:-1]
    u = jnp.broadcast_to(line_mean[:, None, :], source.shape)
    for sweep in range(COARSE_SWEEPS):
        lo = sweep
        centre = u[1:-1]
        sl = slice(lo, width - 2 - lo)
        upper = jnp.concatenate([centre[:, :, 1:], centre[:, :, :1]], axis=2)
        lower = jnp.concatenate([centre[:, :, -1:], centre[:, :, :-1]], axis=2)
        fl = east[sl] * (centre - u[2:]) + west[sl] * (centre - u[:-2])
        fl = fl + north[sl] * (centre - jnp.roll(centre, -1, axis=1))
        fl = fl + south[sl] * (centre - jnp.roll(centre, 1, axis=1))
        fl = fl + above[sl] * (centre - upper) + below[sl] * (centre - lower)
        applied = cst[sl] * centre + fl
        u = centre + jacobi_weight * ((csrc[sl] - applied) / cdiag[sl])
    um = (hm + 1) // 2
    have = reach * nc - COARSE_SWEEPS
    u = u[have - um : u.shape[0] - (have - um)]
    rows = [(k % lines) for k in range(-um, nc + um)]
    runs = []
    for r in rows:
        if runs and runs[-1][1] == r:
            runs[-1][1] = r + 1
        else:
            runs.append([r, r + 1])
    u = jnp.concatenate([u[:, a:b] for a, b in runs], axis=1)
    kept = iy * nc + jnp.arange(-um, nc + um)
    u = jnp.where(((kept >= 0) & (kept < lines))[None, :, None], u, 0.0)
    s1e = win(mext[0], nm, hm, hm) + win(prolong(u), nm, 2 * um, hm)
    b1e = mext[1]
    y1, y1m = chebyshev(b1e, hm, s1e, hm, mid)
    fm = 2 * y1m
    s0 = win(x0, n, x0m, fm) + prolong(y1)
    fs = min(fm, CHEB)
    s0 = win(s0, n, fm, fs)
    out, om = chebyshev(rhs, hf, s0, fs, fine)
    return out


def solution(mesh):
    placed = (P("gx", "gy", None), P("gx", "gy", None), P("gx", "gy", None), P())
    return jax.shard_map(
        local, mesh=mesh, in_specs=placed, out_specs=P("gx", "gy", None), check_vma=False
    )
```

```python
import jax
import jax.numpy as jnp
from jax import lax
from jax.sharding import PartitionSpec as P
from jax.experimental import pallas as pl
from jax.experimental.pallas import tpu as pltpu

CHEB = 3
COARSE_SWEEPS = 8

storage_scale = 0.05
cheb_centre = 1.1
cheb_half = 0.9
cheb_ratio = cheb_centre / cheb_half
jacobi_weight = 0.8

FINE_HALO = 10
MID_HALO = 5
HIGH = lax.Precision.HIGHEST


def shift_from(cells, axis, offset):
    count = lax.axis_size(axis)
    if offset > 0:
        pairs = [(i + offset, i) for i in range(count - offset)]
    else:
        pairs = [(i, i - offset) for i in range(count + offset)]
    if not pairs:
        return jnp.zeros_like(cells)
    return lax.ppermute(cells, axis, pairs)


def halo(cells, sides, width):
    for axis, dim in sides:
        size = cells.shape[dim]
        head = lax.slice_in_dim(cells, 0, width, axis=dim)
        tail = lax.slice_in_dim(cells, size - width, size, axis=dim)
        cells = jnp.concatenate(
            [shift_from(tail, axis, -1), cells, shift_from(head, axis, 1)], axis=dim
        )
    return cells


def harmonic(first, second):
    return first * second / jnp.maximum(0.5 * (first + second), 0.1)


def win(a, n, margin, r, dx=0, dy=0):
    lo = margin - r
    hi = margin + n + r
    return a[..., lo + dx : hi + dx, lo + dy : hi + dy, :]


def pair_matrix(size, dtype=jnp.float32):
    rows = jnp.arange(size)[:, None] // 2
    cols = jnp.arange(size // 2)[None, :]
    return (rows == cols).astype(dtype)


def coarsen(values):
    lead = values.shape[:-3]
    sx, sy, sz = values.shape[-3:]
    v = values.reshape(lead + (sx // 2, 2, sy, sz))
    v = v[..., 0, :, :] + v[..., 1, :, :]
    v = jnp.einsum("...yz,zw->...yw", v, pair_matrix(sz), precision=HIGH)
    rows = v.reshape((-1, sy, sz // 2))
    pick = jnp.broadcast_to(pair_matrix(sy).T, (rows.shape[0], sy // 2, sy))
    rows = lax.dot_general(pick, rows, (((2,), (1,)), ((0,), (0,))), precision=HIGH)
    v = rows.reshape(lead + (sx // 2, sy // 2, sz // 2))
    return v * 0.125


def prolong(values):
    sx, sy, sz = values.shape
    v = jnp.einsum("xyz,wz->xyw", values, pair_matrix(2 * sz), precision=HIGH)
    pick = jnp.broadcast_to(pair_matrix(2 * sy), (sx, 2 * sy, sy))
    v = lax.dot_general(pick, v, (((2,), (1,)), ((0,), (0,))), precision=HIGH)
    v = jnp.broadcast_to(v[:, None], (sx, 2) + v.shape[1:]).reshape((2 * sx,) + v.shape[1:])
    return v


def build_level(coeffs, n, margin, spacing):
    kx, ky, kz, store = coeffs[0], coeffs[1], coeffs[2], coeffs[3]
    fx = harmonic(kx[1:], kx[:-1]) * spacing
    fy = harmonic(ky[:, 1:], ky[:, :-1]) * spacing
    vertical = harmonic(kz[:, :, 1:], kz[:, :, :-1]) * spacing
    closed = jnp.zeros_like(kz[:, :, :1])
    above = jnp.concatenate([vertical, closed], axis=2)
    below = jnp.concatenate([closed, vertical], axis=2)
    level = dict(n=n, m=margin, fx=fx, fy=fy, above=above, below=below, store=store)
    r = margin - 1
    level["diag"] = jnp.maximum(faces_sum(level, r) + win(store, n, margin, r), 0.01)
    level["dm"] = r
    return level


def faces_sum(level, r):
    n, m = level["n"], level["m"]
    east = win(level["fx"], n, m, r)
    west = win(level["fx"], n, m, r, dx=-1)
    north = win(level["fy"], n, m, r)
    south = win(level["fy"], n, m, r, dy=-1)
    above = win(level["above"], n, m, r)
    below = win(level["below"], n, m, r)
    return east + west + north + south + above + below


def operate(values, vm, level):
    n, m = level["n"], level["m"]
    r = vm - 1
    centre = win(values, n, vm, r)
    upper = jnp.concatenate([centre[:, :, 1:], centre[:, :, :1]], axis=2)
    lower = jnp.concatenate([centre[:, :, -1:], centre[:, :, :-1]], axis=2)
    fx, fy = level["fx"], level["fy"]
    fluxes = win(fx, n, m, r) * (centre - win(values, n, vm, r, dx=1))
    fluxes = fluxes + win(fx, n, m, r, dx=-1) * (centre - win(values, n, vm, r, dx=-1))
    fluxes = fluxes + win(fy, n, m, r) * (centre - win(values, n, vm, r, dy=1))
    fluxes = fluxes + win(fy, n, m, r, dy=-1) * (centre - win(values, n, vm, r, dy=-1))
    fluxes = fluxes + win(level["above"], n, m, r) * (centre - upper)
    fluxes = fluxes + win(level["below"], n, m, r) * (centre - lower)
    return win(level["store"], n, m, r) * centre + fluxes


def chebyshev(target, tm, initial, im, level):
    n = level["n"]
    diag, dm = level["diag"], level["dm"]
    if initial is None:
        cur = min(tm, dm)
        misfit = win(target, n, tm, cur)
        update = misfit / win(diag, n, dm, cur) * (1.0 / cheb_centre)
        iterate = update
    else:
        applied = operate(initial, im, level)
        cur = im - 1
        misfit = win(target, n, tm, cur) - applied
        update = misfit / win(diag, n, dm, cur) * (1.0 / cheb_centre)
        iterate = win(initial, n, im, cur) + update
    factor = 1.0 / cheb_ratio
    for repeat in range(CHEB - 1):
        applied = operate(iterate, cur, level)
        nxt = cur - 1
        misfit = win(target, n, tm, nxt) - applied
        factor_new = 1.0 / (2.0 * cheb_ratio - factor)
        update = factor_new * factor * win(update, n, cur, nxt) + 2.0 * factor_new / cheb_half * (
            misfit / win(diag, n, dm, nxt)
        )
        iterate = win(iterate, n, cur, nxt) + update
        cur = nxt
        factor = factor_new
    return iterate, cur


def fields_kernel(bounds_ref, table_ref, conc_ref, idf_ref, out_ref):
    rows = conc_ref.shape[0]
    shape = conc_ref.shape[1:]
    mats = table_ref.shape[1]
    col = lax.broadcasted_iota(jnp.int32, shape, 0)
    col_ok = (col >= bounds_ref[2]) & (col < bounds_ref[3])

    def body(i, carry):
        ids = idf_ref[i]
        conc = conc_ref[i]
        row = jnp.zeros(shape, jnp.int32) + i
        ok = col_ok & (row >= bounds_ref[0]) & (row < bounds_ref[1])
        vals = []
        for record in range(5):
            acc = jnp.zeros(shape, jnp.float32) + table_ref[record, mats - 1]
            for material in range(mats - 2, -1, -1):
                acc = jnp.where(ids == float(material), table_ref[record, material], acc)
            vals.append(acc)
        store = storage_scale * (1.0 + vals[3] * jnp.exp((vals[4] - 1.0) * jnp.log(conc)))
        out_ref[0, i] = jnp.where(ok, vals[0], 0.0)
        out_ref[1, i] = jnp.where(ok, vals[1], 0.0)
        out_ref[2, i] = jnp.where(ok, vals[2], 0.0)
        out_ref[3, i] = jnp.where(ok, store, 0.0)
        return carry

    lax.fori_loop(0, rows, body, 0)


def soil_fields(bounds, soil_table, conc, idf):
    cells = conc.size
    return pl.pallas_call(
        fields_kernel,
        out_shape=jax.ShapeDtypeStruct((4,) + conc.shape, jnp.float32),
        in_specs=[
            pl.BlockSpec(memory_space=pltpu.SMEM),
            pl.BlockSpec(memory_space=pltpu.SMEM),
            pl.BlockSpec(memory_space=pltpu.VMEM),
            pl.BlockSpec(memory_space=pltpu.VMEM),
        ],
        out_specs=pl.BlockSpec(memory_space=pltpu.VMEM),
        cost_estimate=pl.CostEstimate(
            flops=100 * cells, transcendentals=2 * cells, bytes_accessed=24 * cells
        ),
    )(bounds, soil_table, conc, idf)


def local(conc_prev, right_side, soil_id, soil_table):
    n = conc_prev.shape[0]
    ny = conc_prev.shape[1]
    hf = FINE_HALO
    gx_count = lax.axis_size("gx")
    gy_count = lax.axis_size("gy")
    ix = lax.axis_index("gx")
    iy = lax.axis_index("gy")

    stacked = jnp.stack([conc_prev, right_side, soil_id.astype(jnp.float32)])
    ext = halo(stacked, (("gx", 1), ("gy", 2)), hf)
    conc, rhs, idf = ext[0], ext[1], ext[2]
    x_lo = hf - ix * n
    y_lo = hf - iy * ny
    bounds = jnp.stack([x_lo, x_lo + gx_count * n, y_lo, y_lo + gy_count * ny]).astype(jnp.int32)
    fine_c = soil_fields(bounds, soil_table, conc, idf)
    fine = build_level(fine_c, n, hf, 1.0)

    x0, x0m = chebyshev(rhs, hf, None, 0, fine)
    r0 = win(rhs, n, hf, x0m - 1) - operate(x0, x0m, fine)
    r0m = x0m - 1
    nm = n // 2
    mm = hf // 2
    mid_c = coarsen(fine_c)
    mid = build_level(mid_c, nm, mm, 0.25)
    b1 = coarsen(win(r0, n, r0m, 2 * (r0m // 2)))
    b1m = r0m // 2
    x1, x1m = chebyshev(b1, b1m, None, 0, mid)
    r1 = win(b1, nm, b1m, x1m - 1) - operate(x1, x1m, mid)
    r1m = x1m - 1
    b2 = coarsen(win(r1, nm, r1m, 0))
    coarse_own = coarsen(win(mid_c, nm, mm, 0))

    nc = b2.shape[0]
    cpack = jnp.concatenate([b2[None], coarse_own], axis=0)
    mpack = jnp.stack([win(x1, nm, x1m, 0), win(b1, nm, b1m, 0)])
    hm = MID_HALO
    blocks = [cpack]
    for step in range(1, gy_count):
        pairs = [(j, (j - step) % gy_count) for j in range(gy_count)]
        blocks.append(lax.ppermute(cpack, "gy", pairs))
    north = shift_from(mpack[:, :, :hm], "gy", 1)
    south = shift_from(mpack[:, :, nm - hm :], "gy", -1)
    mext = jnp.concatenate([south, mpack, north], axis=2)
    full = jnp.concatenate(blocks, axis=2)
    reach = 3
    every = lax.all_gather(full, "gx", axis=0)
    every = jnp.pad(every, ((reach, reach),) + ((0, 0),) * full.ndim)
    near = lax.dynamic_slice_in_dim(every, ix, 2 * reach + 1, axis=0)
    cpack = jnp.concatenate([near[k] for k in range(2 * reach + 1)], axis=1)
    west_m = shift_from(mext[:, nm - hm :], "gx", -1)
    east_m = shift_from(mext[:, :hm], "gx", 1)
    mext = jnp.concatenate([west_m, mext, east_m], axis=1)
    source = cpack[0]
    cc = cpack[1:]
    line_total = jnp.sum(source, axis=1)
    line_store = jnp.sum(cc[3], axis=1)
    line_mean = jnp.where(line_store > 0, line_total / jnp.where(line_store > 0, line_store, 1.0), 0.0)
    width = source.shape[0]
    lines = source.shape[1]
    gline = (iy * nc + jnp.arange(lines)) % lines
    kx_, ky_, kz_, st_ = cc[0], cc[1], cc[2], cc[3]
    q = 0.0625
    cx = kx_[1:-1]
    cy = ky_[1:-1]
    cz = kz_[1:-1]
    east = harmonic(kx_[2:], cx) * q
    west = harmonic(kx_[:-2], cx) * q
    north = harmonic(jnp.roll(cy, -1, axis=1), cy) * q
    north = jnp.where((gline != lines - 1)[None, :, None], north, 0.0)
    south = jnp.roll(north, 1, axis=1)
    vert = harmonic(cz[:, :, 1:], cz[:, :, :-1]) * q
    closed = jnp.zeros_like(cz[:, :, :1])
    above = jnp.concatenate([vert, closed], axis=2)
    below = jnp.concatenate([closed, vert], axis=2)
    cst = st_[1:-1]
    cdiag = jnp.maximum(cst + east + west + north + south + above + below, 0.01)
    csrc = source[1:-1]
    u = jnp.broadcast_to(line_mean[:, None, :], source.shape)
    for sweep in range(COARSE_SWEEPS):
        lo = sweep
        centre = u[1:-1]
        sl = slice(lo, width - 2 - lo)
        upper = jnp.concatenate([centre[:, :, 1:], centre[:, :, :1]], axis=2)
        lower = jnp.concatenate([centre[:, :, -1:], centre[:, :, :-1]], axis=2)
        fl = east[sl] * (centre - u[2:]) + west[sl] * (centre - u[:-2])
        fl = fl + north[sl] * (centre - jnp.roll(centre, -1, axis=1))
        fl = fl + south[sl] * (centre - jnp.roll(centre, 1, axis=1))
        fl = fl + above[sl] * (centre - upper) + below[sl] * (centre - lower)
        applied = cst[sl] * centre + fl
        u = centre + jacobi_weight * ((csrc[sl] - applied) / cdiag[sl])
    um = (hm + 1) // 2
    have = reach * nc - COARSE_SWEEPS
    u = u[have - um : u.shape[0] - (have - um)]
    rows = [(k % lines) for k in range(-um, nc + um)]
    runs = []
    for r in rows:
        if runs and runs[-1][1] == r:
            runs[-1][1] = r + 1
        else:
            runs.append([r, r + 1])
    u = jnp.concatenate([u[:, a:b] for a, b in runs], axis=1)
    kept = iy * nc + jnp.arange(-um, nc + um)
    u = jnp.where(((kept >= 0) & (kept < lines))[None, :, None], u, 0.0)
    s1e = win(mext[0], nm, hm, hm) + win(prolong(u), nm, 2 * um, hm)
    b1e = mext[1]
    y1, y1m = chebyshev(b1e, hm, s1e, hm, mid)
    fm = 2 * y1m
    s0 = win(x0, n, x0m, fm) + prolong(y1)
    fs = min(fm, CHEB)
    s0 = win(s0, n, fm, fs)
    out, om = chebyshev(rhs, hf, s0, fs, fine)
    return out


def solution(mesh):
    placed = (P("gx", "gy", None), P("gx", "gy", None), P("gx", "gy", None), P())
    return jax.shard_map(
        local, mesh=mesh, in_specs=placed, out_specs=P("gx", "gy", None), check_vma=False
    )
```

```python
import jax
import jax.numpy as jnp
from jax import lax
from jax.sharding import PartitionSpec as P
from jax.experimental import pallas as pl
from jax.experimental.pallas import tpu as pltpu

CHEB = 3
COARSE_SWEEPS = 8

storage_scale = 0.05
cheb_centre = 1.1
cheb_half = 0.9
cheb_ratio = cheb_centre / cheb_half
jacobi_weight = 0.8

FINE_HALO = 10
MID_HALO = 5
HIGH = lax.Precision.HIGHEST


def shift_from(cells, axis, offset):
    count = lax.axis_size(axis)
    if offset > 0:
        pairs = [(i + offset, i) for i in range(count - offset)]
    else:
        pairs = [(i, i - offset) for i in range(count + offset)]
    if not pairs:
        return jnp.zeros_like(cells)
    return lax.ppermute(cells, axis, pairs)


def halo(cells, sides, width):
    for axis, dim in sides:
        size = cells.shape[dim]
        head = lax.slice_in_dim(cells, 0, width, axis=dim)
        tail = lax.slice_in_dim(cells, size - width, size, axis=dim)
        cells = jnp.concatenate(
            [shift_from(tail, axis, -1), cells, shift_from(head, axis, 1)], axis=dim
        )
    return cells


def corner_from(cells, dx, dy):
    cx, cy = lax.axis_size("gx"), lax.axis_size("gy")
    pairs = []
    for i in range(cx):
        for j in range(cy):
            si, sj = i + dx, j + dy
            if 0 <= si < cx and 0 <= sj < cy:
                pairs.append((si * cy + sj, i * cy + j))
    if not pairs:
        return jnp.zeros_like(cells)
    return lax.ppermute(cells, ("gx", "gy"), pairs)


def halo_once(cells, width):
    sx, sy = cells.shape[1], cells.shape[2]
    lo_x, hi_x = cells[:, sx - width :], cells[:, :width]
    lo_y, hi_y = cells[:, :, sy - width :], cells[:, :, :width]
    west = shift_from(lo_x, "gx", -1)
    east = shift_from(hi_x, "gx", 1)
    south = shift_from(lo_y, "gy", -1)
    north = shift_from(hi_y, "gy", 1)
    sw = corner_from(cells[:, sx - width :, sy - width :], -1, -1)
    se = corner_from(cells[:, sx - width :, :width], -1, 1)
    nw = corner_from(cells[:, :width, sy - width :], 1, -1)
    ne = corner_from(cells[:, :width, :width], 1, 1)
    top = jnp.concatenate([sw, west, se], axis=2)
    mid = jnp.concatenate([south, cells, north], axis=2)
    bottom = jnp.concatenate([nw, east, ne], axis=2)
    return jnp.concatenate([top, mid, bottom], axis=1)


def harmonic(first, second):
    return first * second / jnp.maximum(0.5 * (first + second), 0.1)


def win(a, n, margin, r, dx=0, dy=0):
    lo = margin - r
    hi = margin + n + r
    return a[..., lo + dx : hi + dx, lo + dy : hi + dy, :]


def pair_matrix(size, dtype=jnp.float32):
    rows = jnp.arange(size)[:, None] // 2
    cols = jnp.arange(size // 2)[None, :]
    return (rows == cols).astype(dtype)


def coarsen(values):
    lead = values.shape[:-3]
    sx, sy, sz = values.shape[-3:]
    v = values.reshape(lead + (sx // 2, 2, sy, sz))
    v = v[..., 0, :, :] + v[..., 1, :, :]
    v = jnp.einsum("...yz,zw->...yw", v, pair_matrix(sz), precision=HIGH)
    rows = v.reshape((-1, sy, sz // 2))
    pick = jnp.broadcast_to(pair_matrix(sy).T, (rows.shape[0], sy // 2, sy))
    rows = lax.dot_general(pick, rows, (((2,), (1,)), ((0,), (0,))), precision=HIGH)
    v = rows.reshape(lead + (sx // 2, sy // 2, sz // 2))
    return v * 0.125


def prolong(values):
    sx, sy, sz = values.shape
    v = jnp.einsum("xyz,wz->xyw", values, pair_matrix(2 * sz), precision=HIGH)
    pick = jnp.broadcast_to(pair_matrix(2 * sy), (sx, 2 * sy, sy))
    v = lax.dot_general(pick, v, (((2,), (1,)), ((0,), (0,))), precision=HIGH)
    v = jnp.broadcast_to(v[:, None], (sx, 2) + v.shape[1:]).reshape((2 * sx,) + v.shape[1:])
    return v


def build_level(coeffs, n, margin, spacing):
    kx, ky, kz, store = coeffs[0], coeffs[1], coeffs[2], coeffs[3]
    fx = harmonic(kx[1:], kx[:-1]) * spacing
    fy = harmonic(ky[:, 1:], ky[:, :-1]) * spacing
    vertical = harmonic(kz[:, :, 1:], kz[:, :, :-1]) * spacing
    closed = jnp.zeros_like(kz[:, :, :1])
    above = jnp.concatenate([vertical, closed], axis=2)
    below = jnp.concatenate([closed, vertical], axis=2)
    level = dict(n=n, m=margin, fx=fx, fy=fy, above=above, below=below, store=store)
    r = margin - 1
    level["diag"] = jnp.maximum(faces_sum(level, r) + win(store, n, margin, r), 0.01)
    level["dm"] = r
    return level


def faces_sum(level, r):
    n, m = level["n"], level["m"]
    east = win(level["fx"], n, m, r)
    west = win(level["fx"], n, m, r, dx=-1)
    north = win(level["fy"], n, m, r)
    south = win(level["fy"], n, m, r, dy=-1)
    above = win(level["above"], n, m, r)
    below = win(level["below"], n, m, r)
    return east + west + north + south + above + below


def operate(values, vm, level):
    n, m = level["n"], level["m"]
    r = vm - 1
    centre = win(values, n, vm, r)
    upper = jnp.concatenate([centre[:, :, 1:], centre[:, :, :1]], axis=2)
    lower = jnp.concatenate([centre[:, :, -1:], centre[:, :, :-1]], axis=2)
    fx, fy = level["fx"], level["fy"]
    fluxes = win(fx, n, m, r) * (centre - win(values, n, vm, r, dx=1))
    fluxes = fluxes + win(fx, n, m, r, dx=-1) * (centre - win(values, n, vm, r, dx=-1))
    fluxes = fluxes + win(fy, n, m, r) * (centre - win(values, n, vm, r, dy=1))
    fluxes = fluxes + win(fy, n, m, r, dy=-1) * (centre - win(values, n, vm, r, dy=-1))
    fluxes = fluxes + win(level["above"], n, m, r) * (centre - upper)
    fluxes = fluxes + win(level["below"], n, m, r) * (centre - lower)
    return win(level["store"], n, m, r) * centre + fluxes


def chebyshev(target, tm, initial, im, level):
    n = level["n"]
    diag, dm = level["diag"], level["dm"]
    if initial is None:
        cur = min(tm, dm)
        misfit = win(target, n, tm, cur)
        update = misfit / win(diag, n, dm, cur) * (1.0 / cheb_centre)
        iterate = update
    else:
        applied = operate(initial, im, level)
        cur = im - 1
        misfit = win(target, n, tm, cur) - applied
        update = misfit / win(diag, n, dm, cur) * (1.0 / cheb_centre)
        iterate = win(initial, n, im, cur) + update
    factor = 1.0 / cheb_ratio
    for repeat in range(CHEB - 1):
        applied = operate(iterate, cur, level)
        nxt = cur - 1
        misfit = win(target, n, tm, nxt) - applied
        factor_new = 1.0 / (2.0 * cheb_ratio - factor)
        update = factor_new * factor * win(update, n, cur, nxt) + 2.0 * factor_new / cheb_half * (
            misfit / win(diag, n, dm, nxt)
        )
        iterate = win(iterate, n, cur, nxt) + update
        cur = nxt
        factor = factor_new
    return iterate, cur


def fields_kernel(bounds_ref, table_ref, conc_ref, idf_ref, out_ref):
    rows = conc_ref.shape[0]
    shape = conc_ref.shape[1:]
    mats = table_ref.shape[1]
    col = lax.broadcasted_iota(jnp.int32, shape, 0)
    col_ok = (col >= bounds_ref[2]) & (col < bounds_ref[3])

    def body(i, carry):
        ids = idf_ref[i]
        conc = conc_ref[i]
        row = jnp.zeros(shape, jnp.int32) + i
        ok = col_ok & (row >= bounds_ref[0]) & (row < bounds_ref[1])
        vals = []
        for record in range(5):
            acc = jnp.zeros(shape, jnp.float32) + table_ref[record, mats - 1]
            for material in range(mats - 2, -1, -1):
                acc = jnp.where(ids == float(material), table_ref[record, material], acc)
            vals.append(acc)
        store = storage_scale * (1.0 + vals[3] * jnp.exp((vals[4] - 1.0) * jnp.log(conc)))
        out_ref[0, i] = jnp.where(ok, vals[0], 0.0)
        out_ref[1, i] = jnp.where(ok, vals[1], 0.0)
        out_ref[2, i] = jnp.where(ok, vals[2], 0.0)
        out_ref[3, i] = jnp.where(ok, store, 0.0)
        return carry

    lax.fori_loop(0, rows, body, 0)


def soil_fields(bounds, soil_table, conc, idf):
    cells = conc.size
    return pl.pallas_call(
        fields_kernel,
        out_shape=jax.ShapeDtypeStruct((4,) + conc.shape, jnp.float32),
        in_specs=[
            pl.BlockSpec(memory_space=pltpu.SMEM),
            pl.BlockSpec(memory_space=pltpu.SMEM),
            pl.BlockSpec(memory_space=pltpu.VMEM),
            pl.BlockSpec(memory_space=pltpu.VMEM),
        ],
        out_specs=pl.BlockSpec(memory_space=pltpu.VMEM),
        cost_estimate=pl.CostEstimate(
            flops=100 * cells, transcendentals=2 * cells, bytes_accessed=24 * cells
        ),
    )(bounds, soil_table, conc, idf)


def local(conc_prev, right_side, soil_id, soil_table):
    n = conc_prev.shape[0]
    ny = conc_prev.shape[1]
    hf = FINE_HALO
    gx_count = lax.axis_size("gx")
    gy_count = lax.axis_size("gy")
    ix = lax.axis_index("gx")
    iy = lax.axis_index("gy")

    stacked = jnp.stack([conc_prev, right_side, soil_id.astype(jnp.float32)])
    ext = halo_once(stacked, hf)
    conc, rhs, idf = ext[0], ext[1], ext[2]
    x_lo = hf - ix * n
    y_lo = hf - iy * ny
    bounds = jnp.stack([x_lo, x_lo + gx_count * n, y_lo, y_lo + gy_count * ny]).astype(jnp.int32)
    fine_c = soil_fields(bounds, soil_table, conc, idf)
    fine = build_level(fine_c, n, hf, 1.0)

    x0, x0m = chebyshev(rhs, hf, None, 0, fine)
    r0 = win(rhs, n, hf, x0m - 1) - operate(x0, x0m, fine)
    r0m = x0m - 1
    nm = n // 2
    mm = hf // 2
    mid_c = coarsen(fine_c)
    mid = build_level(mid_c, nm, mm, 0.25)
    b1 = coarsen(win(r0, n, r0m, 2 * (r0m // 2)))
    b1m = r0m // 2
    x1, x1m = chebyshev(b1, b1m, None, 0, mid)
    r1 = win(b1, nm, b1m, x1m - 1) - operate(x1, x1m, mid)
    r1m = x1m - 1
    b2 = coarsen(win(r1, nm, r1m, 0))
    coarse_own = coarsen(win(mid_c, nm, mm, 0))

    nc = b2.shape[0]
    cpack = jnp.concatenate([b2[None], coarse_own], axis=0)
    mpack = jnp.stack([win(x1, nm, x1m, 0), win(b1, nm, b1m, 0)])
    hm = MID_HALO
    blocks = [cpack]
    for step in range(1, gy_count):
        pairs = [(j, (j - step) % gy_count) for j in range(gy_count)]
        blocks.append(lax.ppermute(cpack, "gy", pairs))
    north = shift_from(mpack[:, :, :hm], "gy", 1)
    south = shift_from(mpack[:, :, nm - hm :], "gy", -1)
    mext = jnp.concatenate([south, mpack, north], axis=2)
    full = jnp.concatenate(blocks, axis=2)
    reach = 3
    parts = [shift_from(full, "gx", -d) for d in range(reach, 0, -1)]
    parts += [full]
    parts += [shift_from(full, "gx", d) for d in range(1, reach + 1)]
    cpack = jnp.concatenate(parts, axis=1)
    west_m = shift_from(mext[:, nm - hm :], "gx", -1)
    east_m = shift_from(mext[:, :hm], "gx", 1)
    mext = jnp.concatenate([west_m, mext, east_m], axis=1)
    source = cpack[0]
    cc = cpack[1:]
    line_total = jnp.sum(source, axis=1)
    line_store = jnp.sum(cc[3], axis=1)
    line_mean = jnp.where(line_store > 0, line_total / jnp.where(line_store > 0, line_store, 1.0), 0.0)
    width = source.shape[0]
    lines = source.shape[1]
    gline = (iy * nc + jnp.arange(lines)) % lines
    kx_, ky_, kz_, st_ = cc[0], cc[1], cc[2], cc[3]
    q = 0.0625
    cx = kx_[1:-1]
    cy = ky_[1:-1]
    cz = kz_[1:-1]
    east = harmonic(kx_[2:], cx) * q
    west = harmonic(kx_[:-2], cx) * q
    north = harmonic(jnp.roll(cy, -1, axis=1), cy) * q
    north = jnp.where((gline != lines - 1)[None, :, None], north, 0.0)
    south = jnp.roll(north, 1, axis=1)
    vert = harmonic(cz[:, :, 1:], cz[:, :, :-1]) * q
    closed = jnp.zeros_like(cz[:, :, :1])
    above = jnp.concatenate([vert, closed], axis=2)
    below = jnp.concatenate([closed, vert], axis=2)
    cst = st_[1:-1]
    cdiag = jnp.maximum(cst + east + west + north + south + above + below, 0.01)
    csrc = source[1:-1]
    u = jnp.broadcast_to(line_mean[:, None, :], source.shape)
    for sweep in range(COARSE_SWEEPS):
        lo = sweep
        centre = u[1:-1]
        sl = slice(lo, width - 2 - lo)
        upper = jnp.concatenate([centre[:, :, 1:], centre[:, :, :1]], axis=2)
        lower = jnp.concatenate([centre[:, :, -1:], centre[:, :, :-1]], axis=2)
        fl = east[sl] * (centre - u[2:]) + west[sl] * (centre - u[:-2])
        fl = fl + north[sl] * (centre - jnp.roll(centre, -1, axis=1))
        fl = fl + south[sl] * (centre - jnp.roll(centre, 1, axis=1))
        fl = fl + above[sl] * (centre - upper) + below[sl] * (centre - lower)
        applied = cst[sl] * centre + fl
        u = centre + jacobi_weight * ((csrc[sl] - applied) / cdiag[sl])
    um = (hm + 1) // 2
    have = reach * nc - COARSE_SWEEPS
    u = u[have - um : u.shape[0] - (have - um)]
    rows = [(k % lines) for k in range(-um, nc + um)]
    runs = []
    for r in rows:
        if runs and runs[-1][1] == r:
            runs[-1][1] = r + 1
        else:
            runs.append([r, r + 1])
    u = jnp.concatenate([u[:, a:b] for a, b in runs], axis=1)
    kept = iy * nc + jnp.arange(-um, nc + um)
    u = jnp.where(((kept >= 0) & (kept < lines))[None, :, None], u, 0.0)
    s1e = win(mext[0], nm, hm, hm) + win(prolong(u), nm, 2 * um, hm)
    b1e = mext[1]
    y1, y1m = chebyshev(b1e, hm, s1e, hm, mid)
    fm = 2 * y1m
    s0 = win(x0, n, x0m, fm) + prolong(y1)
    fs = min(fm, CHEB)
    s0 = win(s0, n, fm, fs)
    out, om = chebyshev(rhs, hf, s0, fs, fine)
    return out


def solution(mesh):
    placed = (P("gx", "gy", None), P("gx", "gy", None), P("gx", "gy", None), P())
    return jax.shard_map(
        local, mesh=mesh, in_specs=placed, out_specs=P("gx", "gy", None), check_vma=False
    )
```

```python
import jax
import jax.numpy as jnp
from jax import lax
from jax.sharding import PartitionSpec as P
from jax.experimental import pallas as pl
from jax.experimental.pallas import tpu as pltpu

CHEB = 3
COARSE_SWEEPS = 8

storage_scale = 0.05
cheb_centre = 1.1
cheb_half = 0.9
cheb_ratio = cheb_centre / cheb_half
jacobi_weight = 0.8

FINE_HALO = 10
MID_HALO = 5
HIGH = lax.Precision.HIGHEST


def shift_from(cells, axis, offset):
    count = lax.axis_size(axis)
    if offset > 0:
        pairs = [(i + offset, i) for i in range(count - offset)]
    else:
        pairs = [(i, i - offset) for i in range(count + offset)]
    if not pairs:
        return jnp.zeros_like(cells)
    return lax.ppermute(cells, axis, pairs)


def halo(cells, sides, width):
    for axis, dim in sides:
        size = cells.shape[dim]
        head = lax.slice_in_dim(cells, 0, width, axis=dim)
        tail = lax.slice_in_dim(cells, size - width, size, axis=dim)
        cells = jnp.concatenate(
            [shift_from(tail, axis, -1), cells, shift_from(head, axis, 1)], axis=dim
        )
    return cells


def joined(first, second):
    tail = tuple(max(a, b) for a, b in zip(first.shape[-2:], second.shape[-2:]))

    def fit(a):
        pad = [(0, 0)] * (a.ndim - 2) + [(0, t - d) for t, d in zip(tail, a.shape[-2:])]
        return jnp.pad(a, pad).reshape((-1,) + tail)

    return jnp.concatenate([fit(first), fit(second)], axis=0)


def split(both, first, second):
    lead = first.size // (first.shape[-2] * first.shape[-1])
    a = both[:lead].reshape(first.shape[:-2] + both.shape[-2:])
    b = both[lead:].reshape(second.shape[:-2] + both.shape[-2:])
    a = a[..., : first.shape[-2], : first.shape[-1]]
    b = b[..., : second.shape[-2], : second.shape[-1]]
    return a, b


def harmonic(first, second):
    return first * second / jnp.maximum(0.5 * (first + second), 0.1)


def win(a, n, margin, r, dx=0, dy=0):
    lo = margin - r
    hi = margin + n + r
    return a[..., lo + dx : hi + dx, lo + dy : hi + dy, :]


def pair_matrix(size, dtype=jnp.float32):
    rows = jnp.arange(size)[:, None] // 2
    cols = jnp.arange(size // 2)[None, :]
    return (rows == cols).astype(dtype)


def coarsen(values):
    lead = values.shape[:-3]
    sx, sy, sz = values.shape[-3:]
    v = values.reshape(lead + (sx // 2, 2, sy, sz))
    v = v[..., 0, :, :] + v[..., 1, :, :]
    v = jnp.einsum("...yz,zw->...yw", v, pair_matrix(sz), precision=HIGH)
    rows = v.reshape((-1, sy, sz // 2))
    pick = jnp.broadcast_to(pair_matrix(sy).T, (rows.shape[0], sy // 2, sy))
    rows = lax.dot_general(pick, rows, (((2,), (1,)), ((0,), (0,))), precision=HIGH)
    v = rows.reshape(lead + (sx // 2, sy // 2, sz // 2))
    return v * 0.125


def prolong(values):
    sx, sy, sz = values.shape
    v = jnp.einsum("xyz,wz->xyw", values, pair_matrix(2 * sz), precision=HIGH)
    pick = jnp.broadcast_to(pair_matrix(2 * sy), (sx, 2 * sy, sy))
    v = lax.dot_general(pick, v, (((2,), (1,)), ((0,), (0,))), precision=HIGH)
    v = jnp.broadcast_to(v[:, None], (sx, 2) + v.shape[1:]).reshape((2 * sx,) + v.shape[1:])
    return v


def build_level(coeffs, n, margin, spacing):
    kx, ky, kz, store = coeffs[0], coeffs[1], coeffs[2], coeffs[3]
    fx = harmonic(kx[1:], kx[:-1]) * spacing
    fy = harmonic(ky[:, 1:], ky[:, :-1]) * spacing
    vertical = harmonic(kz[:, :, 1:], kz[:, :, :-1]) * spacing
    closed = jnp.zeros_like(kz[:, :, :1])
    above = jnp.concatenate([vertical, closed], axis=2)
    below = jnp.concatenate([closed, vertical], axis=2)
    level = dict(n=n, m=margin, fx=fx, fy=fy, above=above, below=below, store=store)
    r = margin - 1
    level["diag"] = jnp.maximum(faces_sum(level, r) + win(store, n, margin, r), 0.01)
    level["dm"] = r
    return level


def faces_sum(level, r):
    n, m = level["n"], level["m"]
    east = win(level["fx"], n, m, r)
    west = win(level["fx"], n, m, r, dx=-1)
    north = win(level["fy"], n, m, r)
    south = win(level["fy"], n, m, r, dy=-1)
    above = win(level["above"], n, m, r)
    below = win(level["below"], n, m, r)
    return east + west + north + south + above + below


def operate(values, vm, level):
    n, m = level["n"], level["m"]
    r = vm - 1
    centre = win(values, n, vm, r)
    upper = jnp.concatenate([centre[:, :, 1:], centre[:, :, :1]], axis=2)
    lower = jnp.concatenate([centre[:, :, -1:], centre[:, :, :-1]], axis=2)
    fx, fy = level["fx"], level["fy"]
    fluxes = win(fx, n, m, r) * (centre - win(values, n, vm, r, dx=1))
    fluxes = fluxes + win(fx, n, m, r, dx=-1) * (centre - win(values, n, vm, r, dx=-1))
    fluxes = fluxes + win(fy, n, m, r) * (centre - win(values, n, vm, r, dy=1))
    fluxes = fluxes + win(fy, n, m, r, dy=-1) * (centre - win(values, n, vm, r, dy=-1))
    fluxes = fluxes + win(level["above"], n, m, r) * (centre - upper)
    fluxes = fluxes + win(level["below"], n, m, r) * (centre - lower)
    return win(level["store"], n, m, r) * centre + fluxes


def chebyshev(target, tm, initial, im, level):
    n = level["n"]
    diag, dm = level["diag"], level["dm"]
    if initial is None:
        cur = min(tm, dm)
        misfit = win(target, n, tm, cur)
        update = misfit / win(diag, n, dm, cur) * (1.0 / cheb_centre)
        iterate = update
    else:
        applied = operate(initial, im, level)
        cur = im - 1
        misfit = win(target, n, tm, cur) - applied
        update = misfit / win(diag, n, dm, cur) * (1.0 / cheb_centre)
        iterate = win(initial, n, im, cur) + update
    factor = 1.0 / cheb_ratio
    for repeat in range(CHEB - 1):
        applied = operate(iterate, cur, level)
        nxt = cur - 1
        misfit = win(target, n, tm, nxt) - applied
        factor_new = 1.0 / (2.0 * cheb_ratio - factor)
        update = factor_new * factor * win(update, n, cur, nxt) + 2.0 * factor_new / cheb_half * (
            misfit / win(diag, n, dm, nxt)
        )
        iterate = win(iterate, n, cur, nxt) + update
        cur = nxt
        factor = factor_new
    return iterate, cur


def fields_kernel(bounds_ref, table_ref, conc_ref, idf_ref, out_ref):
    rows = conc_ref.shape[0]
    shape = conc_ref.shape[1:]
    mats = table_ref.shape[1]
    col = lax.broadcasted_iota(jnp.int32, shape, 0)
    col_ok = (col >= bounds_ref[2]) & (col < bounds_ref[3])

    def body(i, carry):
        ids = idf_ref[i]
        conc = conc_ref[i]
        row = jnp.zeros(shape, jnp.int32) + i
        ok = col_ok & (row >= bounds_ref[0]) & (row < bounds_ref[1])
        vals = []
        for record in range(5):
            acc = jnp.zeros(shape, jnp.float32) + table_ref[record, mats - 1]
            for material in range(mats - 2, -1, -1):
                acc = jnp.where(ids == float(material), table_ref[record, material], acc)
            vals.append(acc)
        store = storage_scale * (1.0 + vals[3] * jnp.exp((vals[4] - 1.0) * jnp.log(conc)))
        out_ref[0, i] = jnp.where(ok, vals[0], 0.0)
        out_ref[1, i] = jnp.where(ok, vals[1], 0.0)
        out_ref[2, i] = jnp.where(ok, vals[2], 0.0)
        out_ref[3, i] = jnp.where(ok, store, 0.0)
        return carry

    lax.fori_loop(0, rows, body, 0)


def soil_fields(bounds, soil_table, conc, idf):
    cells = conc.size
    return pl.pallas_call(
        fields_kernel,
        out_shape=jax.ShapeDtypeStruct((4,) + conc.shape, jnp.float32),
        in_specs=[
            pl.BlockSpec(memory_space=pltpu.SMEM),
            pl.BlockSpec(memory_space=pltpu.SMEM),
            pl.BlockSpec(memory_space=pltpu.VMEM),
            pl.BlockSpec(memory_space=pltpu.VMEM),
        ],
        out_specs=pl.BlockSpec(memory_space=pltpu.VMEM),
        cost_estimate=pl.CostEstimate(
            flops=100 * cells, transcendentals=2 * cells, bytes_accessed=24 * cells
        ),
    )(bounds, soil_table, conc, idf)


def local(conc_prev, right_side, soil_id, soil_table):
    n = conc_prev.shape[0]
    ny = conc_prev.shape[1]
    hf = FINE_HALO
    gx_count = lax.axis_size("gx")
    gy_count = lax.axis_size("gy")
    ix = lax.axis_index("gx")
    iy = lax.axis_index("gy")

    stacked = jnp.stack([conc_prev, right_side, soil_id.astype(jnp.float32)])
    ext = halo(stacked, (("gx", 1), ("gy", 2)), hf)
    conc, rhs, idf = ext[0], ext[1], ext[2]
    x_lo = hf - ix * n
    y_lo = hf - iy * ny
    bounds = jnp.stack([x_lo, x_lo + gx_count * n, y_lo, y_lo + gy_count * ny]).astype(jnp.int32)
    fine_c = soil_fields(bounds, soil_table, conc, idf)
    fine = build_level(fine_c, n, hf, 1.0)

    x0, x0m = chebyshev(rhs, hf, None, 0, fine)
    r0 = win(rhs, n, hf, x0m - 1) - operate(x0, x0m, fine)
    r0m = x0m - 1
    nm = n // 2
    mm = hf // 2
    mid_c = coarsen(fine_c)
    mid = build_level(mid_c, nm, mm, 0.25)
    b1 = coarsen(win(r0, n, r0m, 2 * (r0m // 2)))
    b1m = r0m // 2
    x1, x1m = chebyshev(b1, b1m, None, 0, mid)
    r1 = win(b1, nm, b1m, x1m - 1) - operate(x1, x1m, mid)
    r1m = x1m - 1
    b2 = coarsen(win(r1, nm, r1m, 0))
    coarse_own = coarsen(win(mid_c, nm, mm, 0))

    nc = b2.shape[0]
    cpack = jnp.concatenate([b2[None], coarse_own], axis=0)
    mpack = jnp.stack([win(x1, nm, x1m, 0), win(b1, nm, b1m, 0)])
    hm = MID_HALO
    north_slab = mpack[:, :, :hm]
    south_slab = mpack[:, :, nm - hm :]
    blocks = [cpack]
    north = south = None
    for step in range(1, gy_count):
        pairs = [(j, (j - step) % gy_count) for j in range(gy_count)]
        if step == 1 and gy_count > 2:
            got, north = split(lax.ppermute(joined(cpack, north_slab), "gy", pairs), cpack, north_slab)
        elif step == gy_count - 1 and gy_count > 2:
            got, south = split(lax.ppermute(joined(cpack, south_slab), "gy", pairs), cpack, south_slab)
        else:
            got = lax.ppermute(cpack, "gy", pairs)
        blocks.append(got)
    if north is None:
        north = shift_from(north_slab, "gy", 1)
        south = shift_from(south_slab, "gy", -1)
    north = jnp.where(iy < gy_count - 1, north, 0.0)
    south = jnp.where(iy > 0, south, 0.0)
    mext = jnp.concatenate([south, mpack, north], axis=2)
    full = jnp.concatenate(blocks, axis=2)
    reach = 3
    west_slab = mext[:, nm - hm :]
    east_slab = mext[:, :hm]
    low, west_m = split(shift_from(joined(full, west_slab), "gx", -1), full, west_slab)
    high, east_m = split(shift_from(joined(full, east_slab), "gx", 1), full, east_slab)
    parts = [shift_from(full, "gx", -d) for d in range(reach, 1, -1)]
    parts += [low, full, high]
    parts += [shift_from(full, "gx", d) for d in range(2, reach + 1)]
    cpack = jnp.concatenate(parts, axis=1)
    mext = jnp.concatenate([west_m, mext, east_m], axis=1)
    source = cpack[0]
    cc = cpack[1:]
    line_total = jnp.sum(source, axis=1)
    line_store = jnp.sum(cc[3], axis=1)
    line_mean = jnp.where(line_store > 0, line_total / jnp.where(line_store > 0, line_store, 1.0), 0.0)
    width = source.shape[0]
    lines = source.shape[1]
    gline = (iy * nc + jnp.arange(lines)) % lines
    kx_, ky_, kz_, st_ = cc[0], cc[1], cc[2], cc[3]
    q = 0.0625
    cx = kx_[1:-1]
    cy = ky_[1:-1]
    cz = kz_[1:-1]
    east = harmonic(kx_[2:], cx) * q
    west = harmonic(kx_[:-2], cx) * q
    north = harmonic(jnp.roll(cy, -1, axis=1), cy) * q
    north = jnp.where((gline != lines - 1)[None, :, None], north, 0.0)
    south = jnp.roll(north, 1, axis=1)
    vert = harmonic(cz[:, :, 1:], cz[:, :, :-1]) * q
    closed = jnp.zeros_like(cz[:, :, :1])
    above = jnp.concatenate([vert, closed], axis=2)
    below = jnp.concatenate([closed, vert], axis=2)
    cst = st_[1:-1]
    cdiag = jnp.maximum(cst + east + west + north + south + above + below, 0.01)
    csrc = source[1:-1]
    u = jnp.broadcast_to(line_mean[:, None, :], source.shape)
    for sweep in range(COARSE_SWEEPS):
        lo = sweep
        centre = u[1:-1]
        sl = slice(lo, width - 2 - lo)
        upper = jnp.concatenate([centre[:, :, 1:], centre[:, :, :1]], axis=2)
        lower = jnp.concatenate([centre[:, :, -1:], centre[:, :, :-1]], axis=2)
        fl = east[sl] * (centre - u[2:]) + west[sl] * (centre - u[:-2])
        fl = fl + north[sl] * (centre - jnp.roll(centre, -1, axis=1))
        fl = fl + south[sl] * (centre - jnp.roll(centre, 1, axis=1))
        fl = fl + above[sl] * (centre - upper) + below[sl] * (centre - lower)
        applied = cst[sl] * centre + fl
        u = centre + jacobi_weight * ((csrc[sl] - applied) / cdiag[sl])
    um = (hm + 1) // 2
    have = reach * nc - COARSE_SWEEPS
    u = u[have - um : u.shape[0] - (have - um)]
    rows = [(k % lines) for k in range(-um, nc + um)]
    runs = []
    for r in rows:
        if runs and runs[-1][1] == r:
            runs[-1][1] = r + 1
        else:
            runs.append([r, r + 1])
    u = jnp.concatenate([u[:, a:b] for a, b in runs], axis=1)
    kept = iy * nc + jnp.arange(-um, nc + um)
    u = jnp.where(((kept >= 0) & (kept < lines))[None, :, None], u, 0.0)
    s1e = win(mext[0], nm, hm, hm) + win(prolong(u), nm, 2 * um, hm)
    b1e = mext[1]
    y1, y1m = chebyshev(b1e, hm, s1e, hm, mid)
    fm = 2 * y1m
    s0 = win(x0, n, x0m, fm) + prolong(y1)
    fs = min(fm, CHEB)
    s0 = win(s0, n, fm, fs)
    out, om = chebyshev(rhs, hf, s0, fs, fine)
    return out


def solution(mesh):
    placed = (P("gx", "gy", None), P("gx", "gy", None), P("gx", "gy", None), P())
    return jax.shard_map(
        local, mesh=mesh, in_specs=placed, out_specs=P("gx", "gy", None), check_vma=False
    )
```

```python
import functools

import jax
import jax.numpy as jnp
from jax import lax
from jax.sharding import PartitionSpec as P
from jax.experimental import pallas as pl
from jax.experimental.pallas import tpu as pltpu

CHEB = 3
COARSE_SWEEPS = 8

storage_scale = 0.05
cheb_centre = 1.1
cheb_half = 0.9
cheb_ratio = cheb_centre / cheb_half
jacobi_weight = 0.8

FINE_HALO = 10
MID_HALO = 5
HIGH = lax.Precision.HIGHEST


def shift_from(cells, axis, offset):
    count = lax.axis_size(axis)
    if offset > 0:
        pairs = [(i + offset, i) for i in range(count - offset)]
    else:
        pairs = [(i, i - offset) for i in range(count + offset)]
    if not pairs:
        return jnp.zeros_like(cells)
    return lax.ppermute(cells, axis, pairs)


def halo(cells, sides, width):
    for axis, dim in sides:
        size = cells.shape[dim]
        head = lax.slice_in_dim(cells, 0, width, axis=dim)
        tail = lax.slice_in_dim(cells, size - width, size, axis=dim)
        cells = jnp.concatenate(
            [shift_from(tail, axis, -1), cells, shift_from(head, axis, 1)], axis=dim
        )
    return cells


def harmonic(first, second):
    return first * second / jnp.maximum(0.5 * (first + second), 0.1)


def win(a, n, margin, r, dx=0, dy=0):
    lo = margin - r
    hi = margin + n + r
    return a[..., lo + dx : hi + dx, lo + dy : hi + dy, :]


def pair_matrix(size, dtype=jnp.float32):
    rows = jnp.arange(size)[:, None] // 2
    cols = jnp.arange(size // 2)[None, :]
    return (rows == cols).astype(dtype)


def coarsen(values):
    lead = values.shape[:-3]
    sx, sy, sz = values.shape[-3:]
    v = values.reshape(lead + (sx // 2, 2, sy, sz))
    v = v[..., 0, :, :] + v[..., 1, :, :]
    v = jnp.einsum("...yz,zw->...yw", v, pair_matrix(sz), precision=HIGH)
    rows = v.reshape((-1, sy, sz // 2))
    pick = jnp.broadcast_to(pair_matrix(sy).T, (rows.shape[0], sy // 2, sy))
    rows = lax.dot_general(pick, rows, (((2,), (1,)), ((0,), (0,))), precision=HIGH)
    v = rows.reshape(lead + (sx // 2, sy // 2, sz // 2))
    return v * 0.125


def prolong(values):
    sx, sy, sz = values.shape
    v = jnp.einsum("xyz,wz->xyw", values, pair_matrix(2 * sz), precision=HIGH)
    pick = jnp.broadcast_to(pair_matrix(2 * sy), (sx, 2 * sy, sy))
    v = lax.dot_general(pick, v, (((2,), (1,)), ((0,), (0,))), precision=HIGH)
    v = jnp.broadcast_to(v[:, None], (sx, 2) + v.shape[1:]).reshape((2 * sx,) + v.shape[1:])
    return v


def build_level(coeffs, n, margin, spacing):
    kx, ky, kz, store = coeffs[0], coeffs[1], coeffs[2], coeffs[3]
    fx = harmonic(kx[1:], kx[:-1]) * spacing
    fy = harmonic(ky[:, 1:], ky[:, :-1]) * spacing
    vertical = harmonic(kz[:, :, 1:], kz[:, :, :-1]) * spacing
    closed = jnp.zeros_like(kz[:, :, :1])
    above = jnp.concatenate([vertical, closed], axis=2)
    below = jnp.concatenate([closed, vertical], axis=2)
    level = dict(n=n, m=margin, fx=fx, fy=fy, above=above, below=below, store=store)
    r = margin - 1
    level["diag"] = jnp.maximum(faces_sum(level, r) + win(store, n, margin, r), 0.01)
    level["dm"] = r
    return level


def faces_sum(level, r):
    n, m = level["n"], level["m"]
    east = win(level["fx"], n, m, r)
    west = win(level["fx"], n, m, r, dx=-1)
    north = win(level["fy"], n, m, r)
    south = win(level["fy"], n, m, r, dy=-1)
    above = win(level["above"], n, m, r)
    below = win(level["below"], n, m, r)
    return east + west + north + south + above + below


def operate(values, vm, level):
    n, m = level["n"], level["m"]
    r = vm - 1
    centre = win(values, n, vm, r)
    upper = jnp.concatenate([centre[:, :, 1:], centre[:, :, :1]], axis=2)
    lower = jnp.concatenate([centre[:, :, -1:], centre[:, :, :-1]], axis=2)
    fx, fy = level["fx"], level["fy"]
    fluxes = win(fx, n, m, r) * (centre - win(values, n, vm, r, dx=1))
    fluxes = fluxes + win(fx, n, m, r, dx=-1) * (centre - win(values, n, vm, r, dx=-1))
    fluxes = fluxes + win(fy, n, m, r) * (centre - win(values, n, vm, r, dy=1))
    fluxes = fluxes + win(fy, n, m, r, dy=-1) * (centre - win(values, n, vm, r, dy=-1))
    fluxes = fluxes + win(level["above"], n, m, r) * (centre - upper)
    fluxes = fluxes + win(level["below"], n, m, r) * (centre - lower)
    return win(level["store"], n, m, r) * centre + fluxes


def chebyshev(target, tm, initial, im, level):
    n = level["n"]
    diag, dm = level["diag"], level["dm"]
    if initial is None:
        cur = min(tm, dm)
        misfit = win(target, n, tm, cur)
        update = misfit / win(diag, n, dm, cur) * (1.0 / cheb_centre)
        iterate = update
    else:
        applied = operate(initial, im, level)
        cur = im - 1
        misfit = win(target, n, tm, cur) - applied
        update = misfit / win(diag, n, dm, cur) * (1.0 / cheb_centre)
        iterate = win(initial, n, im, cur) + update
    factor = 1.0 / cheb_ratio
    for repeat in range(CHEB - 1):
        applied = operate(iterate, cur, level)
        nxt = cur - 1
        misfit = win(target, n, tm, nxt) - applied
        factor_new = 1.0 / (2.0 * cheb_ratio - factor)
        update = factor_new * factor * win(update, n, cur, nxt) + 2.0 * factor_new / cheb_half * (
            misfit / win(diag, n, dm, nxt)
        )
        iterate = win(iterate, n, cur, nxt) + update
        cur = nxt
        factor = factor_new
    return iterate, cur


def fields_kernel(frame, table_ref, conc_ref, idf_ref, out_ref):
    rows = conc_ref.shape[0]
    shape = conc_ref.shape[1:]
    mats = table_ref.shape[1]
    nx, ny, hf = frame
    x_lo = hf - lax.axis_index("gx") * nx
    y_lo = hf - lax.axis_index("gy") * ny
    x_hi = x_lo + lax.axis_size("gx") * nx
    y_hi = y_lo + lax.axis_size("gy") * ny
    col = lax.broadcasted_iota(jnp.int32, shape, 0)
    col_ok = (col >= y_lo) & (col < y_hi)

    def body(i, carry):
        ids = idf_ref[i]
        conc = conc_ref[i]
        row = jnp.zeros(shape, jnp.int32) + i
        ok = col_ok & (row >= x_lo) & (row < x_hi)
        vals = []
        for record in range(5):
            acc = jnp.zeros(shape, jnp.float32) + table_ref[record, mats - 1]
            for material in range(mats - 2, -1, -1):
                acc = jnp.where(ids == float(material), table_ref[record, material], acc)
            vals.append(acc)
        store = storage_scale * (1.0 + vals[3] * jnp.exp((vals[4] - 1.0) * jnp.log(conc)))
        out_ref[0, i] = jnp.where(ok, vals[0], 0.0)
        out_ref[1, i] = jnp.where(ok, vals[1], 0.0)
        out_ref[2, i] = jnp.where(ok, vals[2], 0.0)
        out_ref[3, i] = jnp.where(ok, store, 0.0)
        return carry

    lax.fori_loop(0, rows, body, 0, unroll=2)


def soil_fields(frame, soil_table, conc, idf):
    cells = conc.size
    return pl.pallas_call(
        functools.partial(fields_kernel, frame),
        out_shape=jax.ShapeDtypeStruct((4,) + conc.shape, jnp.float32),
        in_specs=[
            pl.BlockSpec(memory_space=pltpu.SMEM),
            pl.BlockSpec(memory_space=pltpu.VMEM),
            pl.BlockSpec(memory_space=pltpu.VMEM),
        ],
        out_specs=pl.BlockSpec(memory_space=pltpu.VMEM),
        cost_estimate=pl.CostEstimate(
            flops=100 * cells, transcendentals=2 * cells, bytes_accessed=24 * cells
        ),
    )(soil_table, conc, idf)


def local(conc_prev, right_side, soil_id, soil_table):
    n = conc_prev.shape[0]
    ny = conc_prev.shape[1]
    hf = FINE_HALO
    gx_count = lax.axis_size("gx")
    gy_count = lax.axis_size("gy")
    ix = lax.axis_index("gx")
    iy = lax.axis_index("gy")

    stacked = jnp.stack([conc_prev, right_side, soil_id.astype(jnp.float32)])
    ext = halo(stacked, (("gx", 1), ("gy", 2)), hf)
    conc, rhs, idf = ext[0], ext[1], ext[2]
    fine_c = soil_fields((n, ny, hf), soil_table, conc, idf)
    fine = build_level(fine_c, n, hf, 1.0)

    x0, x0m = chebyshev(rhs, hf, None, 0, fine)
    r0 = win(rhs, n, hf, x0m - 1) - operate(x0, x0m, fine)
    r0m = x0m - 1
    nm = n // 2
    mm = hf // 2
    mid_c = coarsen(fine_c)
    mid = build_level(mid_c, nm, mm, 0.25)
    b1 = coarsen(win(r0, n, r0m, 2 * (r0m // 2)))
    b1m = r0m // 2
    x1, x1m = chebyshev(b1, b1m, None, 0, mid)
    r1 = win(b1, nm, b1m, x1m - 1) - operate(x1, x1m, mid)
    r1m = x1m - 1
    b2 = coarsen(win(r1, nm, r1m, 0))
    coarse_own = coarsen(win(mid_c, nm, mm, 0))

    nc = b2.shape[0]
    cpack = jnp.concatenate([b2[None], coarse_own], axis=0)
    mpack = jnp.stack([win(x1, nm, x1m, 0), win(b1, nm, b1m, 0)])
    hm = MID_HALO
    blocks = [cpack]
    for step in range(1, gy_count):
        pairs = [(j, (j - step) % gy_count) for j in range(gy_count)]
        blocks.append(lax.ppermute(cpack, "gy", pairs))
    north = shift_from(mpack[:, :, :hm], "gy", 1)
    south = shift_from(mpack[:, :, nm - hm :], "gy", -1)
    mext = jnp.concatenate([south, mpack, north], axis=2)
    full = jnp.concatenate(blocks, axis=2)
    reach = 3
    parts = [shift_from(full, "gx", -d) for d in range(reach, 0, -1)]
    parts += [full]
    parts += [shift_from(full, "gx", d) for d in range(1, reach + 1)]
    cpack = jnp.concatenate(parts, axis=1)
    west_m = shift_from(mext[:, nm - hm :], "gx", -1)
    east_m = shift_from(mext[:, :hm], "gx", 1)
    mext = jnp.concatenate([west_m, mext, east_m], axis=1)
    source = cpack[0]
    cc = cpack[1:]
    line_total = jnp.sum(source, axis=1)
    line_store = jnp.sum(cc[3], axis=1)
    line_mean = jnp.where(line_store > 0, line_total / jnp.where(line_store > 0, line_store, 1.0), 0.0)
    width = source.shape[0]
    lines = source.shape[1]
    gline = (iy * nc + jnp.arange(lines)) % lines
    kx_, ky_, kz_, st_ = cc[0], cc[1], cc[2], cc[3]
    q = 0.0625
    cx = kx_[1:-1]
    cy = ky_[1:-1]
    cz = kz_[1:-1]
    east = harmonic(kx_[2:], cx) * q
    west = harmonic(kx_[:-2], cx) * q
    north = harmonic(jnp.roll(cy, -1, axis=1), cy) * q
    north = jnp.where((gline != lines - 1)[None, :, None], north, 0.0)
    south = jnp.roll(north, 1, axis=1)
    vert = harmonic(cz[:, :, 1:], cz[:, :, :-1]) * q
    closed = jnp.zeros_like(cz[:, :, :1])
    above = jnp.concatenate([vert, closed], axis=2)
    below = jnp.concatenate([closed, vert], axis=2)
    cst = st_[1:-1]
    cdiag = jnp.maximum(cst + east + west + north + south + above + below, 0.01)
    csrc = source[1:-1]
    u = jnp.broadcast_to(line_mean[:, None, :], source.shape)
    for sweep in range(COARSE_SWEEPS):
        lo = sweep
        centre = u[1:-1]
        sl = slice(lo, width - 2 - lo)
        upper = jnp.concatenate([centre[:, :, 1:], centre[:, :, :1]], axis=2)
        lower = jnp.concatenate([centre[:, :, -1:], centre[:, :, :-1]], axis=2)
        fl = east[sl] * (centre - u[2:]) + west[sl] * (centre - u[:-2])
        fl = fl + north[sl] * (centre - jnp.roll(centre, -1, axis=1))
        fl = fl + south[sl] * (centre - jnp.roll(centre, 1, axis=1))
        fl = fl + above[sl] * (centre - upper) + below[sl] * (centre - lower)
        applied = cst[sl] * centre + fl
        u = centre + jacobi_weight * ((csrc[sl] - applied) / cdiag[sl])
    um = (hm + 1) // 2
    have = reach * nc - COARSE_SWEEPS
    u = u[have - um : u.shape[0] - (have - um)]
    rows = [(k % lines) for k in range(-um, nc + um)]
    runs = []
    for r in rows:
        if runs and runs[-1][1] == r:
            runs[-1][1] = r + 1
        else:
            runs.append([r, r + 1])
    u = jnp.concatenate([u[:, a:b] for a, b in runs], axis=1)
    kept = iy * nc + jnp.arange(-um, nc + um)
    u = jnp.where(((kept >= 0) & (kept < lines))[None, :, None], u, 0.0)
    s1e = win(mext[0], nm, hm, hm) + win(prolong(u), nm, 2 * um, hm)
    b1e = mext[1]
    y1, y1m = chebyshev(b1e, hm, s1e, hm, mid)
    fm = 2 * y1m
    s0 = win(x0, n, x0m, fm) + prolong(y1)
    fs = min(fm, CHEB)
    s0 = win(s0, n, fm, fs)
    out, om = chebyshev(rhs, hf, s0, fs, fine)
    return out


def solution(mesh):
    placed = (P("gx", "gy", None), P("gx", "gy", None), P("gx", "gy", None), P())
    return jax.shard_map(
        local, mesh=mesh, in_specs=placed, out_specs=P("gx", "gy", None), check_vma=False
    )
```

```python
import functools

import jax
import jax.numpy as jnp
from jax import lax
from jax.sharding import PartitionSpec as P
from jax.experimental import pallas as pl
from jax.experimental.pallas import tpu as pltpu

CHEB = 3
COARSE_SWEEPS = 8

storage_scale = 0.05
cheb_centre = 1.1
cheb_half = 0.9
cheb_ratio = cheb_centre / cheb_half
jacobi_weight = 0.8

FINE_HALO = 10
MID_HALO = 5
HIGH = lax.Precision.HIGHEST


def shift_from(cells, axis, offset):
    count = lax.axis_size(axis)
    if offset > 0:
        pairs = [(i + offset, i) for i in range(count - offset)]
    else:
        pairs = [(i, i - offset) for i in range(count + offset)]
    if not pairs:
        return jnp.zeros_like(cells)
    return lax.ppermute(cells, axis, pairs)


def halo(cells, sides, width):
    for axis, dim in sides:
        size = cells.shape[dim]
        head = lax.slice_in_dim(cells, 0, width, axis=dim)
        tail = lax.slice_in_dim(cells, size - width, size, axis=dim)
        cells = jnp.concatenate(
            [shift_from(tail, axis, -1), cells, shift_from(head, axis, 1)], axis=dim
        )
    return cells


def harmonic(first, second):
    return first * second / jnp.maximum(0.5 * (first + second), 0.1)


def win(a, n, margin, r, dx=0, dy=0):
    lo = margin - r
    hi = margin + n + r
    return a[..., lo + dx : hi + dx, lo + dy : hi + dy, :]


def pair_matrix(size, dtype=jnp.float32):
    rows = jnp.arange(size)[:, None] // 2
    cols = jnp.arange(size // 2)[None, :]
    return (rows == cols).astype(dtype)


def coarsen(values):
    lead = values.shape[:-3]
    sx, sy, sz = values.shape[-3:]
    v = values.reshape(lead + (sx // 2, 2, sy, sz))
    v = v[..., 0, :, :] + v[..., 1, :, :]
    v = jnp.einsum("...yz,zw->...yw", v, pair_matrix(sz), precision=HIGH)
    rows = v.reshape((-1, sy, sz // 2))
    pick = jnp.broadcast_to(pair_matrix(sy).T, (rows.shape[0], sy // 2, sy))
    rows = lax.dot_general(pick, rows, (((2,), (1,)), ((0,), (0,))), precision=HIGH)
    v = rows.reshape(lead + (sx // 2, sy // 2, sz // 2))
    return v * 0.125


def prolong(values):
    sx, sy, sz = values.shape
    v = jnp.einsum("xyz,wz->xyw", values, pair_matrix(2 * sz), precision=HIGH)
    pick = jnp.broadcast_to(pair_matrix(2 * sy), (sx, 2 * sy, sy))
    v = lax.dot_general(pick, v, (((2,), (1,)), ((0,), (0,))), precision=HIGH)
    v = jnp.broadcast_to(v[:, None], (sx, 2) + v.shape[1:]).reshape((2 * sx,) + v.shape[1:])
    return v


def build_level(coeffs, n, margin, spacing):
    kx, ky, kz, store = coeffs[0], coeffs[1], coeffs[2], coeffs[3]
    fx = harmonic(kx[1:], kx[:-1]) * spacing
    fy = harmonic(ky[:, 1:], ky[:, :-1]) * spacing
    vertical = harmonic(kz[:, :, 1:], kz[:, :, :-1]) * spacing
    closed = jnp.zeros_like(kz[:, :, :1])
    above = jnp.concatenate([vertical, closed], axis=2)
    below = jnp.concatenate([closed, vertical], axis=2)
    level = dict(n=n, m=margin, fx=fx, fy=fy, above=above, below=below, store=store)
    r = margin - 1
    level["diag"] = jnp.maximum(faces_sum(level, r) + win(store, n, margin, r), 0.01)
    level["dm"] = r
    return level


def faces_sum(level, r):
    n, m = level["n"], level["m"]
    east = win(level["fx"], n, m, r)
    west = win(level["fx"], n, m, r, dx=-1)
    north = win(level["fy"], n, m, r)
    south = win(level["fy"], n, m, r, dy=-1)
    above = win(level["above"], n, m, r)
    below = win(level["below"], n, m, r)
    return east + west + north + south + above + below


def operate(values, vm, level):
    n, m = level["n"], level["m"]
    r = vm - 1
    centre = win(values, n, vm, r)
    upper = jnp.concatenate([centre[:, :, 1:], centre[:, :, :1]], axis=2)
    lower = jnp.concatenate([centre[:, :, -1:], centre[:, :, :-1]], axis=2)
    fx, fy = level["fx"], level["fy"]
    fluxes = win(fx, n, m, r) * (centre - win(values, n, vm, r, dx=1))
    fluxes = fluxes + win(fx, n, m, r, dx=-1) * (centre - win(values, n, vm, r, dx=-1))
    fluxes = fluxes + win(fy, n, m, r) * (centre - win(values, n, vm, r, dy=1))
    fluxes = fluxes + win(fy, n, m, r, dy=-1) * (centre - win(values, n, vm, r, dy=-1))
    fluxes = fluxes + win(level["above"], n, m, r) * (centre - upper)
    fluxes = fluxes + win(level["below"], n, m, r) * (centre - lower)
    return win(level["store"], n, m, r) * centre + fluxes


def chebyshev(target, tm, initial, im, level):
    n = level["n"]
    diag, dm = level["diag"], level["dm"]
    if initial is None:
        cur = min(tm, dm)
        misfit = win(target, n, tm, cur)
        update = misfit / win(diag, n, dm, cur) * (1.0 / cheb_centre)
        iterate = update
    else:
        applied = operate(initial, im, level)
        cur = im - 1
        misfit = win(target, n, tm, cur) - applied
        update = misfit / win(diag, n, dm, cur) * (1.0 / cheb_centre)
        iterate = win(initial, n, im, cur) + update
    factor = 1.0 / cheb_ratio
    for repeat in range(CHEB - 1):
        applied = operate(iterate, cur, level)
        nxt = cur - 1
        misfit = win(target, n, tm, nxt) - applied
        factor_new = 1.0 / (2.0 * cheb_ratio - factor)
        update = factor_new * factor * win(update, n, cur, nxt) + 2.0 * factor_new / cheb_half * (
            misfit / win(diag, n, dm, nxt)
        )
        iterate = win(iterate, n, cur, nxt) + update
        cur = nxt
        factor = factor_new
    return iterate, cur


def fields_kernel(frame, table_ref, conc_ref, idf_ref, out_ref):
    rows = conc_ref.shape[0]
    shape = conc_ref.shape[1:]
    mats = table_ref.shape[1]
    nx, ny, hf = frame
    x_lo = hf - lax.axis_index("gx") * nx
    y_lo = hf - lax.axis_index("gy") * ny
    x_hi = x_lo + lax.axis_size("gx") * nx
    y_hi = y_lo + lax.axis_size("gy") * ny
    col = lax.broadcasted_iota(jnp.int32, shape, 0)
    col_ok = (col >= y_lo) & (col < y_hi)

    def body(i, carry):
        ids = idf_ref[i]
        conc = conc_ref[i]
        row = jnp.zeros(shape, jnp.int32) + i
        ok = col_ok & (row >= x_lo) & (row < x_hi)
        vals = []
        for record in range(5):
            acc = jnp.zeros(shape, jnp.float32) + table_ref[record, mats - 1]
            for material in range(mats - 2, -1, -1):
                acc = jnp.where(ids == float(material), table_ref[record, material], acc)
            vals.append(acc)
        store = storage_scale * (1.0 + vals[3] * jnp.exp((vals[4] - 1.0) * jnp.log(conc)))
        out_ref[0, i] = jnp.where(ok, vals[0], 0.0)
        out_ref[1, i] = jnp.where(ok, vals[1], 0.0)
        out_ref[2, i] = jnp.where(ok, vals[2], 0.0)
        out_ref[3, i] = jnp.where(ok, store, 0.0)
        return carry

    lax.fori_loop(0, rows, body, 0, unroll=2)


def soil_fields(frame, soil_table, conc, idf):
    cells = conc.size
    return pl.pallas_call(
        functools.partial(fields_kernel, frame),
        out_shape=jax.ShapeDtypeStruct((4,) + conc.shape, jnp.float32),
        in_specs=[
            pl.BlockSpec(memory_space=pltpu.SMEM),
            pl.BlockSpec(memory_space=pltpu.VMEM),
            pl.BlockSpec(memory_space=pltpu.VMEM),
        ],
        out_specs=pl.BlockSpec(memory_space=pltpu.VMEM),
        cost_estimate=pl.CostEstimate(
            flops=100 * cells, transcendentals=2 * cells, bytes_accessed=24 * cells
        ),
    )(soil_table, conc, idf)


def local(conc_prev, right_side, soil_id, soil_table):
    n = conc_prev.shape[0]
    ny = conc_prev.shape[1]
    hf = FINE_HALO
    gx_count = lax.axis_size("gx")
    gy_count = lax.axis_size("gy")
    ix = lax.axis_index("gx")
    iy = lax.axis_index("gy")

    stacked = jnp.stack([conc_prev, right_side, soil_id.astype(jnp.float32)])
    ext = halo(stacked, (("gy", 2), ("gx", 1)), hf)
    conc, rhs, idf = ext[0], ext[1], ext[2]
    fine_c = soil_fields((n, ny, hf), soil_table, conc, idf)
    fine = build_level(fine_c, n, hf, 1.0)

    x0, x0m = chebyshev(rhs, hf, None, 0, fine)
    r0 = win(rhs, n, hf, x0m - 1) - operate(x0, x0m, fine)
    r0m = x0m - 1
    nm = n // 2
    mm = hf // 2
    mid_c = coarsen(fine_c)
    mid = build_level(mid_c, nm, mm, 0.25)
    b1 = coarsen(win(r0, n, r0m, 2 * (r0m // 2)))
    b1m = r0m // 2
    x1, x1m = chebyshev(b1, b1m, None, 0, mid)
    r1 = win(b1, nm, b1m, x1m - 1) - operate(x1, x1m, mid)
    r1m = x1m - 1
    b2 = coarsen(win(r1, nm, r1m, 0))
    coarse_own = coarsen(win(mid_c, nm, mm, 0))

    nc = b2.shape[0]
    cpack = jnp.concatenate([b2[None], coarse_own], axis=0)
    mpack = jnp.stack([win(x1, nm, x1m, 0), win(b1, nm, b1m, 0)])
    hm = MID_HALO
    blocks = [cpack]
    for step in range(1, gy_count):
        pairs = [(j, (j - step) % gy_count) for j in range(gy_count)]
        blocks.append(lax.ppermute(cpack, "gy", pairs))
    north = shift_from(mpack[:, :, :hm], "gy", 1)
    south = shift_from(mpack[:, :, nm - hm :], "gy", -1)
    mext = jnp.concatenate([south, mpack, north], axis=2)
    full = jnp.concatenate(blocks, axis=2)
    reach = 3
    parts = [shift_from(full, "gx", -d) for d in range(reach, 0, -1)]
    parts += [full]
    parts += [shift_from(full, "gx", d) for d in range(1, reach + 1)]
    cpack = jnp.concatenate(parts, axis=1)
    west_m = shift_from(mext[:, nm - hm :], "gx", -1)
    east_m = shift_from(mext[:, :hm], "gx", 1)
    mext = jnp.concatenate([west_m, mext, east_m], axis=1)
    source = cpack[0]
    cc = cpack[1:]
    line_total = jnp.sum(source, axis=1)
    line_store = jnp.sum(cc[3], axis=1)
    line_mean = jnp.where(line_store > 0, line_total / jnp.where(line_store > 0, line_store, 1.0), 0.0)
    width = source.shape[0]
    lines = source.shape[1]
    gline = (iy * nc + jnp.arange(lines)) % lines
    kx_, ky_, kz_, st_ = cc[0], cc[1], cc[2], cc[3]
    q = 0.0625
    cx = kx_[1:-1]
    cy = ky_[1:-1]
    cz = kz_[1:-1]
    east = harmonic(kx_[2:], cx) * q
    west = harmonic(kx_[:-2], cx) * q
    north = harmonic(jnp.roll(cy, -1, axis=1), cy) * q
    north = jnp.where((gline != lines - 1)[None, :, None], north, 0.0)
    south = jnp.roll(north, 1, axis=1)
    vert = harmonic(cz[:, :, 1:], cz[:, :, :-1]) * q
    closed = jnp.zeros_like(cz[:, :, :1])
    above = jnp.concatenate([vert, closed], axis=2)
    below = jnp.concatenate([closed, vert], axis=2)
    cst = st_[1:-1]
    cdiag = jnp.maximum(cst + east + west + north + south + above + below, 0.01)
    csrc = source[1:-1]
    u = jnp.broadcast_to(line_mean[:, None, :], source.shape)
    for sweep in range(COARSE_SWEEPS):
        lo = sweep
        centre = u[1:-1]
        sl = slice(lo, width - 2 - lo)
        upper = jnp.concatenate([centre[:, :, 1:], centre[:, :, :1]], axis=2)
        lower = jnp.concatenate([centre[:, :, -1:], centre[:, :, :-1]], axis=2)
        fl = east[sl] * (centre - u[2:]) + west[sl] * (centre - u[:-2])
        fl = fl + north[sl] * (centre - jnp.roll(centre, -1, axis=1))
        fl = fl + south[sl] * (centre - jnp.roll(centre, 1, axis=1))
        fl = fl + above[sl] * (centre - upper) + below[sl] * (centre - lower)
        applied = cst[sl] * centre + fl
        u = centre + jacobi_weight * ((csrc[sl] - applied) / cdiag[sl])
    um = (hm + 1) // 2
    have = reach * nc - COARSE_SWEEPS
    u = u[have - um : u.shape[0] - (have - um)]
    rows = [(k % lines) for k in range(-um, nc + um)]
    runs = []
    for r in rows:
        if runs and runs[-1][1] == r:
            runs[-1][1] = r + 1
        else:
            runs.append([r, r + 1])
    u = jnp.concatenate([u[:, a:b] for a, b in runs], axis=1)
    kept = iy * nc + jnp.arange(-um, nc + um)
    u = jnp.where(((kept >= 0) & (kept < lines))[None, :, None], u, 0.0)
    s1e = win(mext[0], nm, hm, hm) + win(prolong(u), nm, 2 * um, hm)
    b1e = mext[1]
    y1, y1m = chebyshev(b1e, hm, s1e, hm, mid)
    fm = 2 * y1m
    s0 = win(x0, n, x0m, fm) + prolong(y1)
    fs = min(fm, CHEB)
    s0 = win(s0, n, fm, fs)
    out, om = chebyshev(rhs, hf, s0, fs, fine)
    return out


def solution(mesh):
    placed = (P("gx", "gy", None), P("gx", "gy", None), P("gx", "gy", None), P())
    return jax.shard_map(
        local, mesh=mesh, in_specs=placed, out_specs=P("gx", "gy", None), check_vma=False
    )
```

```python
import functools

import jax
import jax.numpy as jnp
from jax import lax
from jax.sharding import PartitionSpec as P
from jax.experimental import pallas as pl
from jax.experimental.pallas import tpu as pltpu

CHEB = 3
COARSE_SWEEPS = 8

storage_scale = 0.05
cheb_centre = 1.1
cheb_half = 0.9
cheb_ratio = cheb_centre / cheb_half
jacobi_weight = 0.8

FINE_HALO = 10
MID_HALO = 5
HIGH = lax.Precision.HIGHEST


def shift_from(cells, axis, offset):
    count = lax.axis_size(axis)
    if offset > 0:
        pairs = [(i + offset, i) for i in range(count - offset)]
    else:
        pairs = [(i, i - offset) for i in range(count + offset)]
    if not pairs:
        return jnp.zeros_like(cells)
    return lax.ppermute(cells, axis, pairs)


def halo(cells, sides, width):
    for axis, dim in sides:
        size = cells.shape[dim]
        head = lax.slice_in_dim(cells, 0, width, axis=dim)
        tail = lax.slice_in_dim(cells, size - width, size, axis=dim)
        cells = jnp.concatenate(
            [shift_from(tail, axis, -1), cells, shift_from(head, axis, 1)], axis=dim
        )
    return cells


def halo_overlapped(cells, width):
    sx, sy = cells.shape[1], cells.shape[2]
    west = shift_from(cells[:, sx - width :], "gx", -1)
    east = shift_from(cells[:, :width], "gx", 1)
    south = shift_from(cells[:, :, sy - width :], "gy", -1)
    north = shift_from(cells[:, :, :width], "gy", 1)
    low = shift_from(jnp.concatenate([west[:, :, sy - width :], east[:, :, sy - width :]], axis=1), "gy", -1)
    high = shift_from(jnp.concatenate([west[:, :, :width], east[:, :, :width]], axis=1), "gy", 1)
    top = jnp.concatenate([low[:, :width], west, high[:, :width]], axis=2)
    mid = jnp.concatenate([south, cells, north], axis=2)
    bottom = jnp.concatenate([low[:, width:], east, high[:, width:]], axis=2)
    return jnp.concatenate([top, mid, bottom], axis=1)


def harmonic(first, second):
    return first * second / jnp.maximum(0.5 * (first + second), 0.1)


def win(a, n, margin, r, dx=0, dy=0):
    lo = margin - r
    hi = margin + n + r
    return a[..., lo + dx : hi + dx, lo + dy : hi + dy, :]


def pair_matrix(size, dtype=jnp.float32):
    rows = jnp.arange(size)[:, None] // 2
    cols = jnp.arange(size // 2)[None, :]
    return (rows == cols).astype(dtype)


def coarsen(values):
    lead = values.shape[:-3]
    sx, sy, sz = values.shape[-3:]
    v = values.reshape(lead + (sx // 2, 2, sy, sz))
    v = v[..., 0, :, :] + v[..., 1, :, :]
    v = jnp.einsum("...yz,zw->...yw", v, pair_matrix(sz), precision=HIGH)
    rows = v.reshape((-1, sy, sz // 2))
    pick = jnp.broadcast_to(pair_matrix(sy).T, (rows.shape[0], sy // 2, sy))
    rows = lax.dot_general(pick, rows, (((2,), (1,)), ((0,), (0,))), precision=HIGH)
    v = rows.reshape(lead + (sx // 2, sy // 2, sz // 2))
    return v * 0.125


def prolong(values):
    sx, sy, sz = values.shape
    v = jnp.einsum("xyz,wz->xyw", values, pair_matrix(2 * sz), precision=HIGH)
    pick = jnp.broadcast_to(pair_matrix(2 * sy), (sx, 2 * sy, sy))
    v = lax.dot_general(pick, v, (((2,), (1,)), ((0,), (0,))), precision=HIGH)
    v = jnp.broadcast_to(v[:, None], (sx, 2) + v.shape[1:]).reshape((2 * sx,) + v.shape[1:])
    return v


def build_level(coeffs, n, margin, spacing):
    kx, ky, kz, store = coeffs[0], coeffs[1], coeffs[2], coeffs[3]
    fx = harmonic(kx[1:], kx[:-1]) * spacing
    fy = harmonic(ky[:, 1:], ky[:, :-1]) * spacing
    vertical = harmonic(kz[:, :, 1:], kz[:, :, :-1]) * spacing
    closed = jnp.zeros_like(kz[:, :, :1])
    above = jnp.concatenate([vertical, closed], axis=2)
    below = jnp.concatenate([closed, vertical], axis=2)
    level = dict(n=n, m=margin, fx=fx, fy=fy, above=above, below=below, store=store)
    r = margin - 1
    level["diag"] = jnp.maximum(faces_sum(level, r) + win(store, n, margin, r), 0.01)
    level["dm"] = r
    return level


def faces_sum(level, r):
    n, m = level["n"], level["m"]
    east = win(level["fx"], n, m, r)
    west = win(level["fx"], n, m, r, dx=-1)
    north = win(level["fy"], n, m, r)
    south = win(level["fy"], n, m, r, dy=-1)
    above = win(level["above"], n, m, r)
    below = win(level["below"], n, m, r)
    return east + west + north + south + above + below


def operate(values, vm, level):
    n, m = level["n"], level["m"]
    r = vm - 1
    centre = win(values, n, vm, r)
    upper = jnp.concatenate([centre[:, :, 1:], centre[:, :, :1]], axis=2)
    lower = jnp.concatenate([centre[:, :, -1:], centre[:, :, :-1]], axis=2)
    fx, fy = level["fx"], level["fy"]
    fluxes = win(fx, n, m, r) * (centre - win(values, n, vm, r, dx=1))
    fluxes = fluxes + win(fx, n, m, r, dx=-1) * (centre - win(values, n, vm, r, dx=-1))
    fluxes = fluxes + win(fy, n, m, r) * (centre - win(values, n, vm, r, dy=1))
    fluxes = fluxes + win(fy, n, m, r, dy=-1) * (centre - win(values, n, vm, r, dy=-1))
    fluxes = fluxes + win(level["above"], n, m, r) * (centre - upper)
    fluxes = fluxes + win(level["below"], n, m, r) * (centre - lower)
    return win(level["store"], n, m, r) * centre + fluxes


def chebyshev(target, tm, initial, im, level):
    n = level["n"]
    diag, dm = level["diag"], level["dm"]
    if initial is None:
        cur = min(tm, dm)
        misfit = win(target, n, tm, cur)
        update = misfit / win(diag, n, dm, cur) * (1.0 / cheb_centre)
        iterate = update
    else:
        applied = operate(initial, im, level)
        cur = im - 1
        misfit = win(target, n, tm, cur) - applied
        update = misfit / win(diag, n, dm, cur) * (1.0 / cheb_centre)
        iterate = win(initial, n, im, cur) + update
    factor = 1.0 / cheb_ratio
    for repeat in range(CHEB - 1):
        applied = operate(iterate, cur, level)
        nxt = cur - 1
        misfit = win(target, n, tm, nxt) - applied
        factor_new = 1.0 / (2.0 * cheb_ratio - factor)
        update = factor_new * factor * win(update, n, cur, nxt) + 2.0 * factor_new / cheb_half * (
            misfit / win(diag, n, dm, nxt)
        )
        iterate = win(iterate, n, cur, nxt) + update
        cur = nxt
        factor = factor_new
    return iterate, cur


def fields_kernel(frame, table_ref, conc_ref, idf_ref, out_ref):
    rows = conc_ref.shape[0]
    shape = conc_ref.shape[1:]
    mats = table_ref.shape[1]
    nx, ny, hf = frame
    x_lo = hf - lax.axis_index("gx") * nx
    y_lo = hf - lax.axis_index("gy") * ny
    x_hi = x_lo + lax.axis_size("gx") * nx
    y_hi = y_lo + lax.axis_size("gy") * ny
    col = lax.broadcasted_iota(jnp.int32, shape, 0)
    col_ok = (col >= y_lo) & (col < y_hi)

    def body(i, carry):
        ids = idf_ref[i]
        conc = conc_ref[i]
        row = jnp.zeros(shape, jnp.int32) + i
        ok = col_ok & (row >= x_lo) & (row < x_hi)
        vals = []
        for record in range(5):
            acc = jnp.zeros(shape, jnp.float32) + table_ref[record, mats - 1]
            for material in range(mats - 2, -1, -1):
                acc = jnp.where(ids == float(material), table_ref[record, material], acc)
            vals.append(acc)
        store = storage_scale * (1.0 + vals[3] * jnp.exp((vals[4] - 1.0) * jnp.log(conc)))
        out_ref[0, i] = jnp.where(ok, vals[0], 0.0)
        out_ref[1, i] = jnp.where(ok, vals[1], 0.0)
        out_ref[2, i] = jnp.where(ok, vals[2], 0.0)
        out_ref[3, i] = jnp.where(ok, store, 0.0)
        return carry

    lax.fori_loop(0, rows, body, 0, unroll=2)


def soil_fields(frame, soil_table, conc, idf):
    cells = conc.size
    return pl.pallas_call(
        functools.partial(fields_kernel, frame),
        out_shape=jax.ShapeDtypeStruct((4,) + conc.shape, jnp.float32),
        in_specs=[
            pl.BlockSpec(memory_space=pltpu.SMEM),
            pl.BlockSpec(memory_space=pltpu.VMEM),
            pl.BlockSpec(memory_space=pltpu.VMEM),
        ],
        out_specs=pl.BlockSpec(memory_space=pltpu.VMEM),
        cost_estimate=pl.CostEstimate(
            flops=100 * cells, transcendentals=2 * cells, bytes_accessed=24 * cells
        ),
    )(soil_table, conc, idf)


def local(conc_prev, right_side, soil_id, soil_table):
    n = conc_prev.shape[0]
    ny = conc_prev.shape[1]
    hf = FINE_HALO
    gx_count = lax.axis_size("gx")
    gy_count = lax.axis_size("gy")
    ix = lax.axis_index("gx")
    iy = lax.axis_index("gy")

    stacked = jnp.stack([conc_prev, right_side, soil_id.astype(jnp.float32)])
    ext = halo_overlapped(stacked, hf)
    conc, rhs, idf = ext[0], ext[1], ext[2]
    fine_c = soil_fields((n, ny, hf), soil_table, conc, idf)
    fine = build_level(fine_c, n, hf, 1.0)

    x0, x0m = chebyshev(rhs, hf, None, 0, fine)
    r0 = win(rhs, n, hf, x0m - 1) - operate(x0, x0m, fine)
    r0m = x0m - 1
    nm = n // 2
    mm = hf // 2
    mid_c = coarsen(fine_c)
    mid = build_level(mid_c, nm, mm, 0.25)
    b1 = coarsen(win(r0, n, r0m, 2 * (r0m // 2)))
    b1m = r0m // 2
    x1, x1m = chebyshev(b1, b1m, None, 0, mid)
    r1 = win(b1, nm, b1m, x1m - 1) - operate(x1, x1m, mid)
    r1m = x1m - 1
    b2 = coarsen(win(r1, nm, r1m, 0))
    coarse_own = coarsen(win(mid_c, nm, mm, 0))

    nc = b2.shape[0]
    cpack = jnp.concatenate([b2[None], coarse_own], axis=0)
    mpack = jnp.stack([win(x1, nm, x1m, 0), win(b1, nm, b1m, 0)])
    hm = MID_HALO
    blocks = [cpack]
    for step in range(1, gy_count):
        pairs = [(j, (j - step) % gy_count) for j in range(gy_count)]
        blocks.append(lax.ppermute(cpack, "gy", pairs))
    north = shift_from(mpack[:, :, :hm], "gy", 1)
    south = shift_from(mpack[:, :, nm - hm :], "gy", -1)
    mext = jnp.concatenate([south, mpack, north], axis=2)
    full = jnp.concatenate(blocks, axis=2)
    reach = 3
    parts = [shift_from(full, "gx", -d) for d in range(reach, 0, -1)]
    parts += [full]
    parts += [shift_from(full, "gx", d) for d in range(1, reach + 1)]
    cpack = jnp.concatenate(parts, axis=1)
    west_m = shift_from(mext[:, nm - hm :], "gx", -1)
    east_m = shift_from(mext[:, :hm], "gx", 1)
    mext = jnp.concatenate([west_m, mext, east_m], axis=1)
    source = cpack[0]
    cc = cpack[1:]
    line_total = jnp.sum(source, axis=1)
    line_store = jnp.sum(cc[3], axis=1)
    line_mean = jnp.where(line_store > 0, line_total / jnp.where(line_store > 0, line_store, 1.0), 0.0)
    width = source.shape[0]
    lines = source.shape[1]
    gline = (iy * nc + jnp.arange(lines)) % lines
    kx_, ky_, kz_, st_ = cc[0], cc[1], cc[2], cc[3]
    q = 0.0625
    cx = kx_[1:-1]
    cy = ky_[1:-1]
    cz = kz_[1:-1]
    east = harmonic(kx_[2:], cx) * q
    west = harmonic(kx_[:-2], cx) * q
    north = harmonic(jnp.roll(cy, -1, axis=1), cy) * q
    north = jnp.where((gline != lines - 1)[None, :, None], north, 0.0)
    south = jnp.roll(north, 1, axis=1)
    vert = harmonic(cz[:, :, 1:], cz[:, :, :-1]) * q
    closed = jnp.zeros_like(cz[:, :, :1])
    above = jnp.concatenate([vert, closed], axis=2)
    below = jnp.concatenate([closed, vert], axis=2)
    cst = st_[1:-1]
    cdiag = jnp.maximum(cst + east + west + north + south + above + below, 0.01)
    csrc = source[1:-1]
    u = jnp.broadcast_to(line_mean[:, None, :], source.shape)
    for sweep in range(COARSE_SWEEPS):
        lo = sweep
        centre = u[1:-1]
        sl = slice(lo, width - 2 - lo)
        upper = jnp.concatenate([centre[:, :, 1:], centre[:, :, :1]], axis=2)
        lower = jnp.concatenate([centre[:, :, -1:], centre[:, :, :-1]], axis=2)
        fl = east[sl] * (centre - u[2:]) + west[sl] * (centre - u[:-2])
        fl = fl + north[sl] * (centre - jnp.roll(centre, -1, axis=1))
        fl = fl + south[sl] * (centre - jnp.roll(centre, 1, axis=1))
        fl = fl + above[sl] * (centre - upper) + below[sl] * (centre - lower)
        applied = cst[sl] * centre + fl
        u = centre + jacobi_weight * ((csrc[sl] - applied) / cdiag[sl])
    um = (hm + 1) // 2
    have = reach * nc - COARSE_SWEEPS
    u = u[have - um : u.shape[0] - (have - um)]
    rows = [(k % lines) for k in range(-um, nc + um)]
    runs = []
    for r in rows:
        if runs and runs[-1][1] == r:
            runs[-1][1] = r + 1
        else:
            runs.append([r, r + 1])
    u = jnp.concatenate([u[:, a:b] for a, b in runs], axis=1)
    kept = iy * nc + jnp.arange(-um, nc + um)
    u = jnp.where(((kept >= 0) & (kept < lines))[None, :, None], u, 0.0)
    s1e = win(mext[0], nm, hm, hm) + win(prolong(u), nm, 2 * um, hm)
    b1e = mext[1]
    y1, y1m = chebyshev(b1e, hm, s1e, hm, mid)
    fm = 2 * y1m
    s0 = win(x0, n, x0m, fm) + prolong(y1)
    fs = min(fm, CHEB)
    s0 = win(s0, n, fm, fs)
    out, om = chebyshev(rhs, hf, s0, fs, fine)
    return out


def solution(mesh):
    placed = (P("gx", "gy", None), P("gx", "gy", None), P("gx", "gy", None), P())
    return jax.shard_map(
        local, mesh=mesh, in_specs=placed, out_specs=P("gx", "gy", None), check_vma=False
    )
```

```python
import functools

import jax
import jax.numpy as jnp
from jax import lax
from jax.sharding import PartitionSpec as P
from jax.experimental import pallas as pl
from jax.experimental.pallas import tpu as pltpu

CHEB = 3
COARSE_SWEEPS = 8

storage_scale = 0.05
cheb_centre = 1.1
cheb_half = 0.9
cheb_ratio = cheb_centre / cheb_half
jacobi_weight = 0.8

FINE_HALO = 10
MID_HALO = 5
HIGH = lax.Precision.HIGHEST


def shift_from(cells, axis, offset):
    count = lax.axis_size(axis)
    if offset > 0:
        pairs = [(i + offset, i) for i in range(count - offset)]
    else:
        pairs = [(i, i - offset) for i in range(count + offset)]
    if not pairs:
        return jnp.zeros_like(cells)
    return lax.ppermute(cells, axis, pairs)


def halo(cells, sides, width):
    for axis, dim in sides:
        size = cells.shape[dim]
        head = lax.slice_in_dim(cells, 0, width, axis=dim)
        tail = lax.slice_in_dim(cells, size - width, size, axis=dim)
        cells = jnp.concatenate(
            [shift_from(tail, axis, -1), cells, shift_from(head, axis, 1)], axis=dim
        )
    return cells


def halo_overlapped(cells, width):
    sx, sy = cells.shape[1], cells.shape[2]
    west = shift_from(cells[:, sx - width :], "gx", -1)
    east = shift_from(cells[:, :width], "gx", 1)
    south = shift_from(cells[:, :, sy - width :], "gy", -1)
    north = shift_from(cells[:, :, :width], "gy", 1)
    low = shift_from(jnp.concatenate([west[:, :, sy - width :], east[:, :, sy - width :]], axis=1), "gy", -1)
    high = shift_from(jnp.concatenate([west[:, :, :width], east[:, :, :width]], axis=1), "gy", 1)
    top = jnp.concatenate([low[:, :width], west, high[:, :width]], axis=2)
    mid = jnp.concatenate([south, cells, north], axis=2)
    bottom = jnp.concatenate([low[:, width:], east, high[:, width:]], axis=2)
    return jnp.concatenate([top, mid, bottom], axis=1)


def frames_overlapped(fields, width):
    sx, sy = fields[0].shape[0], fields[0].shape[1]

    def slab(xs, ys):
        return jnp.stack([f[xs, ys] for f in fields])

    every = slice(None)
    west = shift_from(slab(slice(sx - width, sx), every), "gx", -1)
    east = shift_from(slab(slice(0, width), every), "gx", 1)
    south = shift_from(slab(every, slice(sy - width, sy)), "gy", -1)
    north = shift_from(slab(every, slice(0, width)), "gy", 1)
    low = shift_from(jnp.concatenate([west[:, :, sy - width :], east[:, :, sy - width :]], axis=1), "gy", -1)
    high = shift_from(jnp.concatenate([west[:, :, :width], east[:, :, :width]], axis=1), "gy", 1)
    out = []
    for k, f in enumerate(fields):
        top = jnp.concatenate([low[k, :width], west[k], high[k, :width]], axis=1)
        mid = jnp.concatenate([south[k], f, north[k]], axis=1)
        bottom = jnp.concatenate([low[k, width:], east[k], high[k, width:]], axis=1)
        out.append(jnp.concatenate([top, mid, bottom], axis=0))
    return out


def harmonic(first, second):
    return first * second / jnp.maximum(0.5 * (first + second), 0.1)


def win(a, n, margin, r, dx=0, dy=0):
    lo = margin - r
    hi = margin + n + r
    return a[..., lo + dx : hi + dx, lo + dy : hi + dy, :]


def pair_matrix(size, dtype=jnp.float32):
    rows = jnp.arange(size)[:, None] // 2
    cols = jnp.arange(size // 2)[None, :]
    return (rows == cols).astype(dtype)


def coarsen(values):
    lead = values.shape[:-3]
    sx, sy, sz = values.shape[-3:]
    v = values.reshape(lead + (sx // 2, 2, sy, sz))
    v = v[..., 0, :, :] + v[..., 1, :, :]
    v = jnp.einsum("...yz,zw->...yw", v, pair_matrix(sz), precision=HIGH)
    rows = v.reshape((-1, sy, sz // 2))
    pick = jnp.broadcast_to(pair_matrix(sy).T, (rows.shape[0], sy // 2, sy))
    rows = lax.dot_general(pick, rows, (((2,), (1,)), ((0,), (0,))), precision=HIGH)
    v = rows.reshape(lead + (sx // 2, sy // 2, sz // 2))
    return v * 0.125


def prolong(values):
    sx, sy, sz = values.shape
    v = jnp.einsum("xyz,wz->xyw", values, pair_matrix(2 * sz), precision=HIGH)
    pick = jnp.broadcast_to(pair_matrix(2 * sy), (sx, 2 * sy, sy))
    v = lax.dot_general(pick, v, (((2,), (1,)), ((0,), (0,))), precision=HIGH)
    v = jnp.broadcast_to(v[:, None], (sx, 2) + v.shape[1:]).reshape((2 * sx,) + v.shape[1:])
    return v


def build_level(coeffs, n, margin, spacing):
    kx, ky, kz, store = coeffs[0], coeffs[1], coeffs[2], coeffs[3]
    fx = harmonic(kx[1:], kx[:-1]) * spacing
    fy = harmonic(ky[:, 1:], ky[:, :-1]) * spacing
    vertical = harmonic(kz[:, :, 1:], kz[:, :, :-1]) * spacing
    closed = jnp.zeros_like(kz[:, :, :1])
    above = jnp.concatenate([vertical, closed], axis=2)
    below = jnp.concatenate([closed, vertical], axis=2)
    level = dict(n=n, m=margin, fx=fx, fy=fy, above=above, below=below, store=store)
    r = margin - 1
    level["diag"] = jnp.maximum(faces_sum(level, r) + win(store, n, margin, r), 0.01)
    level["dm"] = r
    return level


def faces_sum(level, r):
    n, m = level["n"], level["m"]
    east = win(level["fx"], n, m, r)
    west = win(level["fx"], n, m, r, dx=-1)
    north = win(level["fy"], n, m, r)
    south = win(level["fy"], n, m, r, dy=-1)
    above = win(level["above"], n, m, r)
    below = win(level["below"], n, m, r)
    return east + west + north + south + above + below


def operate(values, vm, level):
    n, m = level["n"], level["m"]
    r = vm - 1
    centre = win(values, n, vm, r)
    upper = jnp.concatenate([centre[:, :, 1:], centre[:, :, :1]], axis=2)
    lower = jnp.concatenate([centre[:, :, -1:], centre[:, :, :-1]], axis=2)
    fx, fy = level["fx"], level["fy"]
    fluxes = win(fx, n, m, r) * (centre - win(values, n, vm, r, dx=1))
    fluxes = fluxes + win(fx, n, m, r, dx=-1) * (centre - win(values, n, vm, r, dx=-1))
    fluxes = fluxes + win(fy, n, m, r) * (centre - win(values, n, vm, r, dy=1))
    fluxes = fluxes + win(fy, n, m, r, dy=-1) * (centre - win(values, n, vm, r, dy=-1))
    fluxes = fluxes + win(level["above"], n, m, r) * (centre - upper)
    fluxes = fluxes + win(level["below"], n, m, r) * (centre - lower)
    return win(level["store"], n, m, r) * centre + fluxes


def chebyshev(target, tm, initial, im, level):
    n = level["n"]
    diag, dm = level["diag"], level["dm"]
    if initial is None:
        cur = min(tm, dm)
        misfit = win(target, n, tm, cur)
        update = misfit / win(diag, n, dm, cur) * (1.0 / cheb_centre)
        iterate = update
    else:
        applied = operate(initial, im, level)
        cur = im - 1
        misfit = win(target, n, tm, cur) - applied
        update = misfit / win(diag, n, dm, cur) * (1.0 / cheb_centre)
        iterate = win(initial, n, im, cur) + update
    factor = 1.0 / cheb_ratio
    for repeat in range(CHEB - 1):
        applied = operate(iterate, cur, level)
        nxt = cur - 1
        misfit = win(target, n, tm, nxt) - applied
        factor_new = 1.0 / (2.0 * cheb_ratio - factor)
        update = factor_new * factor * win(update, n, cur, nxt) + 2.0 * factor_new / cheb_half * (
            misfit / win(diag, n, dm, nxt)
        )
        iterate = win(iterate, n, cur, nxt) + update
        cur = nxt
        factor = factor_new
    return iterate, cur


def fields_kernel(frame, table_ref, conc_ref, idf_ref, out_ref):
    rows = conc_ref.shape[0]
    shape = conc_ref.shape[1:]
    mats = table_ref.shape[1]
    nx, ny, hf = frame
    x_lo = hf - lax.axis_index("gx") * nx
    y_lo = hf - lax.axis_index("gy") * ny
    x_hi = x_lo + lax.axis_size("gx") * nx
    y_hi = y_lo + lax.axis_size("gy") * ny
    col = lax.broadcasted_iota(jnp.int32, shape, 0)
    col_ok = (col >= y_lo) & (col < y_hi)

    def body(i, carry):
        ids = idf_ref[i]
        conc = conc_ref[i]
        row = jnp.zeros(shape, jnp.int32) + i
        ok = col_ok & (row >= x_lo) & (row < x_hi)
        vals = []
        for record in range(5):
            acc = jnp.zeros(shape, jnp.float32) + table_ref[record, mats - 1]
            for material in range(mats - 2, -1, -1):
                acc = jnp.where(ids == float(material), table_ref[record, material], acc)
            vals.append(acc)
        store = storage_scale * (1.0 + vals[3] * jnp.exp((vals[4] - 1.0) * jnp.log(conc)))
        out_ref[0, i] = jnp.where(ok, vals[0], 0.0)
        out_ref[1, i] = jnp.where(ok, vals[1], 0.0)
        out_ref[2, i] = jnp.where(ok, vals[2], 0.0)
        out_ref[3, i] = jnp.where(ok, store, 0.0)
        return carry

    lax.fori_loop(0, rows, body, 0, unroll=2)


def soil_fields(frame, soil_table, conc, idf):
    cells = conc.size
    return pl.pallas_call(
        functools.partial(fields_kernel, frame),
        out_shape=jax.ShapeDtypeStruct((4,) + conc.shape, jnp.float32),
        in_specs=[
            pl.BlockSpec(memory_space=pltpu.SMEM),
            pl.BlockSpec(memory_space=pltpu.VMEM),
            pl.BlockSpec(memory_space=pltpu.VMEM),
        ],
        out_specs=pl.BlockSpec(memory_space=pltpu.VMEM),
        cost_estimate=pl.CostEstimate(
            flops=100 * cells, transcendentals=2 * cells, bytes_accessed=24 * cells
        ),
    )(soil_table, conc, idf)


def local(conc_prev, right_side, soil_id, soil_table):
    n = conc_prev.shape[0]
    ny = conc_prev.shape[1]
    hf = FINE_HALO
    gx_count = lax.axis_size("gx")
    gy_count = lax.axis_size("gy")
    ix = lax.axis_index("gx")
    iy = lax.axis_index("gy")

    conc, rhs, idf = frames_overlapped([conc_prev, right_side, soil_id.astype(jnp.float32)], hf)
    fine_c = soil_fields((n, ny, hf), soil_table, conc, idf)
    fine = build_level(fine_c, n, hf, 1.0)

    x0, x0m = chebyshev(rhs, hf, None, 0, fine)
    r0 = win(rhs, n, hf, x0m - 1) - operate(x0, x0m, fine)
    r0m = x0m - 1
    nm = n // 2
    mm = hf // 2
    mid_c = coarsen(fine_c)
    mid = build_level(mid_c, nm, mm, 0.25)
    b1 = coarsen(win(r0, n, r0m, 2 * (r0m // 2)))
    b1m = r0m // 2
    x1, x1m = chebyshev(b1, b1m, None, 0, mid)
    r1 = win(b1, nm, b1m, x1m - 1) - operate(x1, x1m, mid)
    r1m = x1m - 1
    b2 = coarsen(win(r1, nm, r1m, 0))
    coarse_own = coarsen(win(mid_c, nm, mm, 0))

    nc = b2.shape[0]
    cpack = jnp.concatenate([b2[None], coarse_own], axis=0)
    mpack = jnp.stack([win(x1, nm, x1m, 0), win(b1, nm, b1m, 0)])
    hm = MID_HALO
    blocks = [cpack]
    for step in range(1, gy_count):
        pairs = [(j, (j - step) % gy_count) for j in range(gy_count)]
        blocks.append(lax.ppermute(cpack, "gy", pairs))
    north = shift_from(mpack[:, :, :hm], "gy", 1)
    south = shift_from(mpack[:, :, nm - hm :], "gy", -1)
    mext = jnp.concatenate([south, mpack, north], axis=2)
    full = jnp.concatenate(blocks, axis=2)
    reach = 3
    parts = [shift_from(full, "gx", -d) for d in range(reach, 0, -1)]
    parts += [full]
    parts += [shift_from(full, "gx", d) for d in range(1, reach + 1)]
    cpack = jnp.concatenate(parts, axis=1)
    west_m = shift_from(mext[:, nm - hm :], "gx", -1)
    east_m = shift_from(mext[:, :hm], "gx", 1)
    mext = jnp.concatenate([west_m, mext, east_m], axis=1)
    source = cpack[0]
    cc = cpack[1:]
    line_total = jnp.sum(source, axis=1)
    line_store = jnp.sum(cc[3], axis=1)
    line_mean = jnp.where(line_store > 0, line_total / jnp.where(line_store > 0, line_store, 1.0), 0.0)
    width = source.shape[0]
    lines = source.shape[1]
    gline = (iy * nc + jnp.arange(lines)) % lines
    kx_, ky_, kz_, st_ = cc[0], cc[1], cc[2], cc[3]
    q = 0.0625
    cx = kx_[1:-1]
    cy = ky_[1:-1]
    cz = kz_[1:-1]
    east = harmonic(kx_[2:], cx) * q
    west = harmonic(kx_[:-2], cx) * q
    north = harmonic(jnp.roll(cy, -1, axis=1), cy) * q
    north = jnp.where((gline != lines - 1)[None, :, None], north, 0.0)
    south = jnp.roll(north, 1, axis=1)
    vert = harmonic(cz[:, :, 1:], cz[:, :, :-1]) * q
    closed = jnp.zeros_like(cz[:, :, :1])
    above = jnp.concatenate([vert, closed], axis=2)
    below = jnp.concatenate([closed, vert], axis=2)
    cst = st_[1:-1]
    cdiag = jnp.maximum(cst + east + west + north + south + above + below, 0.01)
    csrc = source[1:-1]
    u = jnp.broadcast_to(line_mean[:, None, :], source.shape)
    for sweep in range(COARSE_SWEEPS):
        lo = sweep
        centre = u[1:-1]
        sl = slice(lo, width - 2 - lo)
        upper = jnp.concatenate([centre[:, :, 1:], centre[:, :, :1]], axis=2)
        lower = jnp.concatenate([centre[:, :, -1:], centre[:, :, :-1]], axis=2)
        fl = east[sl] * (centre - u[2:]) + west[sl] * (centre - u[:-2])
        fl = fl + north[sl] * (centre - jnp.roll(centre, -1, axis=1))
        fl = fl + south[sl] * (centre - jnp.roll(centre, 1, axis=1))
        fl = fl + above[sl] * (centre - upper) + below[sl] * (centre - lower)
        applied = cst[sl] * centre + fl
        u = centre + jacobi_weight * ((csrc[sl] - applied) / cdiag[sl])
    um = (hm + 1) // 2
    have = reach * nc - COARSE_SWEEPS
    u = u[have - um : u.shape[0] - (have - um)]
    rows = [(k % lines) for k in range(-um, nc + um)]
    runs = []
    for r in rows:
        if runs and runs[-1][1] == r:
            runs[-1][1] = r + 1
        else:
            runs.append([r, r + 1])
    u = jnp.concatenate([u[:, a:b] for a, b in runs], axis=1)
    kept = iy * nc + jnp.arange(-um, nc + um)
    u = jnp.where(((kept >= 0) & (kept < lines))[None, :, None], u, 0.0)
    s1e = win(mext[0], nm, hm, hm) + win(prolong(u), nm, 2 * um, hm)
    b1e = mext[1]
    y1, y1m = chebyshev(b1e, hm, s1e, hm, mid)
    fm = 2 * y1m
    s0 = win(x0, n, x0m, fm) + prolong(y1)
    fs = min(fm, CHEB)
    s0 = win(s0, n, fm, fs)
    out, om = chebyshev(rhs, hf, s0, fs, fine)
    return out


def solution(mesh):
    placed = (P("gx", "gy", None), P("gx", "gy", None), P("gx", "gy", None), P())
    return jax.shard_map(
        local, mesh=mesh, in_specs=placed, out_specs=P("gx", "gy", None), check_vma=False
    )
```

```python
import functools

import jax
import jax.numpy as jnp
from jax import lax
from jax.sharding import PartitionSpec as P
from jax.experimental import pallas as pl
from jax.experimental.pallas import tpu as pltpu

CHEB = 3
COARSE_SWEEPS = 8

storage_scale = 0.05
cheb_centre = 1.1
cheb_half = 0.9
cheb_ratio = cheb_centre / cheb_half
jacobi_weight = 0.8

FINE_HALO = 10
MID_HALO = 5
HIGH = lax.Precision.HIGHEST


def shift_from(cells, axis, offset):
    count = lax.axis_size(axis)
    if offset > 0:
        pairs = [(i + offset, i) for i in range(count - offset)]
    else:
        pairs = [(i, i - offset) for i in range(count + offset)]
    if not pairs:
        return jnp.zeros_like(cells)
    return lax.ppermute(cells, axis, pairs)


def halo(cells, sides, width):
    for axis, dim in sides:
        size = cells.shape[dim]
        head = lax.slice_in_dim(cells, 0, width, axis=dim)
        tail = lax.slice_in_dim(cells, size - width, size, axis=dim)
        cells = jnp.concatenate(
            [shift_from(tail, axis, -1), cells, shift_from(head, axis, 1)], axis=dim
        )
    return cells


def halo_overlapped(cells, width):
    sx, sy = cells.shape[1], cells.shape[2]
    west = shift_from(cells[:, sx - width :], "gx", -1)
    east = shift_from(cells[:, :width], "gx", 1)
    south = shift_from(cells[:, :, sy - width :], "gy", -1)
    north = shift_from(cells[:, :, :width], "gy", 1)
    low = shift_from(jnp.concatenate([west[:, :, sy - width :], east[:, :, sy - width :]], axis=1), "gy", -1)
    high = shift_from(jnp.concatenate([west[:, :, :width], east[:, :, :width]], axis=1), "gy", 1)
    top = jnp.concatenate([low[:, :width], west, high[:, :width]], axis=2)
    mid = jnp.concatenate([south, cells, north], axis=2)
    bottom = jnp.concatenate([low[:, width:], east, high[:, width:]], axis=2)
    return jnp.concatenate([top, mid, bottom], axis=1)


def frames_overlapped(fields, width):
    sx, sy = fields[0].shape[0], fields[0].shape[1]

    def slab(xs, ys):
        return jnp.stack([f[xs, ys].astype(jnp.float32) for f in fields])

    every = slice(None)
    west = shift_from(slab(slice(sx - width, sx), every), "gx", -1)
    east = shift_from(slab(slice(0, width), every), "gx", 1)
    south = shift_from(slab(every, slice(sy - width, sy)), "gy", -1)
    north = shift_from(slab(every, slice(0, width)), "gy", 1)
    low = shift_from(jnp.concatenate([west[:, :, sy - width :], east[:, :, sy - width :]], axis=1), "gy", -1)
    high = shift_from(jnp.concatenate([west[:, :, :width], east[:, :, :width]], axis=1), "gy", 1)
    out = []
    for k, f in enumerate(fields):
        top = jnp.concatenate([low[k, :width], west[k], high[k, :width]], axis=1)
        mid = jnp.concatenate([south[k], f.astype(jnp.float32), north[k]], axis=1)
        bottom = jnp.concatenate([low[k, width:], east[k], high[k, width:]], axis=1)
        out.append(jnp.concatenate([top, mid, bottom], axis=0))
    return out


def harmonic(first, second):
    return first * second / jnp.maximum(0.5 * (first + second), 0.1)


def win(a, n, margin, r, dx=0, dy=0):
    lo = margin - r
    hi = margin + n + r
    return a[..., lo + dx : hi + dx, lo + dy : hi + dy, :]


def pair_matrix(size, dtype=jnp.float32):
    rows = jnp.arange(size)[:, None] // 2
    cols = jnp.arange(size // 2)[None, :]
    return (rows == cols).astype(dtype)


def coarsen(values):
    lead = values.shape[:-3]
    sx, sy, sz = values.shape[-3:]
    v = values.reshape(lead + (sx // 2, 2, sy, sz))
    v = v[..., 0, :, :] + v[..., 1, :, :]
    v = jnp.einsum("...yz,zw->...yw", v, pair_matrix(sz), precision=HIGH)
    rows = v.reshape((-1, sy, sz // 2))
    pick = jnp.broadcast_to(pair_matrix(sy).T, (rows.shape[0], sy // 2, sy))
    rows = lax.dot_general(pick, rows, (((2,), (1,)), ((0,), (0,))), precision=HIGH)
    v = rows.reshape(lead + (sx // 2, sy // 2, sz // 2))
    return v * 0.125


def prolong(values):
    sx, sy, sz = values.shape
    v = jnp.einsum("xyz,wz->xyw", values, pair_matrix(2 * sz), precision=HIGH)
    pick = jnp.broadcast_to(pair_matrix(2 * sy), (sx, 2 * sy, sy))
    v = lax.dot_general(pick, v, (((2,), (1,)), ((0,), (0,))), precision=HIGH)
    v = jnp.broadcast_to(v[:, None], (sx, 2) + v.shape[1:]).reshape((2 * sx,) + v.shape[1:])
    return v


def build_level(coeffs, n, margin, spacing):
    kx, ky, kz, store = coeffs[0], coeffs[1], coeffs[2], coeffs[3]
    fx = harmonic(kx[1:], kx[:-1]) * spacing
    fy = harmonic(ky[:, 1:], ky[:, :-1]) * spacing
    vertical = harmonic(kz[:, :, 1:], kz[:, :, :-1]) * spacing
    closed = jnp.zeros_like(kz[:, :, :1])
    above = jnp.concatenate([vertical, closed], axis=2)
    below = jnp.concatenate([closed, vertical], axis=2)
    level = dict(n=n, m=margin, fx=fx, fy=fy, above=above, below=below, store=store)
    r = margin - 1
    level["diag"] = jnp.maximum(faces_sum(level, r) + win(store, n, margin, r), 0.01)
    level["dm"] = r
    return level


def faces_sum(level, r):
    n, m = level["n"], level["m"]
    east = win(level["fx"], n, m, r)
    west = win(level["fx"], n, m, r, dx=-1)
    north = win(level["fy"], n, m, r)
    south = win(level["fy"], n, m, r, dy=-1)
    above = win(level["above"], n, m, r)
    below = win(level["below"], n, m, r)
    return east + west + north + south + above + below


def operate(values, vm, level):
    n, m = level["n"], level["m"]
    r = vm - 1
    centre = win(values, n, vm, r)
    upper = jnp.concatenate([centre[:, :, 1:], centre[:, :, :1]], axis=2)
    lower = jnp.concatenate([centre[:, :, -1:], centre[:, :, :-1]], axis=2)
    fx, fy = level["fx"], level["fy"]
    fluxes = win(fx, n, m, r) * (centre - win(values, n, vm, r, dx=1))
    fluxes = fluxes + win(fx, n, m, r, dx=-1) * (centre - win(values, n, vm, r, dx=-1))
    fluxes = fluxes + win(fy, n, m, r) * (centre - win(values, n, vm, r, dy=1))
    fluxes = fluxes + win(fy, n, m, r, dy=-1) * (centre - win(values, n, vm, r, dy=-1))
    fluxes = fluxes + win(level["above"], n, m, r) * (centre - upper)
    fluxes = fluxes + win(level["below"], n, m, r) * (centre - lower)
    return win(level["store"], n, m, r) * centre + fluxes


def chebyshev(target, tm, initial, im, level):
    n = level["n"]
    diag, dm = level["diag"], level["dm"]
    if initial is None:
        cur = min(tm, dm)
        misfit = win(target, n, tm, cur)
        update = misfit / win(diag, n, dm, cur) * (1.0 / cheb_centre)
        iterate = update
    else:
        applied = operate(initial, im, level)
        cur = im - 1
        misfit = win(target, n, tm, cur) - applied
        update = misfit / win(diag, n, dm, cur) * (1.0 / cheb_centre)
        iterate = win(initial, n, im, cur) + update
    factor = 1.0 / cheb_ratio
    for repeat in range(CHEB - 1):
        applied = operate(iterate, cur, level)
        nxt = cur - 1
        misfit = win(target, n, tm, nxt) - applied
        factor_new = 1.0 / (2.0 * cheb_ratio - factor)
        update = factor_new * factor * win(update, n, cur, nxt) + 2.0 * factor_new / cheb_half * (
            misfit / win(diag, n, dm, nxt)
        )
        iterate = win(iterate, n, cur, nxt) + update
        cur = nxt
        factor = factor_new
    return iterate, cur


def fields_kernel(frame, table_ref, conc_ref, idf_ref, out_ref):
    rows = conc_ref.shape[0]
    shape = conc_ref.shape[1:]
    mats = table_ref.shape[1]
    nx, ny, hf = frame
    x_lo = hf - lax.axis_index("gx") * nx
    y_lo = hf - lax.axis_index("gy") * ny
    x_hi = x_lo + lax.axis_size("gx") * nx
    y_hi = y_lo + lax.axis_size("gy") * ny
    col = lax.broadcasted_iota(jnp.int32, shape, 0)
    col_ok = (col >= y_lo) & (col < y_hi)

    def body(i, carry):
        ids = idf_ref[i]
        conc = conc_ref[i]
        row = jnp.zeros(shape, jnp.int32) + i
        ok = col_ok & (row >= x_lo) & (row < x_hi)
        vals = []
        for record in range(5):
            acc = jnp.zeros(shape, jnp.float32) + table_ref[record, mats - 1]
            for material in range(mats - 2, -1, -1):
                acc = jnp.where(ids == float(material), table_ref[record, material], acc)
            vals.append(acc)
        store = storage_scale * (1.0 + vals[3] * jnp.exp((vals[4] - 1.0) * jnp.log(conc)))
        out_ref[0, i] = jnp.where(ok, vals[0], 0.0)
        out_ref[1, i] = jnp.where(ok, vals[1], 0.0)
        out_ref[2, i] = jnp.where(ok, vals[2], 0.0)
        out_ref[3, i] = jnp.where(ok, store, 0.0)
        return carry

    lax.fori_loop(0, rows, body, 0, unroll=2)


def soil_fields(frame, soil_table, conc, idf):
    cells = conc.size
    return pl.pallas_call(
        functools.partial(fields_kernel, frame),
        out_shape=jax.ShapeDtypeStruct((4,) + conc.shape, jnp.float32),
        in_specs=[
            pl.BlockSpec(memory_space=pltpu.SMEM),
            pl.BlockSpec(memory_space=pltpu.VMEM),
            pl.BlockSpec(memory_space=pltpu.VMEM),
        ],
        out_specs=pl.BlockSpec(memory_space=pltpu.VMEM),
        cost_estimate=pl.CostEstimate(
            flops=100 * cells, transcendentals=2 * cells, bytes_accessed=24 * cells
        ),
    )(soil_table, conc, idf)


def local(conc_prev, right_side, soil_id, soil_table):
    n = conc_prev.shape[0]
    ny = conc_prev.shape[1]
    hf = FINE_HALO
    gx_count = lax.axis_size("gx")
    gy_count = lax.axis_size("gy")
    ix = lax.axis_index("gx")
    iy = lax.axis_index("gy")

    conc, rhs, idf = frames_overlapped([conc_prev, right_side, soil_id], hf)
    fine_c = soil_fields((n, ny, hf), soil_table, conc, idf)
    fine = build_level(fine_c, n, hf, 1.0)

    x0, x0m = chebyshev(rhs, hf, None, 0, fine)
    r0 = win(rhs, n, hf, x0m - 1) - operate(x0, x0m, fine)
    r0m = x0m - 1
    nm = n // 2
    mm = hf // 2
    mid_c = coarsen(fine_c)
    mid = build_level(mid_c, nm, mm, 0.25)
    b1 = coarsen(win(r0, n, r0m, 2 * (r0m // 2)))
    b1m = r0m // 2
    x1, x1m = chebyshev(b1, b1m, None, 0, mid)
    r1 = win(b1, nm, b1m, x1m - 1) - operate(x1, x1m, mid)
    r1m = x1m - 1
    b2 = coarsen(win(r1, nm, r1m, 0))
    coarse_own = coarsen(win(mid_c, nm, mm, 0))

    nc = b2.shape[0]
    cpack = jnp.concatenate([b2[None], coarse_own], axis=0)
    mpack = jnp.stack([win(x1, nm, x1m, 0), win(b1, nm, b1m, 0)])
    hm = MID_HALO
    blocks = [cpack]
    for step in range(1, gy_count):
        pairs = [(j, (j - step) % gy_count) for j in range(gy_count)]
        blocks.append(lax.ppermute(cpack, "gy", pairs))
    north = shift_from(mpack[:, :, :hm], "gy", 1)
    south = shift_from(mpack[:, :, nm - hm :], "gy", -1)
    mext = jnp.concatenate([south, mpack, north], axis=2)
    full = jnp.concatenate(blocks, axis=2)
    reach = 3
    parts = [shift_from(full, "gx", -d) for d in range(reach, 0, -1)]
    parts += [full]
    parts += [shift_from(full, "gx", d) for d in range(1, reach + 1)]
    cpack = jnp.concatenate(parts, axis=1)
    west_m = shift_from(mext[:, nm - hm :], "gx", -1)
    east_m = shift_from(mext[:, :hm], "gx", 1)
    mext = jnp.concatenate([west_m, mext, east_m], axis=1)
    source = cpack[0]
    cc = cpack[1:]
    line_total = jnp.sum(source, axis=1)
    line_store = jnp.sum(cc[3], axis=1)
    line_mean = jnp.where(line_store > 0, line_total / jnp.where(line_store > 0, line_store, 1.0), 0.0)
    width = source.shape[0]
    lines = source.shape[1]
    gline = (iy * nc + jnp.arange(lines)) % lines
    kx_, ky_, kz_, st_ = cc[0], cc[1], cc[2], cc[3]
    q = 0.0625
    cx = kx_[1:-1]
    cy = ky_[1:-1]
    cz = kz_[1:-1]
    east = harmonic(kx_[2:], cx) * q
    west = harmonic(kx_[:-2], cx) * q
    north = harmonic(jnp.roll(cy, -1, axis=1), cy) * q
    north = jnp.where((gline != lines - 1)[None, :, None], north, 0.0)
    south = jnp.roll(north, 1, axis=1)
    vert = harmonic(cz[:, :, 1:], cz[:, :, :-1]) * q
    closed = jnp.zeros_like(cz[:, :, :1])
    above = jnp.concatenate([vert, closed], axis=2)
    below = jnp.concatenate([closed, vert], axis=2)
    cst = st_[1:-1]
    cdiag = jnp.maximum(cst + east + west + north + south + above + below, 0.01)
    csrc = source[1:-1]
    u = jnp.broadcast_to(line_mean[:, None, :], source.shape)
    for sweep in range(COARSE_SWEEPS):
        lo = sweep
        centre = u[1:-1]
        sl = slice(lo, width - 2 - lo)
        upper = jnp.concatenate([centre[:, :, 1:], centre[:, :, :1]], axis=2)
        lower = jnp.concatenate([centre[:, :, -1:], centre[:, :, :-1]], axis=2)
        fl = east[sl] * (centre - u[2:]) + west[sl] * (centre - u[:-2])
        fl = fl + north[sl] * (centre - jnp.roll(centre, -1, axis=1))
        fl = fl + south[sl] * (centre - jnp.roll(centre, 1, axis=1))
        fl = fl + above[sl] * (centre - upper) + below[sl] * (centre - lower)
        applied = cst[sl] * centre + fl
        u = centre + jacobi_weight * ((csrc[sl] - applied) / cdiag[sl])
    um = (hm + 1) // 2
    have = reach * nc - COARSE_SWEEPS
    u = u[have - um : u.shape[0] - (have - um)]
    rows = [(k % lines) for k in range(-um, nc + um)]
    runs = []
    for r in rows:
        if runs and runs[-1][1] == r:
            runs[-1][1] = r + 1
        else:
            runs.append([r, r + 1])
    u = jnp.concatenate([u[:, a:b] for a, b in runs], axis=1)
    kept = iy * nc + jnp.arange(-um, nc + um)
    u = jnp.where(((kept >= 0) & (kept < lines))[None, :, None], u, 0.0)
    s1e = win(mext[0], nm, hm, hm) + win(prolong(u), nm, 2 * um, hm)
    b1e = mext[1]
    y1, y1m = chebyshev(b1e, hm, s1e, hm, mid)
    fm = 2 * y1m
    s0 = win(x0, n, x0m, fm) + prolong(y1)
    fs = min(fm, CHEB)
    s0 = win(s0, n, fm, fs)
    out, om = chebyshev(rhs, hf, s0, fs, fine)
    return out


def solution(mesh):
    placed = (P("gx", "gy", None), P("gx", "gy", None), P("gx", "gy", None), P())
    return jax.shard_map(
        local, mesh=mesh, in_specs=placed, out_specs=P("gx", "gy", None), check_vma=False
    )
```

```python
import functools

import jax
import jax.numpy as jnp
from jax import lax
from jax.sharding import PartitionSpec as P
from jax.experimental import pallas as pl
from jax.experimental.pallas import tpu as pltpu

CHEB = 3
COARSE_SWEEPS = 8

storage_scale = 0.05
cheb_centre = 1.1
cheb_half = 0.9
cheb_ratio = cheb_centre / cheb_half
jacobi_weight = 0.8

FINE_HALO = 10
MID_HALO = 5
HIGH = lax.Precision.HIGHEST


def shift_from(cells, axis, offset):
    count = lax.axis_size(axis)
    if offset > 0:
        pairs = [(i + offset, i) for i in range(count - offset)]
    else:
        pairs = [(i, i - offset) for i in range(count + offset)]
    if not pairs:
        return jnp.zeros_like(cells)
    return lax.ppermute(cells, axis, pairs)


def halo(cells, sides, width):
    for axis, dim in sides:
        size = cells.shape[dim]
        head = lax.slice_in_dim(cells, 0, width, axis=dim)
        tail = lax.slice_in_dim(cells, size - width, size, axis=dim)
        cells = jnp.concatenate(
            [shift_from(tail, axis, -1), cells, shift_from(head, axis, 1)], axis=dim
        )
    return cells


def halo_overlapped(cells, width):
    sx, sy = cells.shape[1], cells.shape[2]
    west = shift_from(cells[:, sx - width :], "gx", -1)
    east = shift_from(cells[:, :width], "gx", 1)
    south = shift_from(cells[:, :, sy - width :], "gy", -1)
    north = shift_from(cells[:, :, :width], "gy", 1)
    low = shift_from(jnp.concatenate([west[:, :, sy - width :], east[:, :, sy - width :]], axis=1), "gy", -1)
    high = shift_from(jnp.concatenate([west[:, :, :width], east[:, :, :width]], axis=1), "gy", 1)
    top = jnp.concatenate([low[:, :width], west, high[:, :width]], axis=2)
    mid = jnp.concatenate([south, cells, north], axis=2)
    bottom = jnp.concatenate([low[:, width:], east, high[:, width:]], axis=2)
    return jnp.concatenate([top, mid, bottom], axis=1)


def frames_overlapped(fields, width):
    sx, sy = fields[0].shape[0], fields[0].shape[1]

    def slab(xs, ys):
        return jnp.stack([f[xs, ys].astype(jnp.float32) for f in fields])

    every = slice(None)
    west = shift_from(slab(slice(sx - width, sx), every), "gx", -1)
    east = shift_from(slab(slice(0, width), every), "gx", 1)
    south = shift_from(slab(every, slice(sy - width, sy)), "gy", -1)
    north = shift_from(slab(every, slice(0, width)), "gy", 1)
    low = shift_from(jnp.concatenate([west[:, :, sy - width :], east[:, :, sy - width :]], axis=1), "gy", -1)
    high = shift_from(jnp.concatenate([west[:, :, :width], east[:, :, :width]], axis=1), "gy", 1)
    out = []
    for k, f in enumerate(fields):
        top = jnp.concatenate([low[k, :width], west[k], high[k, :width]], axis=1)
        mid = jnp.concatenate([south[k], f.astype(jnp.float32), north[k]], axis=1)
        bottom = jnp.concatenate([low[k, width:], east[k], high[k, width:]], axis=1)
        out.append(jnp.concatenate([top, mid, bottom], axis=0))
    return out


def harmonic(first, second):
    return first * second / jnp.maximum(0.5 * (first + second), 0.1)


def win(a, n, margin, r, dx=0, dy=0):
    lo = margin - r
    hi = margin + n + r
    return a[..., lo + dx : hi + dx, lo + dy : hi + dy, :]


def pair_matrix(size, dtype=jnp.float32):
    rows = jnp.arange(size)[:, None] // 2
    cols = jnp.arange(size // 2)[None, :]
    return (rows == cols).astype(dtype)


def coarsen(values):
    lead = values.shape[:-3]
    sx, sy, sz = values.shape[-3:]
    v = values.reshape(lead + (sx // 2, 2, sy, sz))
    v = v[..., 0, :, :] + v[..., 1, :, :]
    v = jnp.einsum("...yz,zw->...yw", v, pair_matrix(sz), precision=HIGH)
    rows = v.reshape((-1, sy, sz // 2))
    pick = jnp.broadcast_to(pair_matrix(sy).T, (rows.shape[0], sy // 2, sy))
    rows = lax.dot_general(pick, rows, (((2,), (1,)), ((0,), (0,))), precision=HIGH)
    v = rows.reshape(lead + (sx // 2, sy // 2, sz // 2))
    return v * 0.125


def prolong(values):
    sx, sy, sz = values.shape
    v = jnp.einsum("xyz,wz->xyw", values, pair_matrix(2 * sz), precision=HIGH)
    pick = jnp.broadcast_to(pair_matrix(2 * sy), (sx, 2 * sy, sy))
    v = lax.dot_general(pick, v, (((2,), (1,)), ((0,), (0,))), precision=HIGH)
    v = jnp.broadcast_to(v[:, None], (sx, 2) + v.shape[1:]).reshape((2 * sx,) + v.shape[1:])
    return v


def build_level(coeffs, n, margin, spacing):
    kx, ky, kz, store = coeffs[0], coeffs[1], coeffs[2], coeffs[3]
    fx = harmonic(kx[1:], kx[:-1]) * spacing
    fy = harmonic(ky[:, 1:], ky[:, :-1]) * spacing
    vertical = harmonic(kz[:, :, 1:], kz[:, :, :-1]) * spacing
    closed = jnp.zeros_like(kz[:, :, :1])
    above = jnp.concatenate([vertical, closed], axis=2)
    below = jnp.concatenate([closed, vertical], axis=2)
    level = dict(n=n, m=margin, fx=fx, fy=fy, above=above, below=below, store=store)
    r = margin - 1
    level["diag"] = jnp.maximum(faces_sum(level, r) + win(store, n, margin, r), 0.01)
    level["dm"] = r
    return level


def faces_sum(level, r):
    n, m = level["n"], level["m"]
    east = win(level["fx"], n, m, r)
    west = win(level["fx"], n, m, r, dx=-1)
    north = win(level["fy"], n, m, r)
    south = win(level["fy"], n, m, r, dy=-1)
    above = win(level["above"], n, m, r)
    below = win(level["below"], n, m, r)
    return east + west + north + south + above + below


def operate(values, vm, level):
    n, m = level["n"], level["m"]
    r = vm - 1
    centre = win(values, n, vm, r)
    upper = jnp.concatenate([centre[:, :, 1:], centre[:, :, :1]], axis=2)
    lower = jnp.concatenate([centre[:, :, -1:], centre[:, :, :-1]], axis=2)
    fx, fy = level["fx"], level["fy"]
    fluxes = win(fx, n, m, r) * (centre - win(values, n, vm, r, dx=1))
    fluxes = fluxes + win(fx, n, m, r, dx=-1) * (centre - win(values, n, vm, r, dx=-1))
    fluxes = fluxes + win(fy, n, m, r) * (centre - win(values, n, vm, r, dy=1))
    fluxes = fluxes + win(fy, n, m, r, dy=-1) * (centre - win(values, n, vm, r, dy=-1))
    fluxes = fluxes + win(level["above"], n, m, r) * (centre - upper)
    fluxes = fluxes + win(level["below"], n, m, r) * (centre - lower)
    return win(level["store"], n, m, r) * centre + fluxes


def chebyshev(target, tm, initial, im, level):
    n = level["n"]
    diag, dm = level["diag"], level["dm"]
    if initial is None:
        cur = min(tm, dm)
        misfit = win(target, n, tm, cur)
        update = misfit / win(diag, n, dm, cur) * (1.0 / cheb_centre)
        iterate = update
    else:
        applied = operate(initial, im, level)
        cur = im - 1
        misfit = win(target, n, tm, cur) - applied
        update = misfit / win(diag, n, dm, cur) * (1.0 / cheb_centre)
        iterate = win(initial, n, im, cur) + update
    factor = 1.0 / cheb_ratio
    for repeat in range(CHEB - 1):
        applied = operate(iterate, cur, level)
        nxt = cur - 1
        misfit = win(target, n, tm, nxt) - applied
        factor_new = 1.0 / (2.0 * cheb_ratio - factor)
        update = factor_new * factor * win(update, n, cur, nxt) + 2.0 * factor_new / cheb_half * (
            misfit / win(diag, n, dm, nxt)
        )
        iterate = win(iterate, n, cur, nxt) + update
        cur = nxt
        factor = factor_new
    return iterate, cur


def fields_kernel(frame, table_ref, conc_ref, idf_ref, out_ref):
    rows = conc_ref.shape[0]
    shape = conc_ref.shape[1:]
    mats = table_ref.shape[1]
    nx, ny, hf = frame
    x_lo = hf - lax.axis_index("gx") * nx
    y_lo = hf - lax.axis_index("gy") * ny
    x_hi = x_lo + lax.axis_size("gx") * nx
    y_hi = y_lo + lax.axis_size("gy") * ny
    col = lax.broadcasted_iota(jnp.int32, shape, 0)
    col_ok = (col >= y_lo) & (col < y_hi)

    def body(i, carry):
        ids = idf_ref[i]
        conc = conc_ref[i]
        row = jnp.zeros(shape, jnp.int32) + i
        ok = col_ok & (row >= x_lo) & (row < x_hi)
        vals = []
        for record in range(5):
            acc = jnp.zeros(shape, jnp.float32) + table_ref[record, mats - 1]
            for material in range(mats - 2, -1, -1):
                acc = jnp.where(ids == float(material), table_ref[record, material], acc)
            vals.append(acc)
        store = storage_scale * (1.0 + vals[3] * jnp.exp((vals[4] - 1.0) * jnp.log(conc)))
        out_ref[0, i] = jnp.where(ok, vals[0], 0.0)
        out_ref[1, i] = jnp.where(ok, vals[1], 0.0)
        out_ref[2, i] = jnp.where(ok, vals[2], 0.0)
        out_ref[3, i] = jnp.where(ok, store, 0.0)
        return carry

    lax.fori_loop(0, rows, body, 0, unroll=4)


def soil_fields(frame, soil_table, conc, idf):
    cells = conc.size
    return pl.pallas_call(
        functools.partial(fields_kernel, frame),
        out_shape=jax.ShapeDtypeStruct((4,) + conc.shape, jnp.float32),
        in_specs=[
            pl.BlockSpec(memory_space=pltpu.SMEM),
            pl.BlockSpec(memory_space=pltpu.VMEM),
            pl.BlockSpec(memory_space=pltpu.VMEM),
        ],
        out_specs=pl.BlockSpec(memory_space=pltpu.VMEM),
        cost_estimate=pl.CostEstimate(
            flops=100 * cells, transcendentals=2 * cells, bytes_accessed=24 * cells
        ),
    )(soil_table, conc, idf)


def local(conc_prev, right_side, soil_id, soil_table):
    n = conc_prev.shape[0]
    ny = conc_prev.shape[1]
    hf = FINE_HALO
    gx_count = lax.axis_size("gx")
    gy_count = lax.axis_size("gy")
    ix = lax.axis_index("gx")
    iy = lax.axis_index("gy")

    conc, rhs, idf = frames_overlapped([conc_prev, right_side, soil_id], hf)
    fine_c = soil_fields((n, ny, hf), soil_table, conc, idf)
    fine = build_level(fine_c, n, hf, 1.0)

    x0, x0m = chebyshev(rhs, hf, None, 0, fine)
    r0 = win(rhs, n, hf, x0m - 1) - operate(x0, x0m, fine)
    r0m = x0m - 1
    nm = n // 2
    mm = hf // 2
    mid_c = coarsen(fine_c)
    mid = build_level(mid_c, nm, mm, 0.25)
    b1 = coarsen(win(r0, n, r0m, 2 * (r0m // 2)))
    b1m = r0m // 2
    x1, x1m = chebyshev(b1, b1m, None, 0, mid)
    r1 = win(b1, nm, b1m, x1m - 1) - operate(x1, x1m, mid)
    r1m = x1m - 1
    b2 = coarsen(win(r1, nm, r1m, 0))
    coarse_own = coarsen(win(mid_c, nm, mm, 0))

    nc = b2.shape[0]
    cpack = jnp.concatenate([b2[None], coarse_own], axis=0)
    mpack = jnp.stack([win(x1, nm, x1m, 0), win(b1, nm, b1m, 0)])
    hm = MID_HALO
    blocks = [cpack]
    for step in range(1, gy_count):
        pairs = [(j, (j - step) % gy_count) for j in range(gy_count)]
        blocks.append(lax.ppermute(cpack, "gy", pairs))
    north = shift_from(mpack[:, :, :hm], "gy", 1)
    south = shift_from(mpack[:, :, nm - hm :], "gy", -1)
    mext = jnp.concatenate([south, mpack, north], axis=2)
    full = jnp.concatenate(blocks, axis=2)
    reach = 3
    parts = [shift_from(full, "gx", -d) for d in range(reach, 0, -1)]
    parts += [full]
    parts += [shift_from(full, "gx", d) for d in range(1, reach + 1)]
    cpack = jnp.concatenate(parts, axis=1)
    west_m = shift_from(mext[:, nm - hm :], "gx", -1)
    east_m = shift_from(mext[:, :hm], "gx", 1)
    mext = jnp.concatenate([west_m, mext, east_m], axis=1)
    source = cpack[0]
    cc = cpack[1:]
    line_total = jnp.sum(source, axis=1)
    line_store = jnp.sum(cc[3], axis=1)
    line_mean = jnp.where(line_store > 0, line_total / jnp.where(line_store > 0, line_store, 1.0), 0.0)
    width = source.shape[0]
    lines = source.shape[1]
    gline = (iy * nc + jnp.arange(lines)) % lines
    kx_, ky_, kz_, st_ = cc[0], cc[1], cc[2], cc[3]
    q = 0.0625
    cx = kx_[1:-1]
    cy = ky_[1:-1]
    cz = kz_[1:-1]
    east = harmonic(kx_[2:], cx) * q
    west = harmonic(kx_[:-2], cx) * q
    north = harmonic(jnp.roll(cy, -1, axis=1), cy) * q
    north = jnp.where((gline != lines - 1)[None, :, None], north, 0.0)
    south = jnp.roll(north, 1, axis=1)
    vert = harmonic(cz[:, :, 1:], cz[:, :, :-1]) * q
    closed = jnp.zeros_like(cz[:, :, :1])
    above = jnp.concatenate([vert, closed], axis=2)
    below = jnp.concatenate([closed, vert], axis=2)
    cst = st_[1:-1]
    cdiag = jnp.maximum(cst + east + west + north + south + above + below, 0.01)
    csrc = source[1:-1]
    u = jnp.broadcast_to(line_mean[:, None, :], source.shape)
    for sweep in range(COARSE_SWEEPS):
        lo = sweep
        centre = u[1:-1]
        sl = slice(lo, width - 2 - lo)
        upper = jnp.concatenate([centre[:, :, 1:], centre[:, :, :1]], axis=2)
        lower = jnp.concatenate([centre[:, :, -1:], centre[:, :, :-1]], axis=2)
        fl = east[sl] * (centre - u[2:]) + west[sl] * (centre - u[:-2])
        fl = fl + north[sl] * (centre - jnp.roll(centre, -1, axis=1))
        fl = fl + south[sl] * (centre - jnp.roll(centre, 1, axis=1))
        fl = fl + above[sl] * (centre - upper) + below[sl] * (centre - lower)
        applied = cst[sl] * centre + fl
        u = centre + jacobi_weight * ((csrc[sl] - applied) / cdiag[sl])
    um = (hm + 1) // 2
    have = reach * nc - COARSE_SWEEPS
    u = u[have - um : u.shape[0] - (have - um)]
    rows = [(k % lines) for k in range(-um, nc + um)]
    runs = []
    for r in rows:
        if runs and runs[-1][1] == r:
            runs[-1][1] = r + 1
        else:
            runs.append([r, r + 1])
    u = jnp.concatenate([u[:, a:b] for a, b in runs], axis=1)
    kept = iy * nc + jnp.arange(-um, nc + um)
    u = jnp.where(((kept >= 0) & (kept < lines))[None, :, None], u, 0.0)
    s1e = win(mext[0], nm, hm, hm) + win(prolong(u), nm, 2 * um, hm)
    b1e = mext[1]
    y1, y1m = chebyshev(b1e, hm, s1e, hm, mid)
    fm = 2 * y1m
    s0 = win(x0, n, x0m, fm) + prolong(y1)
    fs = min(fm, CHEB)
    s0 = win(s0, n, fm, fs)
    out, om = chebyshev(rhs, hf, s0, fs, fine)
    return out


def solution(mesh):
    placed = (P("gx", "gy", None), P("gx", "gy", None), P("gx", "gy", None), P())
    return jax.shard_map(
        local, mesh=mesh, in_specs=placed, out_specs=P("gx", "gy", None), check_vma=False
    )
```
